32 devices in a mesh: seq: 8 (over z, y), rep: 4 (over x, core).
Axes of the slice: x: 2, y: 2, z: 4, core: 2. Of those that a mesh axis runs over, the one named last changes fastest.
Arguments:
- queries: bfloat16 [8192, 512], P(('rep', 'seq')), parts along dimension 0, may hold values from -40 to 40
- key_tokens: bfloat16 [8192, 512], P(('rep', 'seq')), parts along dimension 0, may hold values from -8 to 8
- value_tokens: bfloat16 [8192, 512], P(('rep', 'seq')), parts along dimension 0, may hold values from -6 to 6
- grad_out: bfloat16 [8192, 512], P(('rep', 'seq')), parts along dimension 0, may hold values from -6 to 6
Outputs:
- attended: bfloat16 [8192, 512], P(('rep', 'seq')), parts along dimension 0
- grad_queries: bfloat16 [8192, 512], P(('rep', 'seq')), parts along dimension 0
- grad_keys: bfloat16 [8192, 512], P(('rep', 'seq')), parts along dimension 0
- grad_values: bfloat16 [8192, 512], P(('rep', 'seq')), parts along dimension 0
The draws below stay inside these ranges and needn't reach their ends.
There are 4 independent parts, one for each index of `rep`. The reference program is written for one: setup_inputs(seed, part) draws one part's arguments, and reference() takes and returns one part's arrays. A program takes and returns all parts, laid end to end along the dimension named above; each array names one. Nothing has to cross between parts.
All inputs are finite; a program needn't handle non-finite values.
Results may differ from the reference program's by a relative error of at most 0.04.
Values may be sent and summed in bfloat16 or wider, within the bound.
No kernel may reach another device: no remote copies, remote signals or barrier semaphores. Data moves between devices by JAX's collectives and lax.ppermute only.
A program may use at most 64 MiB of HBM per device.

```python
import math
import jax
import jax.numpy as jnp
from jax import lax

HEADS = 4
HD = 128
BLK = 128
WINDOW = 4
TOK_DEV = 256
SEQLEN = 2048
N_SEQ = 8


def query_key_pair(key):
    row_width = HEADS * HD
    full_shape = (SEQLEN, row_width)
    key_query = jax.random.fold_in(key, 101)
    key_keys = jax.random.fold_in(key, 202)
    query_draw = jnp.clip(jax.random.normal(key_query, full_shape, jnp.float32), -6.0, 6.0)
    key_draw = jnp.clip(jax.random.normal(key_keys, full_shape, jnp.float32), -6.0, 6.0)
    return (query_draw.astype(jnp.bfloat16), key_draw.astype(jnp.bfloat16))


def draw_queries(key, part):
    return query_key_pair(key)[0]


def draw_key_tokens(key, part):
    return query_key_pair(key)[1]


def shard_levels(stream_key, shape, pieces, low, high):
    def one(axis_at, parts):
        heights = jax.random.uniform(jax.random.fold_in(jax.random.fold_in(stream_key, 6), axis_at), (parts,), jnp.float32, low / len(pieces), high / len(pieces))
        return jnp.repeat(jnp.exp(heights), shape[axis_at] // parts).reshape((-1,) + (1,) * (len(shape) - axis_at - 1))

    level = one(*pieces[0])
    for cut in pieces[1:]:
        level = level * one(*cut)
    return level


def noise(rng, dims, spread, bound, cuts=(), held_as=jnp.bfloat16):
    loudness = shard_levels(rng, dims, cuts, -0.22, 0.18) if cuts else 1.0
    drawn = jax.random.normal(rng, dims, jnp.float32) * spread * loudness
    return jnp.minimum(jnp.maximum(drawn, -bound), bound).astype(held_as)


def setup_inputs(seed: int = 0, part: int = 0) -> dict:
    splits = jax.random.split(jax.random.key(seed), 5)
    own_keys = jax.random.split(jax.random.fold_in(splits[4], part), 5)
    queries = draw_queries(jax.random.fold_in(jax.random.fold_in(splits[4], part), 71), part)
    key_tokens = draw_key_tokens(jax.random.fold_in(jax.random.fold_in(splits[4], part), 71), part)
    value_tokens = noise(own_keys[2], (SEQLEN, HEADS * HD), 1.0, 6.0, ((0, 8),))
    grad_out = noise(own_keys[3], (SEQLEN, HEADS * HD), 1.0, 6.0, ((0, 8),))
    return {"queries": queries, "key_tokens": key_tokens, "value_tokens": value_tokens, "grad_out": grad_out}


NEG = -1e+30
HIGHEST_ACCURACY = lax.Precision.HIGHEST

def offset_lists(blocks_dev, block_total):
    near_list = list(range(WINDOW + 1))
    far_list = []
    stride = 1
    while stride < block_total:
        if stride > WINDOW:
            if stride <= blocks_dev:
                near_list.append(stride)
            else:
                far_list.append(stride)
        stride = stride * 2
    return (near_list, far_list)

def allowed_mask(first_block, blocks_dev, offsets):
    block_ids = first_block + jnp.arange(blocks_dev, dtype=jnp.int32)
    offset_arr = jnp.array(offsets, dtype=jnp.int32)
    block_live = block_ids[:, None] - offset_arr[None, :] >= 0
    row_ids = jnp.arange(BLK, dtype=jnp.int32)
    causal = row_ids[:, None] >= row_ids[None, :]
    later_slab = offset_arr > 0
    slab_causal = jnp.logical_or(later_slab[None, :, None], causal[:, None, :])
    allowed = jnp.logical_and(block_live[:, None, :, None], slab_causal[None, :, :, :])
    return allowed.reshape(blocks_dev, BLK, len(offsets) * BLK)

def head_cols(array_in, col_start):
    return array_in[..., col_start:col_start + HD]

def to_blocks(array_in, block_count):
    return array_in.reshape(block_count, BLK, array_in.shape[-1])

def head_pass(query_per_head, output_gradient_heads, key_slabs, value_slabs, allowed, logit_scale):
    block_count = key_slabs.shape[0]
    key_row_block = key_slabs.reshape(block_count, -1, HD).astype(jnp.float32)
    value_row_block = value_slabs.reshape(block_count, -1, HD).astype(jnp.float32)
    query_wide = query_per_head.astype(jnp.float32)
    output_gradient_wide = output_gradient_heads.astype(jnp.float32)
    score_matrix = jnp.einsum('nmv,njv->nmj', query_wide, key_row_block, precision=HIGHEST_ACCURACY) * logit_scale
    score_matrix = jnp.where(allowed, score_matrix, NEG)
    row_max = lax.optimization_barrier(jnp.max(score_matrix, axis=-1, keepdims=True))
    log_total = row_max + jnp.log(lax.optimization_barrier(jnp.sum(jnp.exp(score_matrix - row_max), axis=-1, keepdims=True)))
    probabilities = jnp.exp(score_matrix - log_total)
    attention_weight = probabilities.astype(jnp.bfloat16)
    attention_weight_wide = attention_weight.astype(jnp.float32)
    attended_per_head = jnp.einsum('jym,jmo->jyo', attention_weight_wide, value_row_block, precision=HIGHEST_ACCURACY).astype(jnp.bfloat16)
    out_dot = lax.optimization_barrier(jnp.sum(output_gradient_wide * attended_per_head.astype(jnp.float32), axis=-1, keepdims=True))
    probability_gradient = jnp.einsum('nmv,njv->nmj', output_gradient_wide, value_row_block, precision=HIGHEST_ACCURACY)
    score_gradient = (probabilities * (probability_gradient - out_dot)).astype(jnp.bfloat16)
    score_gradient_wide = score_gradient.astype(jnp.float32)
    query_gradient_heads = (jnp.einsum('jym,jmo->jyo', score_gradient_wide, key_row_block, precision=HIGHEST_ACCURACY) * logit_scale).astype(jnp.bfloat16)
    key_gradient = jnp.einsum('uwj,uwn->ujn', score_gradient_wide, query_wide, precision=HIGHEST_ACCURACY) * logit_scale
    value_gradient = jnp.einsum('uwj,uwn->ujn', attention_weight_wide, output_gradient_wide, precision=HIGHEST_ACCURACY)
    return (attended_per_head, query_gradient_heads, key_gradient, value_gradient)

def reference(queries, key_tokens, value_tokens, grad_out):
    row_width = HEADS * HD
    blocks_dev = TOK_DEV // BLK
    rim = (WINDOW + blocks_dev - 1) // blocks_dev
    near_list, far_list = offset_lists(blocks_dev, N_SEQ * blocks_dev)
    offsets = near_list + far_list
    near_count = len(near_list)
    logit_scale = 1.0 / math.sqrt(HD)
    span_blocks = (rim + 1) * blocks_dev
    pad_zero = jnp.zeros((rim * TOK_DEV, row_width), jnp.bfloat16)
    padded_keys = jnp.concatenate([pad_zero, key_tokens], axis=0)
    padded_values = jnp.concatenate([pad_zero, value_tokens], axis=0)

    def segment(seg_index, state_now):
        attended_all, grad_q_all, key_acc, value_acc = state_now
        seg_index = seg_index.astype(jnp.int32)
        row_start = (seg_index * TOK_DEV).astype(jnp.int32)
        span_keys = to_blocks(lax.dynamic_slice_in_dim(padded_keys, row_start, (rim + 1) * TOK_DEV, 0), span_blocks)
        span_values = to_blocks(lax.dynamic_slice_in_dim(padded_values, row_start, (rim + 1) * TOK_DEV, 0), span_blocks)
        query_blocks = to_blocks(lax.dynamic_slice_in_dim(queries, row_start, TOK_DEV, 0), blocks_dev)
        grad_blocks = to_blocks(lax.dynamic_slice_in_dim(grad_out, row_start, TOK_DEV, 0), blocks_dev)
        far_sources = []
        far_keys = []
        far_values = []
        for stride in far_list:
            source_seg = jnp.maximum(seg_index - stride // blocks_dev, 0).astype(jnp.int32)
            far_sources.append(source_seg)
            far_keys.append(to_blocks(lax.dynamic_slice_in_dim(key_tokens, source_seg * TOK_DEV, TOK_DEV, 0), blocks_dev))
            far_values.append(to_blocks(lax.dynamic_slice_in_dim(value_tokens, source_seg * TOK_DEV, TOK_DEV, 0), blocks_dev))
        allowed = allowed_mask(seg_index * blocks_dev, blocks_dev, offsets)
        attended_heads = []
        grad_query_heads = []
        near_key_heads = []
        near_value_heads = []
        far_key_parts = [[] for stride in far_list]
        far_value_parts = [[] for stride in far_list]
        lead = rim * blocks_dev
        for head_index in range(HEADS):
            col_start = head_index * HD
            key_slabs = jnp.stack([head_cols(span_keys[lead - offset:lead + blocks_dev - offset], col_start) for offset in near_list] + [head_cols(item, col_start) for item in far_keys], axis=1)
            value_slabs = jnp.stack([head_cols(span_values[lead - offset:lead + blocks_dev - offset], col_start) for offset in near_list] + [head_cols(item, col_start) for item in far_values], axis=1)
            attended_per_head, query_gradient_heads, key_gradient, value_gradient = head_pass(head_cols(query_blocks, col_start), head_cols(grad_blocks, col_start), key_slabs, value_slabs, allowed, logit_scale)
            key_gradient = key_gradient.reshape(blocks_dev, len(offsets), BLK, HD)
            value_gradient = value_gradient.reshape(blocks_dev, len(offsets), BLK, HD)
            near_key = jnp.zeros((span_blocks, BLK, HD), jnp.float32)
            near_value = jnp.zeros((span_blocks, BLK, HD), jnp.float32)
            for slot_index, offset in enumerate(near_list):
                near_key = near_key.at[lead - offset:lead + blocks_dev - offset].add(key_gradient[:, slot_index])
                near_value = near_value.at[lead - offset:lead + blocks_dev - offset].add(value_gradient[:, slot_index])
            for level_index in range(len(far_list)):
                far_key_parts[level_index].append(key_gradient[:, near_count + level_index].astype(jnp.bfloat16))
                far_value_parts[level_index].append(value_gradient[:, near_count + level_index].astype(jnp.bfloat16))
            attended_heads.append(attended_per_head)
            grad_query_heads.append(query_gradient_heads)
            near_key_heads.append(near_key)
            near_value_heads.append(near_value)
        attended_seg = jnp.concatenate(attended_heads, axis=-1).reshape(TOK_DEV, row_width)
        grad_q_seg = jnp.concatenate(grad_query_heads, axis=-1).reshape(TOK_DEV, row_width)
        near_keys = jnp.concatenate(near_key_heads, axis=-1).reshape((rim + 1) * TOK_DEV, row_width)
        near_values = jnp.concatenate(near_value_heads, axis=-1).reshape((rim + 1) * TOK_DEV, row_width)
        for back in range(rim + 1):
            target_seg = jnp.maximum(seg_index - back, 0).astype(jnp.int32)
            piece_start = (rim - back) * TOK_DEV
            key_acc = key_acc.at[target_seg].add(near_keys[piece_start:piece_start + TOK_DEV].astype(jnp.bfloat16).astype(jnp.float32))
            value_acc = value_acc.at[target_seg].add(near_values[piece_start:piece_start + TOK_DEV].astype(jnp.bfloat16).astype(jnp.float32))
        for level_index in range(len(far_list)):
            part_keys = jnp.concatenate(far_key_parts[level_index], axis=-1).reshape(TOK_DEV, row_width)
            part_values = jnp.concatenate(far_value_parts[level_index], axis=-1).reshape(TOK_DEV, row_width)
            key_acc = key_acc.at[far_sources[level_index]].add(part_keys.astype(jnp.float32))
            value_acc = value_acc.at[far_sources[level_index]].add(part_values.astype(jnp.float32))
        attended_all = attended_all.at[seg_index].set(attended_seg)
        grad_q_all = grad_q_all.at[seg_index].set(grad_q_seg)
        return (attended_all, grad_q_all, key_acc, value_acc)
    start_state = (jnp.zeros((N_SEQ, TOK_DEV, row_width), jnp.bfloat16), jnp.zeros((N_SEQ, TOK_DEV, row_width), jnp.bfloat16), jnp.zeros((N_SEQ, TOK_DEV, row_width), jnp.float32), jnp.zeros((N_SEQ, TOK_DEV, row_width), jnp.float32))
    attended_all, grad_q_all, key_acc, value_acc = lax.fori_loop(0, N_SEQ, segment, start_state)
    return (attended_all.reshape(SEQLEN, row_width), grad_q_all.reshape(SEQLEN, row_width), key_acc.reshape(SEQLEN, row_width).astype(jnp.bfloat16), value_acc.reshape(SEQLEN, row_width).astype(jnp.bfloat16))
```

```python
import math

import jax
import jax.numpy as jnp
from jax import lax
from jax.sharding import PartitionSpec as P

HEADS = 4
HD = 128
BLK = 128
WINDOW = 4


NEG = -1e30


def passed_along(value, axis, steps):
    count = lax.axis_size(axis)
    first, last = (max(0, -steps), min(count, count - steps))
    return lax.ppermute(value, axis, [(source, source + steps) for source in range(first, last)])


def offset_lists(block_total):
    near_list = list(range(WINDOW + 1))
    far_list = []
    stride = 1
    while stride < block_total:
        if stride > WINDOW:
            far_list.append(stride)
        stride = stride * 2
    return (near_list, far_list)


def allowed_mask(first_block, blocks_dev, offsets):
    block_ids = first_block + jnp.arange(blocks_dev, dtype=jnp.int32)
    offset_arr = jnp.array(offsets, dtype=jnp.int32)
    block_live = block_ids[:, None] - offset_arr[None, :] >= 0
    row_ids = jnp.arange(BLK, dtype=jnp.int32)
    causal = row_ids[:, None] >= row_ids[None, :]
    later_slab = offset_arr > 0
    slab_causal = jnp.logical_or(later_slab[None, :, None], causal[:, None, :])
    allowed = jnp.logical_and(block_live[:, None, :, None], slab_causal[None, :, :, :])
    return allowed.reshape(blocks_dev, BLK, len(offsets) * BLK)


def head_cols(array_in, col_start):
    return array_in[..., col_start : col_start + HD]


def to_blocks(array_in, block_count):
    return array_in.reshape(block_count, BLK, array_in.shape[-1])


def place_slabs(gradient, near_list, lead, span_blocks):
    blocks_dev = gradient.shape[0]
    placed = []
    for slot_index, offset in enumerate(near_list):
        before = lead - offset
        after = span_blocks - before - blocks_dev
        placed.append(jnp.pad(gradient[:, slot_index], ((before, after), (0, 0), (0, 0))))
    total = placed[0]
    for item in placed[1:]:
        total = total + item
    return total


def head_pass(query_per_head, output_gradient_heads, key_slabs, value_slabs, allowed, logit_scale):
    block_count = key_slabs.shape[0]
    key_row_block = key_slabs.reshape(block_count, -1, HD)
    value_row_block = value_slabs.reshape(block_count, -1, HD)
    score_matrix = (
        jnp.einsum(
            "nmv,njv->nmj", query_per_head, key_row_block, preferred_element_type=jnp.float32
        )
        * logit_scale
    )
    score_matrix = jnp.where(allowed, score_matrix, NEG)
    row_max = jnp.max(score_matrix, axis=-1, keepdims=True)
    log_total = row_max + jnp.log(jnp.sum(jnp.exp(score_matrix - row_max), axis=-1, keepdims=True))
    probabilities = jnp.exp(score_matrix - log_total)
    attention_weight = probabilities.astype(jnp.bfloat16)
    attended_per_head = jnp.einsum(
        "jym,jmo->jyo", attention_weight, value_row_block, preferred_element_type=jnp.float32
    ).astype(jnp.bfloat16)
    out_dot = jnp.sum(
        output_gradient_heads.astype(jnp.float32) * attended_per_head.astype(jnp.float32),
        axis=-1,
        keepdims=True,
    )
    probability_gradient = jnp.einsum(
        "nmv,njv->nmj", output_gradient_heads, value_row_block, preferred_element_type=jnp.float32
    )
    score_gradient = (probabilities * (probability_gradient - out_dot)).astype(jnp.bfloat16)
    query_gradient_heads = (
        jnp.einsum(
            "jym,jmo->jyo", score_gradient, key_row_block, preferred_element_type=jnp.float32
        )
        * logit_scale
    ).astype(jnp.bfloat16)
    key_gradient = (
        jnp.einsum(
            "uwj,uwn->ujn", score_gradient, query_per_head, preferred_element_type=jnp.float32
        )
        * logit_scale
    )
    value_gradient = jnp.einsum(
        "uwj,uwn->ujn", attention_weight, output_gradient_heads, preferred_element_type=jnp.float32
    )
    return (
        attended_per_head,
        query_gradient_heads,
        key_gradient,
        value_gradient,
        log_total[..., 0],
        out_dot[..., 0],
    )


def swap_pairs(count):
    return [(source, source ^ 1) for source in range(count) if source ^ 1 < count]


def relay_ok(count, blocks_dev, rim, far_shifts):
    return count % 2 == 0 and blocks_dev == 2 and rim == 2 and (not far_shifts or far_shifts[0] == 4)


def body(queries, key_tokens, value_tokens, grad_out):
    row_width = queries.shape[1]
    tok_count = queries.shape[0]
    blocks_dev = tok_count // BLK
    rim = (WINDOW + blocks_dev - 1) // blocks_dev
    devices = lax.axis_size("seq")
    near_list, far_list = offset_lists(devices * blocks_dev)
    offsets = near_list + far_list
    near_count = len(near_list)
    logit_scale = 1.0 / math.sqrt(HD)
    span_blocks = (rim + 1) * blocks_dev
    lead = rim * blocks_dev
    far_shifts = [stride // blocks_dev for stride in far_list]
    relay = relay_ok(devices, blocks_dev, rim, far_shifts)
    position = lax.axis_index("seq")
    odd = (position % 2) == 1
    if relay:
        both = jnp.concatenate([key_tokens, value_tokens], axis=1)
        back2 = passed_along(both, "seq", 2)
        back1 = lax.ppermute(jnp.where(odd, back2, both), "seq", swap_pairs(devices))
        far_both = []
        for level_index, shift in enumerate(far_shifts):
            if level_index == 0:
                far_both.append(passed_along(back2, "seq", 2))
            else:
                far_both.append(passed_along(both, "seq", shift))
        earlier_keys = [back2[:, :row_width], back1[:, :row_width]]
        earlier_values = [back2[:, row_width:], back1[:, row_width:]]
        far_keys = [to_blocks(item[:, :row_width], blocks_dev) for item in far_both]
        far_values = [to_blocks(item[:, row_width:], blocks_dev) for item in far_both]
    else:
        earlier_keys = []
        earlier_values = []
        for back in range(rim, 0, -1):
            got_keys, got_values = passed_along((key_tokens, value_tokens), "seq", back)
            earlier_keys.append(got_keys)
            earlier_values.append(got_values)
        far_keys = []
        far_values = []
        for stride in far_list:
            got_keys, got_values = passed_along(
                (key_tokens, value_tokens), "seq", stride // blocks_dev
            )
            far_keys.append(to_blocks(got_keys, blocks_dev))
            far_values.append(to_blocks(got_values, blocks_dev))
    span_keys = to_blocks(jnp.concatenate(earlier_keys + [key_tokens], axis=0), span_blocks)
    span_values = to_blocks(jnp.concatenate(earlier_values + [value_tokens], axis=0), span_blocks)
    allowed = allowed_mask(position * blocks_dev, blocks_dev, offsets)
    query_blocks = to_blocks(queries, blocks_dev)
    grad_blocks = to_blocks(grad_out, blocks_dev)
    attended_heads = []
    grad_query_heads = []
    near_key_heads = []
    near_value_heads = []
    far_key_parts = [[] for stride in far_list]
    far_value_parts = [[] for stride in far_list]
    for head_index in range(HEADS):
        col_start = head_index * HD
        key_slabs = jnp.stack(
            [
                head_cols(span_keys[lead - offset : lead + blocks_dev - offset], col_start)
                for offset in near_list
            ]
            + [head_cols(item, col_start) for item in far_keys],
            axis=1,
        )
        value_slabs = jnp.stack(
            [
                head_cols(span_values[lead - offset : lead + blocks_dev - offset], col_start)
                for offset in near_list
            ]
            + [head_cols(item, col_start) for item in far_values],
            axis=1,
        )
        (
            attended_per_head,
            query_gradient_heads,
            key_gradient,
            value_gradient,
            log_total,
            out_dot,
        ) = head_pass(
            head_cols(query_blocks, col_start),
            head_cols(grad_blocks, col_start),
            key_slabs,
            value_slabs,
            allowed,
            logit_scale,
        )
        key_gradient = key_gradient.reshape(blocks_dev, -1, BLK, HD)
        value_gradient = value_gradient.reshape(blocks_dev, -1, BLK, HD)
        near_key_heads.append(place_slabs(key_gradient, near_list, lead, span_blocks))
        near_value_heads.append(place_slabs(value_gradient, near_list, lead, span_blocks))
        for level_index in range(len(far_list)):
            far_key_parts[level_index].append(key_gradient[:, near_count + level_index])
            far_value_parts[level_index].append(value_gradient[:, near_count + level_index])
        attended_heads.append(attended_per_head)
        grad_query_heads.append(query_gradient_heads)
    attended = jnp.concatenate(attended_heads, axis=-1).reshape(tok_count, row_width)
    grad_queries = jnp.concatenate(grad_query_heads, axis=-1).reshape(tok_count, row_width)
    near_keys = jnp.concatenate(near_key_heads, axis=-1).reshape((rim + 1) * tok_count, row_width)
    near_values = jnp.concatenate(near_value_heads, axis=-1).reshape(
        (rim + 1) * tok_count, row_width
    )
    far_parts = []
    for level_index in range(len(far_list)):
        part_keys = jnp.concatenate(far_key_parts[level_index], axis=-1).reshape(
            tok_count, row_width
        )
        part_values = jnp.concatenate(far_value_parts[level_index], axis=-1).reshape(
            tok_count, row_width
        )
        far_parts.append((part_keys, part_values))
    total_keys = near_keys[lead * BLK :].astype(jnp.bfloat16).astype(jnp.float32)
    total_values = near_values[lead * BLK :].astype(jnp.bfloat16).astype(jnp.float32)
    if relay:
        near_both = jnp.concatenate([near_keys, near_values], axis=1)
        part_two = near_both[:tok_count]
        part_one = near_both[tok_count : 2 * tok_count].astype(jnp.bfloat16)
        swapped = lax.ppermute(part_one, "seq", swap_pairs(devices)).astype(jnp.float32)
        zero = jnp.zeros_like(swapped)
        relayed = part_two + jnp.where(odd, swapped, zero)
        for level_index, shift in enumerate(far_shifts):
            far_both = jnp.concatenate(far_parts[level_index], axis=1).astype(jnp.bfloat16)
            if level_index == 0:
                relayed = relayed + passed_along(far_both, "seq", -2).astype(jnp.float32)
            else:
                got = passed_along(far_both, "seq", -shift).astype(jnp.float32)
                total_keys = total_keys + got[:, :row_width]
                total_values = total_values + got[:, row_width:]
        arrived = passed_along(relayed.astype(jnp.bfloat16), "seq", -2).astype(jnp.float32)
        arrived = arrived + jnp.where(odd, zero, swapped)
        total_keys = total_keys + arrived[:, :row_width]
        total_values = total_values + arrived[:, row_width:]
    else:
        for back in range(1, rim + 1):
            piece_start = (rim - back) * tok_count
            part_keys = near_keys[piece_start : piece_start + tok_count].astype(jnp.bfloat16)
            part_values = near_values[piece_start : piece_start + tok_count].astype(jnp.bfloat16)
            back_keys, back_values = passed_along((part_keys, part_values), "seq", -back)
            total_keys = total_keys + back_keys.astype(jnp.float32)
            total_values = total_values + back_values.astype(jnp.float32)
        for level_index, stride in enumerate(far_list):
            part_keys, part_values = far_parts[level_index]
            got_keys, got_values = passed_along(
                (part_keys.astype(jnp.bfloat16), part_values.astype(jnp.bfloat16)),
                "seq",
                -(stride // blocks_dev),
            )
            total_keys = total_keys + got_keys.astype(jnp.float32)
            total_values = total_values + got_values.astype(jnp.float32)
    return (
        attended,
        grad_queries,
        total_keys.astype(jnp.bfloat16),
        total_values.astype(jnp.bfloat16),
    )


def solution(mesh):
    placed = (
        P(("rep", "seq"), None),
        P(("rep", "seq"), None),
        P(("rep", "seq"), None),
        P(("rep", "seq"), None),
    )
    return jax.shard_map(
        body,
        mesh=mesh,
        in_specs=placed,
        out_specs=(
            P(("rep", "seq"), None),
            P(("rep", "seq"), None),
            P(("rep", "seq"), None),
            P(("rep", "seq"), None),
        ),
        check_vma=False,
    )
```

```python
import math

import jax
import jax.numpy as jnp
from jax import lax
from jax.sharding import PartitionSpec as P

HEADS = 4
HD = 128
BLK = 128
WINDOW = 4


NEG = -1e30
CHUNKS = 2


def passed_along(value, axis, steps):
    count = lax.axis_size(axis)
    first, last = (max(0, -steps), min(count, count - steps))
    return lax.ppermute(value, axis, [(source, source + steps) for source in range(first, last)])


def offset_lists(block_total):
    near_list = list(range(WINDOW + 1))
    far_list = []
    stride = 1
    while stride < block_total:
        if stride > WINDOW:
            far_list.append(stride)
        stride = stride * 2
    return (near_list, far_list)


def allowed_mask(first_block, blocks_dev, offsets):
    block_ids = first_block + jnp.arange(blocks_dev, dtype=jnp.int32)
    offset_arr = jnp.array(offsets, dtype=jnp.int32)
    block_live = block_ids[:, None] - offset_arr[None, :] >= 0
    row_ids = jnp.arange(BLK, dtype=jnp.int32)
    causal = row_ids[:, None] >= row_ids[None, :]
    later_slab = offset_arr > 0
    slab_causal = jnp.logical_or(later_slab[None, :, None], causal[:, None, :])
    allowed = jnp.logical_and(block_live[:, None, :, None], slab_causal[None, :, :, :])
    return allowed.reshape(blocks_dev, BLK, len(offsets) * BLK)


def head_cols(array_in, col_start):
    return array_in[..., col_start : col_start + HD]


def to_blocks(array_in, block_count):
    return array_in.reshape(block_count, BLK, array_in.shape[-1])


def place_slabs(gradient, near_list, lead, span_blocks):
    blocks_dev = gradient.shape[0]
    placed = []
    for slot_index, offset in enumerate(near_list):
        before = lead - offset
        after = span_blocks - before - blocks_dev
        placed.append(jnp.pad(gradient[:, slot_index], ((before, after), (0, 0), (0, 0))))
    total = placed[0]
    for item in placed[1:]:
        total = total + item
    return total


def head_pass(query_per_head, output_gradient_heads, key_slabs, value_slabs, allowed, logit_scale):
    block_count = key_slabs.shape[0]
    key_row_block = key_slabs.reshape(block_count, -1, HD)
    value_row_block = value_slabs.reshape(block_count, -1, HD)
    score_matrix = (
        jnp.einsum(
            "nmv,njv->nmj", query_per_head, key_row_block, preferred_element_type=jnp.float32
        )
        * logit_scale
    )
    score_matrix = jnp.where(allowed, score_matrix, NEG)
    row_max = jnp.max(score_matrix, axis=-1, keepdims=True)
    log_total = row_max + jnp.log(jnp.sum(jnp.exp(score_matrix - row_max), axis=-1, keepdims=True))
    probabilities = jnp.exp(score_matrix - log_total)
    attention_weight = probabilities.astype(jnp.bfloat16)
    attended_per_head = jnp.einsum(
        "jym,jmo->jyo", attention_weight, value_row_block, preferred_element_type=jnp.float32
    ).astype(jnp.bfloat16)
    out_dot = jnp.sum(
        output_gradient_heads.astype(jnp.float32) * attended_per_head.astype(jnp.float32),
        axis=-1,
        keepdims=True,
    )
    probability_gradient = jnp.einsum(
        "nmv,njv->nmj", output_gradient_heads, value_row_block, preferred_element_type=jnp.float32
    )
    score_gradient = (probabilities * (probability_gradient - out_dot)).astype(jnp.bfloat16)
    query_gradient_heads = (
        jnp.einsum(
            "jym,jmo->jyo", score_gradient, key_row_block, preferred_element_type=jnp.float32
        )
        * logit_scale
    ).astype(jnp.bfloat16)
    key_gradient = (
        jnp.einsum(
            "uwj,uwn->ujn", score_gradient, query_per_head, preferred_element_type=jnp.float32
        )
        * logit_scale
    )
    value_gradient = jnp.einsum(
        "uwj,uwn->ujn", attention_weight, output_gradient_heads, preferred_element_type=jnp.float32
    )
    return (
        attended_per_head,
        query_gradient_heads,
        key_gradient,
        value_gradient,
        log_total[..., 0],
        out_dot[..., 0],
    )


def legacy_body(queries, key_tokens, value_tokens, grad_out):
    row_width = queries.shape[1]
    tok_count = queries.shape[0]
    blocks_dev = tok_count // BLK
    rim = (WINDOW + blocks_dev - 1) // blocks_dev
    devices = lax.axis_size("seq")
    near_list, far_list = offset_lists(devices * blocks_dev)
    offsets = near_list + far_list
    near_count = len(near_list)
    logit_scale = 1.0 / math.sqrt(HD)
    span_blocks = (rim + 1) * blocks_dev
    lead = rim * blocks_dev
    earlier_keys = []
    earlier_values = []
    for back in range(rim, 0, -1):
        got_keys, got_values = passed_along((key_tokens, value_tokens), "seq", back)
        earlier_keys.append(got_keys)
        earlier_values.append(got_values)
    span_keys = to_blocks(jnp.concatenate(earlier_keys + [key_tokens], axis=0), span_blocks)
    span_values = to_blocks(jnp.concatenate(earlier_values + [value_tokens], axis=0), span_blocks)
    far_keys = []
    far_values = []
    for stride in far_list:
        got_keys, got_values = passed_along((key_tokens, value_tokens), "seq", stride // blocks_dev)
        far_keys.append(to_blocks(got_keys, blocks_dev))
        far_values.append(to_blocks(got_values, blocks_dev))
    position = lax.axis_index("seq")
    allowed = allowed_mask(position * blocks_dev, blocks_dev, offsets)
    query_blocks = to_blocks(queries, blocks_dev)
    grad_blocks = to_blocks(grad_out, blocks_dev)
    attended_heads = []
    grad_query_heads = []
    near_key_heads = []
    near_value_heads = []
    total_heads = []
    dot_heads = []
    far_key_parts = [[] for stride in far_list]
    far_value_parts = [[] for stride in far_list]
    for head_index in range(HEADS):
        col_start = head_index * HD
        key_slabs = jnp.stack(
            [
                head_cols(span_keys[lead - offset : lead + blocks_dev - offset], col_start)
                for offset in near_list
            ]
            + [head_cols(item, col_start) for item in far_keys],
            axis=1,
        )
        value_slabs = jnp.stack(
            [
                head_cols(span_values[lead - offset : lead + blocks_dev - offset], col_start)
                for offset in near_list
            ]
            + [head_cols(item, col_start) for item in far_values],
            axis=1,
        )
        (
            attended_per_head,
            query_gradient_heads,
            key_gradient,
            value_gradient,
            log_total,
            out_dot,
        ) = head_pass(
            head_cols(query_blocks, col_start),
            head_cols(grad_blocks, col_start),
            key_slabs,
            value_slabs,
            allowed,
            logit_scale,
        )
        key_gradient = key_gradient.reshape(blocks_dev, -1, BLK, HD)
        value_gradient = value_gradient.reshape(blocks_dev, -1, BLK, HD)
        near_key_heads.append(place_slabs(key_gradient, near_list, lead, span_blocks))
        near_value_heads.append(place_slabs(value_gradient, near_list, lead, span_blocks))
        for level_index in range(len(far_list)):
            far_key_parts[level_index].append(
                key_gradient[:, near_count + level_index].astype(jnp.bfloat16)
            )
            far_value_parts[level_index].append(
                value_gradient[:, near_count + level_index].astype(jnp.bfloat16)
            )
        attended_heads.append(attended_per_head)
        grad_query_heads.append(query_gradient_heads)
        total_heads.append(log_total)
        dot_heads.append(out_dot)
    attended = jnp.concatenate(attended_heads, axis=-1).reshape(tok_count, row_width)
    grad_queries = jnp.concatenate(grad_query_heads, axis=-1).reshape(tok_count, row_width)
    near_keys = jnp.concatenate(near_key_heads, axis=-1).reshape((rim + 1) * tok_count, row_width)
    near_values = jnp.concatenate(near_value_heads, axis=-1).reshape(
        (rim + 1) * tok_count, row_width
    )
    total_keys = near_keys[lead * BLK :].astype(jnp.bfloat16).astype(jnp.float32)
    total_values = near_values[lead * BLK :].astype(jnp.bfloat16).astype(jnp.float32)
    for back in range(1, rim + 1):
        piece_start = (rim - back) * tok_count
        part_keys = near_keys[piece_start : piece_start + tok_count].astype(jnp.bfloat16)
        part_values = near_values[piece_start : piece_start + tok_count].astype(jnp.bfloat16)
        back_keys, back_values = passed_along((part_keys, part_values), "seq", -back)
        total_keys = total_keys + back_keys.astype(jnp.float32)
        total_values = total_values + back_values.astype(jnp.float32)
    for level_index, stride in enumerate(far_list):
        part_keys = jnp.concatenate(far_key_parts[level_index], axis=-1).reshape(
            tok_count, row_width
        )
        part_values = jnp.concatenate(far_value_parts[level_index], axis=-1).reshape(
            tok_count, row_width
        )
        got_keys, got_values = passed_along(
            (part_keys, part_values), "seq", -(stride // blocks_dev)
        )
        total_keys = total_keys + got_keys.astype(jnp.float32)
        total_values = total_values + got_values.astype(jnp.float32)
    return (
        attended,
        grad_queries,
        total_keys.astype(jnp.bfloat16),
        total_values.astype(jnp.bfloat16),
    )


def swap_pairs(count):
    return [(source, source ^ 1) for source in range(count) if source ^ 1 < count]


def relay_ok(count, blocks_dev, rim, far_shifts):
    return count % 2 == 0 and blocks_dev == 2 and rim == 2 and (not far_shifts or far_shifts[0] == 4)


def plan(tok_count, devices):
    blocks_dev = tok_count // BLK
    rim = (WINDOW + blocks_dev - 1) // blocks_dev
    near_list, far_list = offset_lists(devices * blocks_dev)
    far_shifts = [stride // blocks_dev for stride in far_list]
    return blocks_dev, rim, near_list, far_list, far_shifts


def forward_round_two(both, back2, odd, devices, far_shifts):
    back1 = lax.ppermute(jnp.where(odd, back2, both), "seq", swap_pairs(devices))
    far_both = []
    for level_index, shift in enumerate(far_shifts):
        if level_index == 0:
            far_both.append(passed_along(back2, "seq", 2))
        else:
            far_both.append(passed_along(both, "seq", shift))
    return back1, far_both


def chunk_compute(queries, grad_out, both, back2, back1, far_both, devices):
    row_width = queries.shape[1]
    tok_count = queries.shape[0]
    blocks_dev, rim, near_list, far_list, far_shifts = plan(tok_count, devices)
    offsets = near_list + far_list
    near_count = len(near_list)
    logit_scale = 1.0 / math.sqrt(HD)
    span_blocks = (rim + 1) * blocks_dev
    lead = rim * blocks_dev
    position = lax.axis_index("seq")
    span_both = jnp.concatenate([back2, back1, both], axis=0)
    span_keys = to_blocks(span_both[:, :row_width], span_blocks)
    span_values = to_blocks(span_both[:, row_width:], span_blocks)
    far_keys = [to_blocks(item[:, :row_width], blocks_dev) for item in far_both]
    far_values = [to_blocks(item[:, row_width:], blocks_dev) for item in far_both]
    allowed = allowed_mask(position * blocks_dev, blocks_dev, offsets)
    query_blocks = to_blocks(queries, blocks_dev)
    grad_blocks = to_blocks(grad_out, blocks_dev)
    attended_heads = []
    grad_query_heads = []
    near_key_heads = []
    near_value_heads = []
    far_key_parts = [[] for stride in far_list]
    far_value_parts = [[] for stride in far_list]
    for head_index in range(row_width // HD):
        col_start = head_index * HD
        key_slabs = jnp.stack(
            [
                head_cols(span_keys[lead - offset : lead + blocks_dev - offset], col_start)
                for offset in near_list
            ]
            + [head_cols(item, col_start) for item in far_keys],
            axis=1,
        )
        value_slabs = jnp.stack(
            [
                head_cols(span_values[lead - offset : lead + blocks_dev - offset], col_start)
                for offset in near_list
            ]
            + [head_cols(item, col_start) for item in far_values],
            axis=1,
        )
        attended_per_head, query_gradient_heads, key_gradient, value_gradient, _, _ = head_pass(
            head_cols(query_blocks, col_start),
            head_cols(grad_blocks, col_start),
            key_slabs,
            value_slabs,
            allowed,
            logit_scale,
        )
        key_gradient = key_gradient.reshape(blocks_dev, -1, BLK, HD)
        value_gradient = value_gradient.reshape(blocks_dev, -1, BLK, HD)
        near_key_heads.append(place_slabs(key_gradient, near_list, lead, span_blocks))
        near_value_heads.append(place_slabs(value_gradient, near_list, lead, span_blocks))
        for level_index in range(len(far_list)):
            far_key_parts[level_index].append(key_gradient[:, near_count + level_index])
            far_value_parts[level_index].append(value_gradient[:, near_count + level_index])
        attended_heads.append(attended_per_head)
        grad_query_heads.append(query_gradient_heads)
    attended = jnp.concatenate(attended_heads, axis=-1).reshape(tok_count, row_width)
    grad_queries = jnp.concatenate(grad_query_heads, axis=-1).reshape(tok_count, row_width)
    near_keys = jnp.concatenate(near_key_heads, axis=-1).reshape((rim + 1) * tok_count, row_width)
    near_values = jnp.concatenate(near_value_heads, axis=-1).reshape(
        (rim + 1) * tok_count, row_width
    )
    near_both = jnp.concatenate([near_keys, near_values], axis=1)
    own = near_both[2 * tok_count :].astype(jnp.bfloat16).astype(jnp.float32)
    part_two = near_both[:tok_count]
    part_one = near_both[tok_count : 2 * tok_count].astype(jnp.bfloat16)
    far_sends = []
    for level_index in range(len(far_list)):
        part_keys = jnp.concatenate(far_key_parts[level_index], axis=-1).reshape(
            tok_count, row_width
        )
        part_values = jnp.concatenate(far_value_parts[level_index], axis=-1).reshape(
            tok_count, row_width
        )
        far_sends.append(jnp.concatenate([part_keys, part_values], axis=1).astype(jnp.bfloat16))
    return attended, grad_queries, own, part_two, part_one, far_sends


def backward_round_one(own, part_one, far_sends, devices, far_shifts):
    swapped = lax.ppermute(part_one, "seq", swap_pairs(devices)).astype(jnp.float32)
    far_first = None
    for level_index, shift in enumerate(far_shifts):
        if level_index == 0:
            far_first = passed_along(far_sends[0], "seq", -2).astype(jnp.float32)
        else:
            own = own + passed_along(far_sends[level_index], "seq", -shift).astype(jnp.float32)
    return own, swapped, far_first


def backward_round_two(own, part_two, swapped, far_first, odd):
    zero = jnp.zeros_like(swapped)
    relayed = part_two + jnp.where(odd, swapped, zero)
    if far_first is not None:
        relayed = relayed + far_first
    arrived = passed_along(relayed.astype(jnp.bfloat16), "seq", -2).astype(jnp.float32)
    return own + arrived + jnp.where(odd, zero, swapped)


def body(queries, key_tokens, value_tokens, grad_out):
    row_width = queries.shape[1]
    tok_count = queries.shape[0]
    devices = lax.axis_size("seq")
    blocks_dev, rim, near_list, far_list, far_shifts = plan(tok_count, devices)
    if not relay_ok(devices, blocks_dev, rim, far_shifts):
        return legacy_body(queries, key_tokens, value_tokens, grad_out)
    odd = (lax.axis_index("seq") % 2) == 1
    width = row_width // CHUNKS
    cols = [slice(chunk * width, (chunk + 1) * width) for chunk in range(CHUNKS)]
    boths = [jnp.concatenate([key_tokens[:, c], value_tokens[:, c]], axis=1) for c in cols]
    back2s = []
    for chunk in range(CHUNKS):
        if chunk > 0:
            boths[chunk], back2s[chunk - 1] = lax.optimization_barrier(
                (boths[chunk], back2s[chunk - 1])
            )
        back2s.append(passed_along(boths[chunk], "seq", 2))
    arrivals = [
        forward_round_two(boths[chunk], back2s[chunk], odd, devices, far_shifts)
        for chunk in range(CHUNKS)
    ]
    outs = []
    pending = None
    for chunk in range(CHUNKS + 1):
        if chunk < CHUNKS:
            chunk_inputs = (queries[:, cols[chunk]], grad_out[:, cols[chunk]]) + arrivals[chunk]
            if pending is not None:
                chunk_inputs, pending = lax.optimization_barrier((chunk_inputs, pending))
        if pending is not None:
            attended, grad_queries, own, part_two, swapped, far_first = pending
            total = backward_round_two(own, part_two, swapped, far_first, odd)
            outs.append((attended, grad_queries, total[:, :width], total[:, width:]))
        if chunk == CHUNKS:
            break
        chunk_queries, chunk_grads, back1, far_both = chunk_inputs
        attended, grad_queries, own, part_two, part_one, far_sends = chunk_compute(
            chunk_queries, chunk_grads, boths[chunk], back2s[chunk], back1, far_both, devices
        )
        own, swapped, far_first = backward_round_one(own, part_one, far_sends, devices, far_shifts)
        pending = (attended, grad_queries, own, part_two, swapped, far_first)
    return tuple(
        jnp.concatenate([item[index] for item in outs], axis=1).astype(jnp.bfloat16)
        for index in range(4)
    )


def solution(mesh):
    placed = (
        P(("rep", "seq"), None),
        P(("rep", "seq"), None),
        P(("rep", "seq"), None),
        P(("rep", "seq"), None),
    )
    return jax.shard_map(
        body,
        mesh=mesh,
        in_specs=placed,
        out_specs=(
            P(("rep", "seq"), None),
            P(("rep", "seq"), None),
            P(("rep", "seq"), None),
            P(("rep", "seq"), None),
        ),
        check_vma=False,
    )
```

```python
import math

import jax
import jax.numpy as jnp
from jax import lax
from jax.sharding import PartitionSpec as P

HEADS = 4
HD = 128
BLK = 128
WINDOW = 4


NEG = -1e30
CHUNKS = 2


def passed_along(value, axis, steps):
    count = lax.axis_size(axis)
    first, last = (max(0, -steps), min(count, count - steps))
    return lax.ppermute(value, axis, [(source, source + steps) for source in range(first, last)])


def offset_lists(block_total):
    near_list = list(range(WINDOW + 1))
    far_list = []
    stride = 1
    while stride < block_total:
        if stride > WINDOW:
            far_list.append(stride)
        stride = stride * 2
    return (near_list, far_list)


def allowed_mask(first_block, blocks_dev, offsets):
    block_ids = first_block + jnp.arange(blocks_dev, dtype=jnp.int32)
    offset_arr = jnp.array(offsets, dtype=jnp.int32)
    block_live = block_ids[:, None] - offset_arr[None, :] >= 0
    row_ids = jnp.arange(BLK, dtype=jnp.int32)
    causal = row_ids[:, None] >= row_ids[None, :]
    later_slab = offset_arr > 0
    slab_causal = jnp.logical_or(later_slab[None, :, None], causal[:, None, :])
    allowed = jnp.logical_and(block_live[:, None, :, None], slab_causal[None, :, :, :])
    return allowed.reshape(blocks_dev, BLK, len(offsets) * BLK)


def head_cols(array_in, col_start):
    return array_in[..., col_start : col_start + HD]


def to_blocks(array_in, block_count):
    return array_in.reshape(block_count, BLK, array_in.shape[-1])


def place_slabs(gradient, near_list, lead, span_blocks):
    blocks_dev = gradient.shape[0]
    placed = []
    for slot_index, offset in enumerate(near_list):
        before = lead - offset
        after = span_blocks - before - blocks_dev
        placed.append(jnp.pad(gradient[:, slot_index], ((before, after), (0, 0), (0, 0))))
    total = placed[0]
    for item in placed[1:]:
        total = total + item
    return total


def head_pass(query_per_head, output_gradient_heads, key_slabs, value_slabs, allowed, logit_scale):
    block_count = key_slabs.shape[0]
    key_row_block = key_slabs.reshape(block_count, -1, HD)
    value_row_block = value_slabs.reshape(block_count, -1, HD)
    score_matrix = (
        jnp.einsum(
            "nmv,njv->nmj", query_per_head, key_row_block, preferred_element_type=jnp.float32
        )
        * logit_scale
    )
    score_matrix = jnp.where(allowed, score_matrix, NEG)
    row_max = jnp.max(score_matrix, axis=-1, keepdims=True)
    log_total = row_max + jnp.log(jnp.sum(jnp.exp(score_matrix - row_max), axis=-1, keepdims=True))
    probabilities = jnp.exp(score_matrix - log_total)
    attention_weight = probabilities.astype(jnp.bfloat16)
    attended_per_head = jnp.einsum(
        "jym,jmo->jyo", attention_weight, value_row_block, preferred_element_type=jnp.float32
    ).astype(jnp.bfloat16)
    out_dot = jnp.sum(
        output_gradient_heads.astype(jnp.float32) * attended_per_head.astype(jnp.float32),
        axis=-1,
        keepdims=True,
    )
    probability_gradient = jnp.einsum(
        "nmv,njv->nmj", output_gradient_heads, value_row_block, preferred_element_type=jnp.float32
    )
    score_gradient = (probabilities * (probability_gradient - out_dot)).astype(jnp.bfloat16)
    query_gradient_heads = (
        jnp.einsum(
            "jym,jmo->jyo", score_gradient, key_row_block, preferred_element_type=jnp.float32
        )
        * logit_scale
    ).astype(jnp.bfloat16)
    key_gradient = (
        jnp.einsum(
            "uwj,uwn->ujn", score_gradient, query_per_head, preferred_element_type=jnp.float32
        )
        * logit_scale
    )
    value_gradient = jnp.einsum(
        "uwj,uwn->ujn", attention_weight, output_gradient_heads, preferred_element_type=jnp.float32
    )
    return (
        attended_per_head,
        query_gradient_heads,
        key_gradient,
        value_gradient,
        log_total[..., 0],
        out_dot[..., 0],
    )


def legacy_body(queries, key_tokens, value_tokens, grad_out):
    row_width = queries.shape[1]
    tok_count = queries.shape[0]
    blocks_dev = tok_count // BLK
    rim = (WINDOW + blocks_dev - 1) // blocks_dev
    devices = lax.axis_size("seq")
    near_list, far_list = offset_lists(devices * blocks_dev)
    offsets = near_list + far_list
    near_count = len(near_list)
    logit_scale = 1.0 / math.sqrt(HD)
    span_blocks = (rim + 1) * blocks_dev
    lead = rim * blocks_dev
    earlier_keys = []
    earlier_values = []
    for back in range(rim, 0, -1):
        got_keys, got_values = passed_along((key_tokens, value_tokens), "seq", back)
        earlier_keys.append(got_keys)
        earlier_values.append(got_values)
    span_keys = to_blocks(jnp.concatenate(earlier_keys + [key_tokens], axis=0), span_blocks)
    span_values = to_blocks(jnp.concatenate(earlier_values + [value_tokens], axis=0), span_blocks)
    far_keys = []
    far_values = []
    for stride in far_list:
        got_keys, got_values = passed_along((key_tokens, value_tokens), "seq", stride // blocks_dev)
        far_keys.append(to_blocks(got_keys, blocks_dev))
        far_values.append(to_blocks(got_values, blocks_dev))
    position = lax.axis_index("seq")
    allowed = allowed_mask(position * blocks_dev, blocks_dev, offsets)
    query_blocks = to_blocks(queries, blocks_dev)
    grad_blocks = to_blocks(grad_out, blocks_dev)
    attended_heads = []
    grad_query_heads = []
    near_key_heads = []
    near_value_heads = []
    total_heads = []
    dot_heads = []
    far_key_parts = [[] for stride in far_list]
    far_value_parts = [[] for stride in far_list]
    for head_index in range(HEADS):
        col_start = head_index * HD
        key_slabs = jnp.stack(
            [
                head_cols(span_keys[lead - offset : lead + blocks_dev - offset], col_start)
                for offset in near_list
            ]
            + [head_cols(item, col_start) for item in far_keys],
            axis=1,
        )
        value_slabs = jnp.stack(
            [
                head_cols(span_values[lead - offset : lead + blocks_dev - offset], col_start)
                for offset in near_list
            ]
            + [head_cols(item, col_start) for item in far_values],
            axis=1,
        )
        (
            attended_per_head,
            query_gradient_heads,
            key_gradient,
            value_gradient,
            log_total,
            out_dot,
        ) = head_pass(
            head_cols(query_blocks, col_start),
            head_cols(grad_blocks, col_start),
            key_slabs,
            value_slabs,
            allowed,
            logit_scale,
        )
        key_gradient = key_gradient.reshape(blocks_dev, -1, BLK, HD)
        value_gradient = value_gradient.reshape(blocks_dev, -1, BLK, HD)
        near_key_heads.append(place_slabs(key_gradient, near_list, lead, span_blocks))
        near_value_heads.append(place_slabs(value_gradient, near_list, lead, span_blocks))
        for level_index in range(len(far_list)):
            far_key_parts[level_index].append(
                key_gradient[:, near_count + level_index].astype(jnp.bfloat16)
            )
            far_value_parts[level_index].append(
                value_gradient[:, near_count + level_index].astype(jnp.bfloat16)
            )
        attended_heads.append(attended_per_head)
        grad_query_heads.append(query_gradient_heads)
        total_heads.append(log_total)
        dot_heads.append(out_dot)
    attended = jnp.concatenate(attended_heads, axis=-1).reshape(tok_count, row_width)
    grad_queries = jnp.concatenate(grad_query_heads, axis=-1).reshape(tok_count, row_width)
    near_keys = jnp.concatenate(near_key_heads, axis=-1).reshape((rim + 1) * tok_count, row_width)
    near_values = jnp.concatenate(near_value_heads, axis=-1).reshape(
        (rim + 1) * tok_count, row_width
    )
    total_keys = near_keys[lead * BLK :].astype(jnp.bfloat16).astype(jnp.float32)
    total_values = near_values[lead * BLK :].astype(jnp.bfloat16).astype(jnp.float32)
    for back in range(1, rim + 1):
        piece_start = (rim - back) * tok_count
        part_keys = near_keys[piece_start : piece_start + tok_count].astype(jnp.bfloat16)
        part_values = near_values[piece_start : piece_start + tok_count].astype(jnp.bfloat16)
        back_keys, back_values = passed_along((part_keys, part_values), "seq", -back)
        total_keys = total_keys + back_keys.astype(jnp.float32)
        total_values = total_values + back_values.astype(jnp.float32)
    for level_index, stride in enumerate(far_list):
        part_keys = jnp.concatenate(far_key_parts[level_index], axis=-1).reshape(
            tok_count, row_width
        )
        part_values = jnp.concatenate(far_value_parts[level_index], axis=-1).reshape(
            tok_count, row_width
        )
        got_keys, got_values = passed_along(
            (part_keys, part_values), "seq", -(stride // blocks_dev)
        )
        total_keys = total_keys + got_keys.astype(jnp.float32)
        total_values = total_values + got_values.astype(jnp.float32)
    return (
        attended,
        grad_queries,
        total_keys.astype(jnp.bfloat16),
        total_values.astype(jnp.bfloat16),
    )


def swap_pairs(count):
    return [(source, source ^ 1) for source in range(count) if source ^ 1 < count]


def relay_ok(count, blocks_dev, rim, far_shifts):
    return count % 2 == 0 and blocks_dev == 2 and rim == 2 and (not far_shifts or far_shifts[0] == 4)


def plan(tok_count, devices):
    blocks_dev = tok_count // BLK
    rim = (WINDOW + blocks_dev - 1) // blocks_dev
    near_list, far_list = offset_lists(devices * blocks_dev)
    far_shifts = [stride // blocks_dev for stride in far_list]
    return blocks_dev, rim, near_list, far_list, far_shifts


def row_pass(query_per_head, output_gradient_heads, key_slabs, value_slabs, allowed, logit_scale):
    block_count = key_slabs.shape[0]
    key_row_block = key_slabs.reshape(block_count, -1, HD)
    value_row_block = value_slabs.reshape(block_count, -1, HD)
    score_matrix = (
        jnp.einsum(
            "nmv,njv->nmj", query_per_head, key_row_block, preferred_element_type=jnp.float32
        )
        * logit_scale
    )
    score_matrix = jnp.where(allowed, score_matrix, NEG)
    row_max = jnp.max(score_matrix, axis=-1, keepdims=True)
    log_total = row_max + jnp.log(jnp.sum(jnp.exp(score_matrix - row_max), axis=-1, keepdims=True))
    probabilities = jnp.exp(score_matrix - log_total)
    attention_weight = probabilities.astype(jnp.bfloat16)
    attended_per_head = jnp.einsum(
        "jym,jmo->jyo", attention_weight, value_row_block, preferred_element_type=jnp.float32
    ).astype(jnp.bfloat16)
    out_dot = jnp.sum(
        output_gradient_heads.astype(jnp.float32) * attended_per_head.astype(jnp.float32),
        axis=-1,
        keepdims=True,
    )
    probability_gradient = jnp.einsum(
        "nmv,njv->nmj", output_gradient_heads, value_row_block, preferred_element_type=jnp.float32
    )
    score_gradient = (probabilities * (probability_gradient - out_dot)).astype(jnp.bfloat16)
    query_gradient_heads = (
        jnp.einsum(
            "jym,jmo->jyo", score_gradient, key_row_block, preferred_element_type=jnp.float32
        )
        * logit_scale
    ).astype(jnp.bfloat16)
    return attended_per_head, query_gradient_heads, log_total[..., 0], out_dot[..., 0]


def key_pass(key_per_head, value_per_head, query_slabs, grad_slabs, total_slabs, dot_slabs, allowed, logit_scale):
    block_count = query_slabs.shape[0]
    query_rows = query_slabs.reshape(block_count, -1, HD)
    grad_rows = grad_slabs.reshape(block_count, -1, HD)
    score_matrix = (
        jnp.einsum("nmv,njv->nmj", query_rows, key_per_head, preferred_element_type=jnp.float32)
        * logit_scale
    )
    total_rows = total_slabs.reshape(block_count, -1, 1)
    dot_rows = dot_slabs.reshape(block_count, -1, 1)
    probabilities = jnp.where(allowed, jnp.exp(score_matrix - total_rows), 0.0)
    probability_gradient = jnp.einsum(
        "nmv,njv->nmj", grad_rows, value_per_head, preferred_element_type=jnp.float32
    )
    score_gradient = (probabilities * (probability_gradient - dot_rows)).astype(jnp.bfloat16)
    attention_weight = probabilities.astype(jnp.bfloat16)
    key_gradient = (
        jnp.einsum("nmj,nmv->njv", score_gradient, query_rows, preferred_element_type=jnp.float32)
        * logit_scale
    )
    value_gradient = jnp.einsum(
        "nmj,nmv->njv", attention_weight, grad_rows, preferred_element_type=jnp.float32
    )
    return key_gradient, value_gradient


def key_allowed(first_block, blocks_dev, offsets, block_total):
    block_ids = first_block + jnp.arange(blocks_dev, dtype=jnp.int32)
    offset_arr = jnp.array(offsets, dtype=jnp.int32)
    query_live = block_ids[:, None] + offset_arr[None, :] < block_total
    row_ids = jnp.arange(BLK, dtype=jnp.int32)
    causal = row_ids[:, None] >= row_ids[None, :]
    later_slab = offset_arr > 0
    slab_causal = jnp.logical_or(later_slab[:, None, None], causal[None, :, :])
    allowed = jnp.logical_and(query_live[:, :, None, None], slab_causal[None, :, :, :])
    return allowed.reshape(blocks_dev, len(offsets) * BLK, BLK)


def body(queries, key_tokens, value_tokens, grad_out):
    row_width = queries.shape[1]
    tok_count = queries.shape[0]
    devices = lax.axis_size("seq")
    blocks_dev, rim, near_list, far_list, far_shifts = plan(tok_count, devices)
    if not relay_ok(devices, blocks_dev, rim, far_shifts):
        return legacy_body(queries, key_tokens, value_tokens, grad_out)
    heads = row_width // HD
    offsets = near_list + far_list
    logit_scale = 1.0 / math.sqrt(HD)
    span_blocks = (rim + 1) * blocks_dev
    lead = rim * blocks_dev
    position = lax.axis_index("seq")
    odd = (position % 2) == 1
    pairs = swap_pairs(devices)
    keys_values = jnp.concatenate([key_tokens, value_tokens], axis=1)
    queries_grads = jnp.concatenate([queries, grad_out], axis=1)
    back2 = passed_along(keys_values, "seq", 2)
    ahead2 = passed_along(queries_grads, "seq", -2)
    swap_one = lax.ppermute(jnp.where(odd, queries_grads, keys_values), "seq", pairs)
    back4 = passed_along(back2, "seq", 2)
    ahead4 = passed_along(ahead2, "seq", -2)
    swap_two = lax.ppermute(jnp.where(odd, back2, ahead2), "seq", pairs)
    back1 = jnp.where(odd, swap_one, swap_two)
    ahead1 = jnp.where(odd, swap_two, swap_one)
    far_back = [back4] + [passed_along(keys_values, "seq", shift) for shift in far_shifts[1:]]
    far_ahead = [ahead4] + [passed_along(queries_grads, "seq", -shift) for shift in far_shifts[1:]]
    far_back = far_back[: len(far_shifts)]
    far_ahead = far_ahead[: len(far_shifts)]

    span_both = to_blocks(jnp.concatenate([back2, back1, keys_values], axis=0), span_blocks)
    far_both = [to_blocks(item, blocks_dev) for item in far_back]
    allowed = allowed_mask(position * blocks_dev, blocks_dev, offsets)
    query_blocks = to_blocks(queries, blocks_dev)
    grad_blocks = to_blocks(grad_out, blocks_dev)
    attended_heads = []
    grad_query_heads = []
    total_heads = []
    dot_heads = []
    for head_index in range(heads):
        key_col = head_index * HD
        value_col = row_width + head_index * HD
        key_slabs = jnp.stack(
            [
                head_cols(span_both[lead - offset : lead + blocks_dev - offset], key_col)
                for offset in near_list
            ]
            + [head_cols(item, key_col) for item in far_both],
            axis=1,
        )
        value_slabs = jnp.stack(
            [
                head_cols(span_both[lead - offset : lead + blocks_dev - offset], value_col)
                for offset in near_list
            ]
            + [head_cols(item, value_col) for item in far_both],
            axis=1,
        )
        attended_per_head, query_gradient_heads, log_total, out_dot = row_pass(
            head_cols(query_blocks, key_col),
            head_cols(grad_blocks, key_col),
            key_slabs,
            value_slabs,
            allowed,
            logit_scale,
        )
        attended_heads.append(attended_per_head.reshape(tok_count, HD))
        grad_query_heads.append(query_gradient_heads.reshape(tok_count, HD))
        total_heads.append(log_total.reshape(tok_count, 1))
        dot_heads.append(out_dot.reshape(tok_count, 1))
    attended = jnp.concatenate(attended_heads, axis=-1)
    grad_queries = jnp.concatenate(grad_query_heads, axis=-1)
    stats = jnp.concatenate(total_heads + dot_heads, axis=-1)
    stats_one = passed_along(stats, "seq", -1)
    stats_two = passed_along(stats, "seq", -2)
    far_stats = [passed_along(stats, "seq", -shift) for shift in far_shifts]

    span_rows = to_blocks(jnp.concatenate([queries_grads, ahead1, ahead2], axis=0), span_blocks)
    span_stats = to_blocks(jnp.concatenate([stats, stats_one, stats_two], axis=0), span_blocks)
    far_rows = [to_blocks(item, blocks_dev) for item in far_ahead]
    far_stat_blocks = [to_blocks(item, blocks_dev) for item in far_stats]
    row_slabs = jnp.stack(
        [
            jnp.stack(
                [span_rows[block + offset] for offset in near_list]
                + [item[block] for item in far_rows],
                axis=0,
            )
            for block in range(blocks_dev)
        ],
        axis=0,
    )
    stat_slabs = jnp.stack(
        [
            jnp.stack(
                [span_stats[block + offset] for offset in near_list]
                + [item[block] for item in far_stat_blocks],
                axis=0,
            )
            for block in range(blocks_dev)
        ],
        axis=0,
    )
    permitted = key_allowed(position * blocks_dev, blocks_dev, offsets, devices * blocks_dev)
    key_blocks = to_blocks(key_tokens, blocks_dev)
    value_blocks = to_blocks(value_tokens, blocks_dev)
    key_grad_heads = []
    value_grad_heads = []
    for head_index in range(heads):
        col = head_index * HD
        key_gradient, value_gradient = key_pass(
            head_cols(key_blocks, col),
            head_cols(value_blocks, col),
            head_cols(row_slabs, col),
            head_cols(row_slabs, row_width + col),
            stat_slabs[..., head_index],
            stat_slabs[..., heads + head_index],
            permitted,
            logit_scale,
        )
        key_grad_heads.append(key_gradient.reshape(tok_count, HD))
        value_grad_heads.append(value_gradient.reshape(tok_count, HD))
    grad_keys = jnp.concatenate(key_grad_heads, axis=-1).astype(jnp.bfloat16)
    grad_values = jnp.concatenate(value_grad_heads, axis=-1).astype(jnp.bfloat16)
    return attended, grad_queries, grad_keys, grad_values


def solution(mesh):
    placed = (
        P(("rep", "seq"), None),
        P(("rep", "seq"), None),
        P(("rep", "seq"), None),
        P(("rep", "seq"), None),
    )
    return jax.shard_map(
        body,
        mesh=mesh,
        in_specs=placed,
        out_specs=(
            P(("rep", "seq"), None),
            P(("rep", "seq"), None),
            P(("rep", "seq"), None),
            P(("rep", "seq"), None),
        ),
        check_vma=False,
    )
```

```python
import functools
import math

import jax
import jax.numpy as jnp
from jax import lax
from jax.experimental import pallas as pl
from jax.experimental.pallas import tpu as pltpu
from jax.sharding import PartitionSpec as P

HEADS = 4
HD = 128
BLK = 128
WINDOW = 4


NEG = -1e30
CHUNKS = 2


def passed_along(value, axis, steps):
    count = lax.axis_size(axis)
    first, last = (max(0, -steps), min(count, count - steps))
    return lax.ppermute(value, axis, [(source, source + steps) for source in range(first, last)])


def offset_lists(block_total):
    near_list = list(range(WINDOW + 1))
    far_list = []
    stride = 1
    while stride < block_total:
        if stride > WINDOW:
            far_list.append(stride)
        stride = stride * 2
    return (near_list, far_list)


def allowed_mask(first_block, blocks_dev, offsets):
    block_ids = first_block + jnp.arange(blocks_dev, dtype=jnp.int32)
    offset_arr = jnp.array(offsets, dtype=jnp.int32)
    block_live = block_ids[:, None] - offset_arr[None, :] >= 0
    row_ids = jnp.arange(BLK, dtype=jnp.int32)
    causal = row_ids[:, None] >= row_ids[None, :]
    later_slab = offset_arr > 0
    slab_causal = jnp.logical_or(later_slab[None, :, None], causal[:, None, :])
    allowed = jnp.logical_and(block_live[:, None, :, None], slab_causal[None, :, :, :])
    return allowed.reshape(blocks_dev, BLK, len(offsets) * BLK)


def head_cols(array_in, col_start):
    return array_in[..., col_start : col_start + HD]


def to_blocks(array_in, block_count):
    return array_in.reshape(block_count, BLK, array_in.shape[-1])


def place_slabs(gradient, near_list, lead, span_blocks):
    blocks_dev = gradient.shape[0]
    placed = []
    for slot_index, offset in enumerate(near_list):
        before = lead - offset
        after = span_blocks - before - blocks_dev
        placed.append(jnp.pad(gradient[:, slot_index], ((before, after), (0, 0), (0, 0))))
    total = placed[0]
    for item in placed[1:]:
        total = total + item
    return total


def head_pass(query_per_head, output_gradient_heads, key_slabs, value_slabs, allowed, logit_scale):
    block_count = key_slabs.shape[0]
    key_row_block = key_slabs.reshape(block_count, -1, HD)
    value_row_block = value_slabs.reshape(block_count, -1, HD)
    score_matrix = (
        jnp.einsum(
            "nmv,njv->nmj", query_per_head, key_row_block, preferred_element_type=jnp.float32
        )
        * logit_scale
    )
    score_matrix = jnp.where(allowed, score_matrix, NEG)
    row_max = jnp.max(score_matrix, axis=-1, keepdims=True)
    log_total = row_max + jnp.log(jnp.sum(jnp.exp(score_matrix - row_max), axis=-1, keepdims=True))
    probabilities = jnp.exp(score_matrix - log_total)
    attention_weight = probabilities.astype(jnp.bfloat16)
    attended_per_head = jnp.einsum(
        "jym,jmo->jyo", attention_weight, value_row_block, preferred_element_type=jnp.float32
    ).astype(jnp.bfloat16)
    out_dot = jnp.sum(
        output_gradient_heads.astype(jnp.float32) * attended_per_head.astype(jnp.float32),
        axis=-1,
        keepdims=True,
    )
    probability_gradient = jnp.einsum(
        "nmv,njv->nmj", output_gradient_heads, value_row_block, preferred_element_type=jnp.float32
    )
    score_gradient = (probabilities * (probability_gradient - out_dot)).astype(jnp.bfloat16)
    query_gradient_heads = (
        jnp.einsum(
            "jym,jmo->jyo", score_gradient, key_row_block, preferred_element_type=jnp.float32
        )
        * logit_scale
    ).astype(jnp.bfloat16)
    key_gradient = (
        jnp.einsum(
            "uwj,uwn->ujn", score_gradient, query_per_head, preferred_element_type=jnp.float32
        )
        * logit_scale
    )
    value_gradient = jnp.einsum(
        "uwj,uwn->ujn", attention_weight, output_gradient_heads, preferred_element_type=jnp.float32
    )
    return (
        attended_per_head,
        query_gradient_heads,
        key_gradient,
        value_gradient,
        log_total[..., 0],
        out_dot[..., 0],
    )


def legacy_body(queries, key_tokens, value_tokens, grad_out):
    row_width = queries.shape[1]
    tok_count = queries.shape[0]
    blocks_dev = tok_count // BLK
    rim = (WINDOW + blocks_dev - 1) // blocks_dev
    devices = lax.axis_size("seq")
    near_list, far_list = offset_lists(devices * blocks_dev)
    offsets = near_list + far_list
    near_count = len(near_list)
    logit_scale = 1.0 / math.sqrt(HD)
    span_blocks = (rim + 1) * blocks_dev
    lead = rim * blocks_dev
    earlier_keys = []
    earlier_values = []
    for back in range(rim, 0, -1):
        got_keys, got_values = passed_along((key_tokens, value_tokens), "seq", back)
        earlier_keys.append(got_keys)
        earlier_values.append(got_values)
    span_keys = to_blocks(jnp.concatenate(earlier_keys + [key_tokens], axis=0), span_blocks)
    span_values = to_blocks(jnp.concatenate(earlier_values + [value_tokens], axis=0), span_blocks)
    far_keys = []
    far_values = []
    for stride in far_list:
        got_keys, got_values = passed_along((key_tokens, value_tokens), "seq", stride // blocks_dev)
        far_keys.append(to_blocks(got_keys, blocks_dev))
        far_values.append(to_blocks(got_values, blocks_dev))
    position = lax.axis_index("seq")
    allowed = allowed_mask(position * blocks_dev, blocks_dev, offsets)
    query_blocks = to_blocks(queries, blocks_dev)
    grad_blocks = to_blocks(grad_out, blocks_dev)
    attended_heads = []
    grad_query_heads = []
    near_key_heads = []
    near_value_heads = []
    total_heads = []
    dot_heads = []
    far_key_parts = [[] for stride in far_list]
    far_value_parts = [[] for stride in far_list]
    for head_index in range(HEADS):
        col_start = head_index * HD
        key_slabs = jnp.stack(
            [
                head_cols(span_keys[lead - offset : lead + blocks_dev - offset], col_start)
                for offset in near_list
            ]
            + [head_cols(item, col_start) for item in far_keys],
            axis=1,
        )
        value_slabs = jnp.stack(
            [
                head_cols(span_values[lead - offset : lead + blocks_dev - offset], col_start)
                for offset in near_list
            ]
            + [head_cols(item, col_start) for item in far_values],
            axis=1,
        )
        (
            attended_per_head,
            query_gradient_heads,
            key_gradient,
            value_gradient,
            log_total,
            out_dot,
        ) = head_pass(
            head_cols(query_blocks, col_start),
            head_cols(grad_blocks, col_start),
            key_slabs,
            value_slabs,
            allowed,
            logit_scale,
        )
        key_gradient = key_gradient.reshape(blocks_dev, -1, BLK, HD)
        value_gradient = value_gradient.reshape(blocks_dev, -1, BLK, HD)
        near_key_heads.append(place_slabs(key_gradient, near_list, lead, span_blocks))
        near_value_heads.append(place_slabs(value_gradient, near_list, lead, span_blocks))
        for level_index in range(len(far_list)):
            far_key_parts[level_index].append(
                key_gradient[:, near_count + level_index].astype(jnp.bfloat16)
            )
            far_value_parts[level_index].append(
                value_gradient[:, near_count + level_index].astype(jnp.bfloat16)
            )
        attended_heads.append(attended_per_head)
        grad_query_heads.append(query_gradient_heads)
        total_heads.append(log_total)
        dot_heads.append(out_dot)
    attended = jnp.concatenate(attended_heads, axis=-1).reshape(tok_count, row_width)
    grad_queries = jnp.concatenate(grad_query_heads, axis=-1).reshape(tok_count, row_width)
    near_keys = jnp.concatenate(near_key_heads, axis=-1).reshape((rim + 1) * tok_count, row_width)
    near_values = jnp.concatenate(near_value_heads, axis=-1).reshape(
        (rim + 1) * tok_count, row_width
    )
    total_keys = near_keys[lead * BLK :].astype(jnp.bfloat16).astype(jnp.float32)
    total_values = near_values[lead * BLK :].astype(jnp.bfloat16).astype(jnp.float32)
    for back in range(1, rim + 1):
        piece_start = (rim - back) * tok_count
        part_keys = near_keys[piece_start : piece_start + tok_count].astype(jnp.bfloat16)
        part_values = near_values[piece_start : piece_start + tok_count].astype(jnp.bfloat16)
        back_keys, back_values = passed_along((part_keys, part_values), "seq", -back)
        total_keys = total_keys + back_keys.astype(jnp.float32)
        total_values = total_values + back_values.astype(jnp.float32)
    for level_index, stride in enumerate(far_list):
        part_keys = jnp.concatenate(far_key_parts[level_index], axis=-1).reshape(
            tok_count, row_width
        )
        part_values = jnp.concatenate(far_value_parts[level_index], axis=-1).reshape(
            tok_count, row_width
        )
        got_keys, got_values = passed_along(
            (part_keys, part_values), "seq", -(stride // blocks_dev)
        )
        total_keys = total_keys + got_keys.astype(jnp.float32)
        total_values = total_values + got_values.astype(jnp.float32)
    return (
        attended,
        grad_queries,
        total_keys.astype(jnp.bfloat16),
        total_values.astype(jnp.bfloat16),
    )


def swap_pairs(count):
    return [(source, source ^ 1) for source in range(count) if source ^ 1 < count]


def relay_ok(count, blocks_dev, rim, far_shifts):
    return count % 2 == 0 and blocks_dev == 2 and rim == 2 and (not far_shifts or far_shifts[0] == 4)


def plan(tok_count, devices):
    blocks_dev = tok_count // BLK
    rim = (WINDOW + blocks_dev - 1) // blocks_dev
    near_list, far_list = offset_lists(devices * blocks_dev)
    far_shifts = [stride // blocks_dev for stride in far_list]
    return blocks_dev, rim, near_list, far_list, far_shifts


def row_pass(query_per_head, output_gradient_heads, key_slabs, value_slabs, allowed, logit_scale):
    block_count = key_slabs.shape[0]
    key_row_block = key_slabs.reshape(block_count, -1, HD)
    value_row_block = value_slabs.reshape(block_count, -1, HD)
    score_matrix = (
        jnp.einsum(
            "nmv,njv->nmj", query_per_head, key_row_block, preferred_element_type=jnp.float32
        )
        * logit_scale
    )
    score_matrix = jnp.where(allowed, score_matrix, NEG)
    row_max = jnp.max(score_matrix, axis=-1, keepdims=True)
    log_total = row_max + jnp.log(jnp.sum(jnp.exp(score_matrix - row_max), axis=-1, keepdims=True))
    probabilities = jnp.exp(score_matrix - log_total)
    attention_weight = probabilities.astype(jnp.bfloat16)
    attended_per_head = jnp.einsum(
        "jym,jmo->jyo", attention_weight, value_row_block, preferred_element_type=jnp.float32
    ).astype(jnp.bfloat16)
    out_dot = jnp.sum(
        output_gradient_heads.astype(jnp.float32) * attended_per_head.astype(jnp.float32),
        axis=-1,
        keepdims=True,
    )
    probability_gradient = jnp.einsum(
        "nmv,njv->nmj", output_gradient_heads, value_row_block, preferred_element_type=jnp.float32
    )
    score_gradient = (probabilities * (probability_gradient - out_dot)).astype(jnp.bfloat16)
    query_gradient_heads = (
        jnp.einsum(
            "jym,jmo->jyo", score_gradient, key_row_block, preferred_element_type=jnp.float32
        )
        * logit_scale
    ).astype(jnp.bfloat16)
    return attended_per_head, query_gradient_heads, log_total[..., 0], out_dot[..., 0]


def key_pass(key_per_head, value_per_head, query_slabs, grad_slabs, total_slabs, dot_slabs, allowed, logit_scale):
    block_count = query_slabs.shape[0]
    query_rows = query_slabs.reshape(block_count, -1, HD)
    grad_rows = grad_slabs.reshape(block_count, -1, HD)
    score_matrix = (
        jnp.einsum("nmv,njv->nmj", query_rows, key_per_head, preferred_element_type=jnp.float32)
        * logit_scale
    )
    total_rows = total_slabs.reshape(block_count, -1, 1)
    dot_rows = dot_slabs.reshape(block_count, -1, 1)
    probabilities = jnp.where(allowed, jnp.exp(score_matrix - total_rows), 0.0)
    probability_gradient = jnp.einsum(
        "nmv,njv->nmj", grad_rows, value_per_head, preferred_element_type=jnp.float32
    )
    score_gradient = (probabilities * (probability_gradient - dot_rows)).astype(jnp.bfloat16)
    attention_weight = probabilities.astype(jnp.bfloat16)
    key_gradient = (
        jnp.einsum("nmj,nmv->njv", score_gradient, query_rows, preferred_element_type=jnp.float32)
        * logit_scale
    )
    value_gradient = jnp.einsum(
        "nmj,nmv->njv", attention_weight, grad_rows, preferred_element_type=jnp.float32
    )
    return key_gradient, value_gradient


def key_allowed(first_block, blocks_dev, offsets, block_total):
    block_ids = first_block + jnp.arange(blocks_dev, dtype=jnp.int32)
    offset_arr = jnp.array(offsets, dtype=jnp.int32)
    query_live = block_ids[:, None] + offset_arr[None, :] < block_total
    row_ids = jnp.arange(BLK, dtype=jnp.int32)
    causal = row_ids[:, None] >= row_ids[None, :]
    later_slab = offset_arr > 0
    slab_causal = jnp.logical_or(later_slab[:, None, None], causal[None, :, :])
    allowed = jnp.logical_and(query_live[:, :, None, None], slab_causal[None, :, :, :])
    return allowed.reshape(blocks_dev, len(offsets) * BLK, BLK)


TRANS_B = (((1,), (1,)), ((), ()))


def row_kernel(near_list, far_list, heads, *refs):
    far_count = len(far_list)
    position_ref, query_ref, grad_ref, back2_ref, back1_ref, own_ref = refs[:6]
    far_refs = refs[6 : 6 + far_count]
    attended_ref, grad_query_ref, stats_ref = refs[6 + far_count :]
    span = (back2_ref, back1_ref, own_ref)
    width = heads * HD
    scale = 1.0 / math.sqrt(HD)
    first = 2 * position_ref[0]
    row_ids = lax.broadcasted_iota(jnp.int32, (BLK, BLK), 0)
    col_ids = lax.broadcasted_iota(jnp.int32, (BLK, BLK), 1)
    causal = row_ids >= col_ids
    lane_ids = lax.broadcasted_iota(jnp.int32, (BLK, 2 * heads), 1)
    for block in range(2):
        rows = pl.ds(block * BLK, BLK)
        slabs = []
        for offset in near_list:
            index = 4 + block - offset
            slabs.append((span[index // 2], (index % 2) * BLK, offset))
        for level, offset in enumerate(far_list):
            slabs.append((far_refs[level], block * BLK, offset))
        stats_tile = jnp.zeros((BLK, 2 * heads), jnp.float32)
        for head in range(heads):
            cols = pl.ds(head * HD, HD)
            value_cols = pl.ds(width + head * HD, HD)
            query = query_ref[rows, cols]
            grad = grad_ref[rows, cols]
            scores = []
            for source, start, offset in slabs:
                key = source[pl.ds(start, BLK), cols]
                score = lax.dot_general(query, key, TRANS_B, preferred_element_type=jnp.float32)
                score = score * scale
                live = first + block - offset >= 0
                mask = jnp.logical_and(causal, live) if offset == 0 else jnp.logical_and(
                    row_ids >= 0, live
                )
                scores.append(jnp.where(mask, score, NEG))
            row_max = scores[0].max(axis=-1, keepdims=True)
            for score in scores[1:]:
                row_max = jnp.maximum(row_max, score.max(axis=-1, keepdims=True))
            row_sum = jnp.exp(scores[0] - row_max).sum(axis=-1, keepdims=True)
            for score in scores[1:]:
                row_sum = row_sum + jnp.exp(score - row_max).sum(axis=-1, keepdims=True)
            log_total = row_max + jnp.log(row_sum)
            probs = [jnp.exp(score - log_total) for score in scores]
            attended = jnp.zeros((BLK, HD), jnp.float32)
            for prob, (source, start, offset) in zip(probs, slabs):
                value = source[pl.ds(start, BLK), value_cols]
                attended = attended + jnp.dot(
                    prob.astype(jnp.bfloat16), value, preferred_element_type=jnp.float32
                )
            attended = attended.astype(jnp.bfloat16)
            attended_ref[rows, cols] = attended
            out_dot = jnp.sum(
                grad.astype(jnp.float32) * attended.astype(jnp.float32), axis=-1, keepdims=True
            )
            grad_query = jnp.zeros((BLK, HD), jnp.float32)
            for prob, (source, start, offset) in zip(probs, slabs):
                value = source[pl.ds(start, BLK), value_cols]
                key = source[pl.ds(start, BLK), cols]
                prob_grad = lax.dot_general(grad, value, TRANS_B, preferred_element_type=jnp.float32)
                score_grad = (prob * (prob_grad - out_dot)).astype(jnp.bfloat16)
                grad_query = grad_query + jnp.dot(
                    score_grad, key, preferred_element_type=jnp.float32
                )
            grad_query_ref[rows, cols] = (grad_query * scale).astype(jnp.bfloat16)
            stats_tile = stats_tile + jnp.where(lane_ids == head, log_total, 0.0)
            stats_tile = stats_tile + jnp.where(lane_ids == heads + head, out_dot, 0.0)
        stats_ref[rows, :] = stats_tile


def key_kernel(near_list, far_list, heads, block_total, *refs):
    far_count = len(far_list)
    position_ref, own_ref, rows0_ref, rows1_ref, rows2_ref = refs[:5]
    far_rows = refs[5 : 5 + far_count]
    stats0_ref, stats1_ref, stats2_ref = refs[5 + far_count : 8 + far_count]
    far_stats = refs[8 + far_count : 8 + 2 * far_count]
    grad_key_ref, grad_value_ref = refs[8 + 2 * far_count :]
    span_rows = (rows0_ref, rows1_ref, rows2_ref)
    span_stats = (stats0_ref, stats1_ref, stats2_ref)
    width = heads * HD
    scale = 1.0 / math.sqrt(HD)
    first = 2 * position_ref[0]
    row_ids = lax.broadcasted_iota(jnp.int32, (BLK, BLK), 0)
    col_ids = lax.broadcasted_iota(jnp.int32, (BLK, BLK), 1)
    causal = row_ids >= col_ids
    lane_ids = lax.broadcasted_iota(jnp.int32, (BLK, 2 * heads), 1)
    for block in range(2):
        rows = pl.ds(block * BLK, BLK)
        slabs = []
        for offset in near_list:
            index = block + offset
            slabs.append((span_rows[index // 2], span_stats[index // 2], (index % 2) * BLK, offset))
        for level, offset in enumerate(far_list):
            slabs.append((far_rows[level], far_stats[level], block * BLK, offset))
        for head in range(heads):
            cols = pl.ds(head * HD, HD)
            value_cols = pl.ds(width + head * HD, HD)
            key = own_ref[rows, cols]
            value = own_ref[rows, value_cols]
            grad_key = jnp.zeros((BLK, HD), jnp.float32)
            grad_value = jnp.zeros((BLK, HD), jnp.float32)
            for source, stats, start, offset in slabs:
                query = source[pl.ds(start, BLK), cols]
                grad = source[pl.ds(start, BLK), value_cols]
                tile = stats[pl.ds(start, BLK), :]
                log_total = jnp.sum(jnp.where(lane_ids == head, tile, 0.0), axis=-1, keepdims=True)
                out_dot = jnp.sum(
                    jnp.where(lane_ids == heads + head, tile, 0.0), axis=-1, keepdims=True
                )
                score = lax.dot_general(query, key, TRANS_B, preferred_element_type=jnp.float32)
                score = score * scale
                live = first + block + offset < block_total
                mask = jnp.logical_and(causal, live) if offset == 0 else jnp.logical_and(
                    row_ids >= 0, live
                )
                prob = jnp.where(mask, jnp.exp(score - log_total), 0.0)
                prob_grad = lax.dot_general(grad, value, TRANS_B, preferred_element_type=jnp.float32)
                score_grad = prob * (prob_grad - out_dot)
                grad_value = grad_value + jnp.dot(
                    prob.T.astype(jnp.bfloat16), grad, preferred_element_type=jnp.float32
                )
                grad_key = grad_key + jnp.dot(
                    score_grad.T.astype(jnp.bfloat16), query, preferred_element_type=jnp.float32
                )
            grad_key_ref[rows, cols] = (grad_key * scale).astype(jnp.bfloat16)
            grad_value_ref[rows, cols] = grad_value.astype(jnp.bfloat16)


def smem_spec():
    return pl.BlockSpec(memory_space=pltpu.SMEM)


def vmem_spec():
    return pl.BlockSpec(memory_space=pltpu.VMEM)


def body(queries, key_tokens, value_tokens, grad_out):
    row_width = queries.shape[1]
    tok_count = queries.shape[0]
    devices = lax.axis_size("seq")
    blocks_dev, rim, near_list, far_list, far_shifts = plan(tok_count, devices)
    if not relay_ok(devices, blocks_dev, rim, far_shifts):
        return legacy_body(queries, key_tokens, value_tokens, grad_out)
    heads = row_width // HD
    offsets = near_list + far_list
    logit_scale = 1.0 / math.sqrt(HD)
    span_blocks = (rim + 1) * blocks_dev
    lead = rim * blocks_dev
    position = lax.axis_index("seq")
    odd = (position % 2) == 1
    pairs = swap_pairs(devices)
    keys_values = jnp.concatenate([key_tokens, value_tokens], axis=1)
    queries_grads = jnp.concatenate([queries, grad_out], axis=1)
    back2 = passed_along(keys_values, "seq", 2)
    ahead2 = passed_along(queries_grads, "seq", -2)
    swap_one = lax.ppermute(jnp.where(odd, queries_grads, keys_values), "seq", pairs)
    back4 = passed_along(back2, "seq", 2)
    ahead4 = passed_along(ahead2, "seq", -2)
    swap_two = lax.ppermute(jnp.where(odd, back2, ahead2), "seq", pairs)
    back1 = jnp.where(odd, swap_one, swap_two)
    ahead1 = jnp.where(odd, swap_two, swap_one)
    far_back = [back4] + [passed_along(keys_values, "seq", shift) for shift in far_shifts[1:]]
    far_ahead = [ahead4] + [passed_along(queries_grads, "seq", -shift) for shift in far_shifts[1:]]
    far_back = far_back[: len(far_shifts)]
    far_ahead = far_ahead[: len(far_shifts)]

    position_arr = jnp.reshape(position, (1,)).astype(jnp.int32)
    far_offsets = list(far_list)
    attended, grad_queries, stats = pl.pallas_call(
        functools.partial(row_kernel, near_list, far_offsets, heads),
        out_shape=(
            jax.ShapeDtypeStruct((tok_count, row_width), jnp.bfloat16),
            jax.ShapeDtypeStruct((tok_count, row_width), jnp.bfloat16),
            jax.ShapeDtypeStruct((tok_count, 2 * heads), jnp.float32),
        ),
        in_specs=[smem_spec()] + [vmem_spec()] * (5 + len(far_back)),
        out_specs=(vmem_spec(), vmem_spec(), vmem_spec()),
        name="rows_pass",
    )(position_arr, queries, grad_out, back2, back1, keys_values, *far_back)
    stats_one = passed_along(stats, "seq", -1)
    stats_two = passed_along(stats, "seq", -2)
    far_stats = [passed_along(stats, "seq", -shift) for shift in far_shifts]
    grad_keys, grad_values = pl.pallas_call(
        functools.partial(key_kernel, near_list, far_offsets, heads, devices * blocks_dev),
        out_shape=(
            jax.ShapeDtypeStruct((tok_count, row_width), jnp.bfloat16),
            jax.ShapeDtypeStruct((tok_count, row_width), jnp.bfloat16),
        ),
        in_specs=[smem_spec()] + [vmem_spec()] * (7 + 2 * len(far_ahead)),
        out_specs=(vmem_spec(), vmem_spec()),
        name="keys_pass",
    )(
        position_arr,
        keys_values,
        queries_grads,
        ahead1,
        ahead2,
        *far_ahead,
        stats,
        stats_one,
        stats_two,
        *far_stats,
    )
    return attended, grad_queries, grad_keys, grad_values


def solution(mesh):
    placed = (
        P(("rep", "seq"), None),
        P(("rep", "seq"), None),
        P(("rep", "seq"), None),
        P(("rep", "seq"), None),
    )
    return jax.shard_map(
        body,
        mesh=mesh,
        in_specs=placed,
        out_specs=(
            P(("rep", "seq"), None),
            P(("rep", "seq"), None),
            P(("rep", "seq"), None),
            P(("rep", "seq"), None),
        ),
        check_vma=False,
    )
```

```python
import functools
import math

import jax
import jax.numpy as jnp
from jax import lax
from jax.experimental import pallas as pl
from jax.experimental.pallas import tpu as pltpu
from jax.sharding import PartitionSpec as P

HEADS = 4
HD = 128
BLK = 128
WINDOW = 4


NEG = -1e30
CHUNKS = 2


def passed_along(value, axis, steps):
    count = lax.axis_size(axis)
    first, last = (max(0, -steps), min(count, count - steps))
    return lax.ppermute(value, axis, [(source, source + steps) for source in range(first, last)])


def offset_lists(block_total):
    near_list = list(range(WINDOW + 1))
    far_list = []
    stride = 1
    while stride < block_total:
        if stride > WINDOW:
            far_list.append(stride)
        stride = stride * 2
    return (near_list, far_list)


def allowed_mask(first_block, blocks_dev, offsets):
    block_ids = first_block + jnp.arange(blocks_dev, dtype=jnp.int32)
    offset_arr = jnp.array(offsets, dtype=jnp.int32)
    block_live = block_ids[:, None] - offset_arr[None, :] >= 0
    row_ids = jnp.arange(BLK, dtype=jnp.int32)
    causal = row_ids[:, None] >= row_ids[None, :]
    later_slab = offset_arr > 0
    slab_causal = jnp.logical_or(later_slab[None, :, None], causal[:, None, :])
    allowed = jnp.logical_and(block_live[:, None, :, None], slab_causal[None, :, :, :])
    return allowed.reshape(blocks_dev, BLK, len(offsets) * BLK)


def head_cols(array_in, col_start):
    return array_in[..., col_start : col_start + HD]


def to_blocks(array_in, block_count):
    return array_in.reshape(block_count, BLK, array_in.shape[-1])


def place_slabs(gradient, near_list, lead, span_blocks):
    blocks_dev = gradient.shape[0]
    placed = []
    for slot_index, offset in enumerate(near_list):
        before = lead - offset
        after = span_blocks - before - blocks_dev
        placed.append(jnp.pad(gradient[:, slot_index], ((before, after), (0, 0), (0, 0))))
    total = placed[0]
    for item in placed[1:]:
        total = total + item
    return total


def head_pass(query_per_head, output_gradient_heads, key_slabs, value_slabs, allowed, logit_scale):
    block_count = key_slabs.shape[0]
    key_row_block = key_slabs.reshape(block_count, -1, HD)
    value_row_block = value_slabs.reshape(block_count, -1, HD)
    score_matrix = (
        jnp.einsum(
            "nmv,njv->nmj", query_per_head, key_row_block, preferred_element_type=jnp.float32
        )
        * logit_scale
    )
    score_matrix = jnp.where(allowed, score_matrix, NEG)
    row_max = jnp.max(score_matrix, axis=-1, keepdims=True)
    log_total = row_max + jnp.log(jnp.sum(jnp.exp(score_matrix - row_max), axis=-1, keepdims=True))
    probabilities = jnp.exp(score_matrix - log_total)
    attention_weight = probabilities.astype(jnp.bfloat16)
    attended_per_head = jnp.einsum(
        "jym,jmo->jyo", attention_weight, value_row_block, preferred_element_type=jnp.float32
    ).astype(jnp.bfloat16)
    out_dot = jnp.sum(
        output_gradient_heads.astype(jnp.float32) * attended_per_head.astype(jnp.float32),
        axis=-1,
        keepdims=True,
    )
    probability_gradient = jnp.einsum(
        "nmv,njv->nmj", output_gradient_heads, value_row_block, preferred_element_type=jnp.float32
    )
    score_gradient = (probabilities * (probability_gradient - out_dot)).astype(jnp.bfloat16)
    query_gradient_heads = (
        jnp.einsum(
            "jym,jmo->jyo", score_gradient, key_row_block, preferred_element_type=jnp.float32
        )
        * logit_scale
    ).astype(jnp.bfloat16)
    key_gradient = (
        jnp.einsum(
            "uwj,uwn->ujn", score_gradient, query_per_head, preferred_element_type=jnp.float32
        )
        * logit_scale
    )
    value_gradient = jnp.einsum(
        "uwj,uwn->ujn", attention_weight, output_gradient_heads, preferred_element_type=jnp.float32
    )
    return (
        attended_per_head,
        query_gradient_heads,
        key_gradient,
        value_gradient,
        log_total[..., 0],
        out_dot[..., 0],
    )


def legacy_body(queries, key_tokens, value_tokens, grad_out):
    row_width = queries.shape[1]
    tok_count = queries.shape[0]
    blocks_dev = tok_count // BLK
    rim = (WINDOW + blocks_dev - 1) // blocks_dev
    devices = lax.axis_size("seq")
    near_list, far_list = offset_lists(devices * blocks_dev)
    offsets = near_list + far_list
    near_count = len(near_list)
    logit_scale = 1.0 / math.sqrt(HD)
    span_blocks = (rim + 1) * blocks_dev
    lead = rim * blocks_dev
    earlier_keys = []
    earlier_values = []
    for back in range(rim, 0, -1):
        got_keys, got_values = passed_along((key_tokens, value_tokens), "seq", back)
        earlier_keys.append(got_keys)
        earlier_values.append(got_values)
    span_keys = to_blocks(jnp.concatenate(earlier_keys + [key_tokens], axis=0), span_blocks)
    span_values = to_blocks(jnp.concatenate(earlier_values + [value_tokens], axis=0), span_blocks)
    far_keys = []
    far_values = []
    for stride in far_list:
        got_keys, got_values = passed_along((key_tokens, value_tokens), "seq", stride // blocks_dev)
        far_keys.append(to_blocks(got_keys, blocks_dev))
        far_values.append(to_blocks(got_values, blocks_dev))
    position = lax.axis_index("seq")
    allowed = allowed_mask(position * blocks_dev, blocks_dev, offsets)
    query_blocks = to_blocks(queries, blocks_dev)
    grad_blocks = to_blocks(grad_out, blocks_dev)
    attended_heads = []
    grad_query_heads = []
    near_key_heads = []
    near_value_heads = []
    total_heads = []
    dot_heads = []
    far_key_parts = [[] for stride in far_list]
    far_value_parts = [[] for stride in far_list]
    for head_index in range(HEADS):
        col_start = head_index * HD
        key_slabs = jnp.stack(
            [
                head_cols(span_keys[lead - offset : lead + blocks_dev - offset], col_start)
                for offset in near_list
            ]
            + [head_cols(item, col_start) for item in far_keys],
            axis=1,
        )
        value_slabs = jnp.stack(
            [
                head_cols(span_values[lead - offset : lead + blocks_dev - offset], col_start)
                for offset in near_list
            ]
            + [head_cols(item, col_start) for item in far_values],
            axis=1,
        )
        (
            attended_per_head,
            query_gradient_heads,
            key_gradient,
            value_gradient,
            log_total,
            out_dot,
        ) = head_pass(
            head_cols(query_blocks, col_start),
            head_cols(grad_blocks, col_start),
            key_slabs,
            value_slabs,
            allowed,
            logit_scale,
        )
        key_gradient = key_gradient.reshape(blocks_dev, -1, BLK, HD)
        value_gradient = value_gradient.reshape(blocks_dev, -1, BLK, HD)
        near_key_heads.append(place_slabs(key_gradient, near_list, lead, span_blocks))
        near_value_heads.append(place_slabs(value_gradient, near_list, lead, span_blocks))
        for level_index in range(len(far_list)):
            far_key_parts[level_index].append(
                key_gradient[:, near_count + level_index].astype(jnp.bfloat16)
            )
            far_value_parts[level_index].append(
                value_gradient[:, near_count + level_index].astype(jnp.bfloat16)
            )
        attended_heads.append(attended_per_head)
        grad_query_heads.append(query_gradient_heads)
        total_heads.append(log_total)
        dot_heads.append(out_dot)
    attended = jnp.concatenate(attended_heads, axis=-1).reshape(tok_count, row_width)
    grad_queries = jnp.concatenate(grad_query_heads, axis=-1).reshape(tok_count, row_width)
    near_keys = jnp.concatenate(near_key_heads, axis=-1).reshape((rim + 1) * tok_count, row_width)
    near_values = jnp.concatenate(near_value_heads, axis=-1).reshape(
        (rim + 1) * tok_count, row_width
    )
    total_keys = near_keys[lead * BLK :].astype(jnp.bfloat16).astype(jnp.float32)
    total_values = near_values[lead * BLK :].astype(jnp.bfloat16).astype(jnp.float32)
    for back in range(1, rim + 1):
        piece_start = (rim - back) * tok_count
        part_keys = near_keys[piece_start : piece_start + tok_count].astype(jnp.bfloat16)
        part_values = near_values[piece_start : piece_start + tok_count].astype(jnp.bfloat16)
        back_keys, back_values = passed_along((part_keys, part_values), "seq", -back)
        total_keys = total_keys + back_keys.astype(jnp.float32)
        total_values = total_values + back_values.astype(jnp.float32)
    for level_index, stride in enumerate(far_list):
        part_keys = jnp.concatenate(far_key_parts[level_index], axis=-1).reshape(
            tok_count, row_width
        )
        part_values = jnp.concatenate(far_value_parts[level_index], axis=-1).reshape(
            tok_count, row_width
        )
        got_keys, got_values = passed_along(
            (part_keys, part_values), "seq", -(stride // blocks_dev)
        )
        total_keys = total_keys + got_keys.astype(jnp.float32)
        total_values = total_values + got_values.astype(jnp.float32)
    return (
        attended,
        grad_queries,
        total_keys.astype(jnp.bfloat16),
        total_values.astype(jnp.bfloat16),
    )


def swap_pairs(count):
    return [(source, source ^ 1) for source in range(count) if source ^ 1 < count]


def relay_ok(count, blocks_dev, rim, far_shifts):
    return count % 2 == 0 and blocks_dev == 2 and rim == 2 and (not far_shifts or far_shifts[0] == 4)


def plan(tok_count, devices):
    blocks_dev = tok_count // BLK
    rim = (WINDOW + blocks_dev - 1) // blocks_dev
    near_list, far_list = offset_lists(devices * blocks_dev)
    far_shifts = [stride // blocks_dev for stride in far_list]
    return blocks_dev, rim, near_list, far_list, far_shifts


def row_pass(query_per_head, output_gradient_heads, key_slabs, value_slabs, allowed, logit_scale):
    block_count = key_slabs.shape[0]
    key_row_block = key_slabs.reshape(block_count, -1, HD)
    value_row_block = value_slabs.reshape(block_count, -1, HD)
    score_matrix = (
        jnp.einsum(
            "nmv,njv->nmj", query_per_head, key_row_block, preferred_element_type=jnp.float32
        )
        * logit_scale
    )
    score_matrix = jnp.where(allowed, score_matrix, NEG)
    row_max = jnp.max(score_matrix, axis=-1, keepdims=True)
    log_total = row_max + jnp.log(jnp.sum(jnp.exp(score_matrix - row_max), axis=-1, keepdims=True))
    probabilities = jnp.exp(score_matrix - log_total)
    attention_weight = probabilities.astype(jnp.bfloat16)
    attended_per_head = jnp.einsum(
        "jym,jmo->jyo", attention_weight, value_row_block, preferred_element_type=jnp.float32
    ).astype(jnp.bfloat16)
    out_dot = jnp.sum(
        output_gradient_heads.astype(jnp.float32) * attended_per_head.astype(jnp.float32),
        axis=-1,
        keepdims=True,
    )
    probability_gradient = jnp.einsum(
        "nmv,njv->nmj", output_gradient_heads, value_row_block, preferred_element_type=jnp.float32
    )
    score_gradient = (probabilities * (probability_gradient - out_dot)).astype(jnp.bfloat16)
    query_gradient_heads = (
        jnp.einsum(
            "jym,jmo->jyo", score_gradient, key_row_block, preferred_element_type=jnp.float32
        )
        * logit_scale
    ).astype(jnp.bfloat16)
    return attended_per_head, query_gradient_heads, log_total[..., 0], out_dot[..., 0]


def key_pass(key_per_head, value_per_head, query_slabs, grad_slabs, total_slabs, dot_slabs, allowed, logit_scale):
    block_count = query_slabs.shape[0]
    query_rows = query_slabs.reshape(block_count, -1, HD)
    grad_rows = grad_slabs.reshape(block_count, -1, HD)
    score_matrix = (
        jnp.einsum("nmv,njv->nmj", query_rows, key_per_head, preferred_element_type=jnp.float32)
        * logit_scale
    )
    total_rows = total_slabs.reshape(block_count, -1, 1)
    dot_rows = dot_slabs.reshape(block_count, -1, 1)
    probabilities = jnp.where(allowed, jnp.exp(score_matrix - total_rows), 0.0)
    probability_gradient = jnp.einsum(
        "nmv,njv->nmj", grad_rows, value_per_head, preferred_element_type=jnp.float32
    )
    score_gradient = (probabilities * (probability_gradient - dot_rows)).astype(jnp.bfloat16)
    attention_weight = probabilities.astype(jnp.bfloat16)
    key_gradient = (
        jnp.einsum("nmj,nmv->njv", score_gradient, query_rows, preferred_element_type=jnp.float32)
        * logit_scale
    )
    value_gradient = jnp.einsum(
        "nmj,nmv->njv", attention_weight, grad_rows, preferred_element_type=jnp.float32
    )
    return key_gradient, value_gradient


def key_allowed(first_block, blocks_dev, offsets, block_total):
    block_ids = first_block + jnp.arange(blocks_dev, dtype=jnp.int32)
    offset_arr = jnp.array(offsets, dtype=jnp.int32)
    query_live = block_ids[:, None] + offset_arr[None, :] < block_total
    row_ids = jnp.arange(BLK, dtype=jnp.int32)
    causal = row_ids[:, None] >= row_ids[None, :]
    later_slab = offset_arr > 0
    slab_causal = jnp.logical_or(later_slab[:, None, None], causal[None, :, :])
    allowed = jnp.logical_and(query_live[:, :, None, None], slab_causal[None, :, :, :])
    return allowed.reshape(blocks_dev, len(offsets) * BLK, BLK)


TRANS_B = (((1,), (1,)), ((), ()))


def row_kernel(near_count, far_list, heads, *refs):
    far_count = len(far_list)
    position_ref, query_ref, grad_ref, span_ref = refs[:4]
    far_refs = refs[4 : 4 + far_count]
    attended_ref, grad_query_ref, stats_ref = refs[4 + far_count :]
    width = heads * HD
    near_rows = near_count * BLK
    scale = 1.0 / math.sqrt(HD)
    first = 2 * position_ref[0]
    near_row_ids = lax.broadcasted_iota(jnp.int32, (BLK, near_rows), 0)
    near_col_ids = lax.broadcasted_iota(jnp.int32, (BLK, near_rows), 1)
    near_offset = (near_count - 1) - near_col_ids // BLK
    near_causal = jnp.logical_or(near_offset > 0, near_row_ids >= near_col_ids % BLK)
    lane_ids = lax.broadcasted_iota(jnp.int32, (BLK, 2 * heads), 1)
    for block in range(2):
        rows = pl.ds(block * BLK, BLK)
        near_span = pl.ds(block * BLK, near_rows)
        near_mask = jnp.logical_and(near_causal, first + block - near_offset >= 0)
        far_live = [first + block - offset >= 0 for offset in far_list]
        stats_tile = jnp.zeros((BLK, 2 * heads), jnp.float32)
        for head in range(heads):
            cols = pl.ds(head * HD, HD)
            value_cols = pl.ds(width + head * HD, HD)
            query = query_ref[rows, cols]
            grad = grad_ref[rows, cols]
            keys = [span_ref[near_span, cols]] + [item[rows, cols] for item in far_refs]
            values = [span_ref[near_span, value_cols]] + [item[rows, value_cols] for item in far_refs]
            masks = [near_mask] + far_live
            scores = []
            for key, mask in zip(keys, masks):
                score = lax.dot_general(query, key, TRANS_B, preferred_element_type=jnp.float32)
                scores.append(jnp.where(mask, score * scale, NEG))
            row_max = scores[0].max(axis=-1, keepdims=True)
            for score in scores[1:]:
                row_max = jnp.maximum(row_max, score.max(axis=-1, keepdims=True))
            shifted = [jnp.exp(score - row_max) for score in scores]
            row_sum = shifted[0].sum(axis=-1, keepdims=True)
            for item in shifted[1:]:
                row_sum = row_sum + item.sum(axis=-1, keepdims=True)
            log_total = row_max + jnp.log(row_sum)
            inverse = 1.0 / row_sum
            probs = [item * inverse for item in shifted]
            attended = jnp.zeros((BLK, HD), jnp.float32)
            for prob, value in zip(probs, values):
                attended = attended + jnp.dot(
                    prob.astype(jnp.bfloat16), value, preferred_element_type=jnp.float32
                )
            attended = attended.astype(jnp.bfloat16)
            attended_ref[rows, cols] = attended
            out_dot = jnp.sum(
                grad.astype(jnp.float32) * attended.astype(jnp.float32), axis=-1, keepdims=True
            )
            grad_query = jnp.zeros((BLK, HD), jnp.float32)
            for prob, key, value in zip(probs, keys, values):
                prob_grad = lax.dot_general(grad, value, TRANS_B, preferred_element_type=jnp.float32)
                score_grad = (prob * (prob_grad - out_dot)).astype(jnp.bfloat16)
                grad_query = grad_query + jnp.dot(
                    score_grad, key, preferred_element_type=jnp.float32
                )
            grad_query_ref[rows, cols] = (grad_query * scale).astype(jnp.bfloat16)
            stats_tile = stats_tile + jnp.where(lane_ids == head, log_total, 0.0)
            stats_tile = stats_tile + jnp.where(lane_ids == heads + head, out_dot, 0.0)
        stats_ref[rows, :] = stats_tile


def key_kernel(near_count, far_list, heads, block_total, *refs):
    far_count = len(far_list)
    position_ref, own_ref, span_ref, stats_span_ref = refs[:4]
    far_rows = refs[4 : 4 + far_count]
    far_stats = refs[4 + far_count : 4 + 2 * far_count]
    grad_key_ref, grad_value_ref = refs[4 + 2 * far_count :]
    width = heads * HD
    near_rows = near_count * BLK
    scale = 1.0 / math.sqrt(HD)
    first = 2 * position_ref[0]
    near_row_ids = lax.broadcasted_iota(jnp.int32, (near_rows, BLK), 0)
    near_col_ids = lax.broadcasted_iota(jnp.int32, (near_rows, BLK), 1)
    near_offset = near_row_ids // BLK
    near_causal = jnp.logical_or(near_offset > 0, near_row_ids % BLK >= near_col_ids)
    near_lanes = lax.broadcasted_iota(jnp.int32, (near_rows, 2 * heads), 1)
    far_lanes = lax.broadcasted_iota(jnp.int32, (BLK, 2 * heads), 1)
    for block in range(2):
        rows = pl.ds(block * BLK, BLK)
        near_span = pl.ds(block * BLK, near_rows)
        near_mask = jnp.logical_and(near_causal, first + block + near_offset < block_total)
        far_live = [first + block + offset < block_total for offset in far_list]
        masks = [near_mask] + far_live
        stat_tiles = [stats_span_ref[near_span, :]] + [item[rows, :] for item in far_stats]
        lanes = [near_lanes] + [far_lanes] * far_count
        for head in range(heads):
            cols = pl.ds(head * HD, HD)
            value_cols = pl.ds(width + head * HD, HD)
            key = own_ref[rows, cols]
            value = own_ref[rows, value_cols]
            queries = [span_ref[near_span, cols]] + [item[rows, cols] for item in far_rows]
            grads = [span_ref[near_span, value_cols]] + [item[rows, value_cols] for item in far_rows]
            grad_key = jnp.zeros((BLK, HD), jnp.float32)
            grad_value = jnp.zeros((BLK, HD), jnp.float32)
            for query, grad, tile, lane, mask in zip(queries, grads, stat_tiles, lanes, masks):
                log_total = jnp.sum(jnp.where(lane == head, tile, 0.0), axis=-1, keepdims=True)
                out_dot = jnp.sum(jnp.where(lane == heads + head, tile, 0.0), axis=-1, keepdims=True)
                score = lax.dot_general(query, key, TRANS_B, preferred_element_type=jnp.float32)
                prob = jnp.where(mask, jnp.exp(score * scale - log_total), 0.0)
                prob_grad = lax.dot_general(grad, value, TRANS_B, preferred_element_type=jnp.float32)
                score_grad = prob * (prob_grad - out_dot)
                grad_value = grad_value + jnp.dot(
                    prob.T.astype(jnp.bfloat16), grad, preferred_element_type=jnp.float32
                )
                grad_key = grad_key + jnp.dot(
                    score_grad.T.astype(jnp.bfloat16), query, preferred_element_type=jnp.float32
                )
            grad_key_ref[rows, cols] = (grad_key * scale).astype(jnp.bfloat16)
            grad_value_ref[rows, cols] = grad_value.astype(jnp.bfloat16)


def smem_spec():
    return pl.BlockSpec(memory_space=pltpu.SMEM)


def vmem_spec():
    return pl.BlockSpec(memory_space=pltpu.VMEM)


def body(queries, key_tokens, value_tokens, grad_out):
    row_width = queries.shape[1]
    tok_count = queries.shape[0]
    devices = lax.axis_size("seq")
    blocks_dev, rim, near_list, far_list, far_shifts = plan(tok_count, devices)
    if not relay_ok(devices, blocks_dev, rim, far_shifts):
        return legacy_body(queries, key_tokens, value_tokens, grad_out)
    heads = row_width // HD
    offsets = near_list + far_list
    logit_scale = 1.0 / math.sqrt(HD)
    span_blocks = (rim + 1) * blocks_dev
    lead = rim * blocks_dev
    position = lax.axis_index("seq")
    odd = (position % 2) == 1
    pairs = swap_pairs(devices)
    keys_values = jnp.concatenate([key_tokens, value_tokens], axis=1)
    queries_grads = jnp.concatenate([queries, grad_out], axis=1)
    back2 = passed_along(keys_values, "seq", 2)
    ahead2 = passed_along(queries_grads, "seq", -2)
    swap_one = lax.ppermute(jnp.where(odd, queries_grads, keys_values), "seq", pairs)
    back4 = passed_along(back2, "seq", 2)
    ahead4 = passed_along(ahead2, "seq", -2)
    swap_two = lax.ppermute(jnp.where(odd, back2, ahead2), "seq", pairs)
    back1 = jnp.where(odd, swap_one, swap_two)
    ahead1 = jnp.where(odd, swap_two, swap_one)
    far_back = [back4] + [passed_along(keys_values, "seq", shift) for shift in far_shifts[1:]]
    far_ahead = [ahead4] + [passed_along(queries_grads, "seq", -shift) for shift in far_shifts[1:]]
    far_back = far_back[: len(far_shifts)]
    far_ahead = far_ahead[: len(far_shifts)]

    position_arr = jnp.reshape(position, (1,)).astype(jnp.int32)
    far_offsets = list(far_list)
    attended, grad_queries, stats = pl.pallas_call(
        functools.partial(row_kernel, len(near_list), far_offsets, heads),
        out_shape=(
            jax.ShapeDtypeStruct((tok_count, row_width), jnp.bfloat16),
            jax.ShapeDtypeStruct((tok_count, row_width), jnp.bfloat16),
            jax.ShapeDtypeStruct((tok_count, 2 * heads), jnp.float32),
        ),
        in_specs=[smem_spec()] + [vmem_spec()] * (3 + len(far_back)),
        out_specs=(vmem_spec(), vmem_spec(), vmem_spec()),
        name="rows_pass",
    )(
        position_arr,
        queries,
        grad_out,
        jnp.concatenate([back2, back1, keys_values], axis=0),
        *far_back,
    )
    stats_one = passed_along(stats, "seq", -1)
    stats_two = passed_along(stats, "seq", -2)
    far_stats = [passed_along(stats, "seq", -shift) for shift in far_shifts]
    grad_keys, grad_values = pl.pallas_call(
        functools.partial(key_kernel, len(near_list), far_offsets, heads, devices * blocks_dev),
        out_shape=(
            jax.ShapeDtypeStruct((tok_count, row_width), jnp.bfloat16),
            jax.ShapeDtypeStruct((tok_count, row_width), jnp.bfloat16),
        ),
        in_specs=[smem_spec()] + [vmem_spec()] * (3 + 2 * len(far_ahead)),
        out_specs=(vmem_spec(), vmem_spec()),
        name="keys_pass",
    )(
        position_arr,
        keys_values,
        jnp.concatenate([queries_grads, ahead1, ahead2], axis=0),
        jnp.concatenate([stats, stats_one, stats_two], axis=0),
        *far_ahead,
        *far_stats,
    )
    return attended, grad_queries, grad_keys, grad_values


def solution(mesh):
    placed = (
        P(("rep", "seq"), None),
        P(("rep", "seq"), None),
        P(("rep", "seq"), None),
        P(("rep", "seq"), None),
    )
    return jax.shard_map(
        body,
        mesh=mesh,
        in_specs=placed,
        out_specs=(
            P(("rep", "seq"), None),
            P(("rep", "seq"), None),
            P(("rep", "seq"), None),
            P(("rep", "seq"), None),
        ),
        check_vma=False,
    )
```

```python
import functools
import math

import jax
import jax.numpy as jnp
from jax import lax
from jax.experimental import pallas as pl
from jax.experimental.pallas import tpu as pltpu
from jax.sharding import PartitionSpec as P

HEADS = 4
HD = 128
BLK = 128
WINDOW = 4


NEG = -1e30
CHUNKS = 2


def passed_along(value, axis, steps):
    count = lax.axis_size(axis)
    first, last = (max(0, -steps), min(count, count - steps))
    return lax.ppermute(value, axis, [(source, source + steps) for source in range(first, last)])


def offset_lists(block_total):
    near_list = list(range(WINDOW + 1))
    far_list = []
    stride = 1
    while stride < block_total:
        if stride > WINDOW:
            far_list.append(stride)
        stride = stride * 2
    return (near_list, far_list)


def allowed_mask(first_block, blocks_dev, offsets):
    block_ids = first_block + jnp.arange(blocks_dev, dtype=jnp.int32)
    offset_arr = jnp.array(offsets, dtype=jnp.int32)
    block_live = block_ids[:, None] - offset_arr[None, :] >= 0
    row_ids = jnp.arange(BLK, dtype=jnp.int32)
    causal = row_ids[:, None] >= row_ids[None, :]
    later_slab = offset_arr > 0
    slab_causal = jnp.logical_or(later_slab[None, :, None], causal[:, None, :])
    allowed = jnp.logical_and(block_live[:, None, :, None], slab_causal[None, :, :, :])
    return allowed.reshape(blocks_dev, BLK, len(offsets) * BLK)


def head_cols(array_in, col_start):
    return array_in[..., col_start : col_start + HD]


def to_blocks(array_in, block_count):
    return array_in.reshape(block_count, BLK, array_in.shape[-1])


def place_slabs(gradient, near_list, lead, span_blocks):
    blocks_dev = gradient.shape[0]
    placed = []
    for slot_index, offset in enumerate(near_list):
        before = lead - offset
        after = span_blocks - before - blocks_dev
        placed.append(jnp.pad(gradient[:, slot_index], ((before, after), (0, 0), (0, 0))))
    total = placed[0]
    for item in placed[1:]:
        total = total + item
    return total


def head_pass(query_per_head, output_gradient_heads, key_slabs, value_slabs, allowed, logit_scale):
    block_count = key_slabs.shape[0]
    key_row_block = key_slabs.reshape(block_count, -1, HD)
    value_row_block = value_slabs.reshape(block_count, -1, HD)
    score_matrix = (
        jnp.einsum(
            "nmv,njv->nmj", query_per_head, key_row_block, preferred_element_type=jnp.float32
        )
        * logit_scale
    )
    score_matrix = jnp.where(allowed, score_matrix, NEG)
    row_max = jnp.max(score_matrix, axis=-1, keepdims=True)
    log_total = row_max + jnp.log(jnp.sum(jnp.exp(score_matrix - row_max), axis=-1, keepdims=True))
    probabilities = jnp.exp(score_matrix - log_total)
    attention_weight = probabilities.astype(jnp.bfloat16)
    attended_per_head = jnp.einsum(
        "jym,jmo->jyo", attention_weight, value_row_block, preferred_element_type=jnp.float32
    ).astype(jnp.bfloat16)
    out_dot = jnp.sum(
        output_gradient_heads.astype(jnp.float32) * attended_per_head.astype(jnp.float32),
        axis=-1,
        keepdims=True,
    )
    probability_gradient = jnp.einsum(
        "nmv,njv->nmj", output_gradient_heads, value_row_block, preferred_element_type=jnp.float32
    )
    score_gradient = (probabilities * (probability_gradient - out_dot)).astype(jnp.bfloat16)
    query_gradient_heads = (
        jnp.einsum(
            "jym,jmo->jyo", score_gradient, key_row_block, preferred_element_type=jnp.float32
        )
        * logit_scale
    ).astype(jnp.bfloat16)
    key_gradient = (
        jnp.einsum(
            "uwj,uwn->ujn", score_gradient, query_per_head, preferred_element_type=jnp.float32
        )
        * logit_scale
    )
    value_gradient = jnp.einsum(
        "uwj,uwn->ujn", attention_weight, output_gradient_heads, preferred_element_type=jnp.float32
    )
    return (
        attended_per_head,
        query_gradient_heads,
        key_gradient,
        value_gradient,
        log_total[..., 0],
        out_dot[..., 0],
    )


def legacy_body(queries, key_tokens, value_tokens, grad_out):
    row_width = queries.shape[1]
    tok_count = queries.shape[0]
    blocks_dev = tok_count // BLK
    rim = (WINDOW + blocks_dev - 1) // blocks_dev
    devices = lax.axis_size("seq")
    near_list, far_list = offset_lists(devices * blocks_dev)
    offsets = near_list + far_list
    near_count = len(near_list)
    logit_scale = 1.0 / math.sqrt(HD)
    span_blocks = (rim + 1) * blocks_dev
    lead = rim * blocks_dev
    earlier_keys = []
    earlier_values = []
    for back in range(rim, 0, -1):
        got_keys, got_values = passed_along((key_tokens, value_tokens), "seq", back)
        earlier_keys.append(got_keys)
        earlier_values.append(got_values)
    span_keys = to_blocks(jnp.concatenate(earlier_keys + [key_tokens], axis=0), span_blocks)
    span_values = to_blocks(jnp.concatenate(earlier_values + [value_tokens], axis=0), span_blocks)
    far_keys = []
    far_values = []
    for stride in far_list:
        got_keys, got_values = passed_along((key_tokens, value_tokens), "seq", stride // blocks_dev)
        far_keys.append(to_blocks(got_keys, blocks_dev))
        far_values.append(to_blocks(got_values, blocks_dev))
    position = lax.axis_index("seq")
    allowed = allowed_mask(position * blocks_dev, blocks_dev, offsets)
    query_blocks = to_blocks(queries, blocks_dev)
    grad_blocks = to_blocks(grad_out, blocks_dev)
    attended_heads = []
    grad_query_heads = []
    near_key_heads = []
    near_value_heads = []
    total_heads = []
    dot_heads = []
    far_key_parts = [[] for stride in far_list]
    far_value_parts = [[] for stride in far_list]
    for head_index in range(HEADS):
        col_start = head_index * HD
        key_slabs = jnp.stack(
            [
                head_cols(span_keys[lead - offset : lead + blocks_dev - offset], col_start)
                for offset in near_list
            ]
            + [head_cols(item, col_start) for item in far_keys],
            axis=1,
        )
        value_slabs = jnp.stack(
            [
                head_cols(span_values[lead - offset : lead + blocks_dev - offset], col_start)
                for offset in near_list
            ]
            + [head_cols(item, col_start) for item in far_values],
            axis=1,
        )
        (
            attended_per_head,
            query_gradient_heads,
            key_gradient,
            value_gradient,
            log_total,
            out_dot,
        ) = head_pass(
            head_cols(query_blocks, col_start),
            head_cols(grad_blocks, col_start),
            key_slabs,
            value_slabs,
            allowed,
            logit_scale,
        )
        key_gradient = key_gradient.reshape(blocks_dev, -1, BLK, HD)
        value_gradient = value_gradient.reshape(blocks_dev, -1, BLK, HD)
        near_key_heads.append(place_slabs(key_gradient, near_list, lead, span_blocks))
        near_value_heads.append(place_slabs(value_gradient, near_list, lead, span_blocks))
        for level_index in range(len(far_list)):
            far_key_parts[level_index].append(
                key_gradient[:, near_count + level_index].astype(jnp.bfloat16)
            )
            far_value_parts[level_index].append(
                value_gradient[:, near_count + level_index].astype(jnp.bfloat16)
            )
        attended_heads.append(attended_per_head)
        grad_query_heads.append(query_gradient_heads)
        total_heads.append(log_total)
        dot_heads.append(out_dot)
    attended = jnp.concatenate(attended_heads, axis=-1).reshape(tok_count, row_width)
    grad_queries = jnp.concatenate(grad_query_heads, axis=-1).reshape(tok_count, row_width)
    near_keys = jnp.concatenate(near_key_heads, axis=-1).reshape((rim + 1) * tok_count, row_width)
    near_values = jnp.concatenate(near_value_heads, axis=-1).reshape(
        (rim + 1) * tok_count, row_width
    )
    total_keys = near_keys[lead * BLK :].astype(jnp.bfloat16).astype(jnp.float32)
    total_values = near_values[lead * BLK :].astype(jnp.bfloat16).astype(jnp.float32)
    for back in range(1, rim + 1):
        piece_start = (rim - back) * tok_count
        part_keys = near_keys[piece_start : piece_start + tok_count].astype(jnp.bfloat16)
        part_values = near_values[piece_start : piece_start + tok_count].astype(jnp.bfloat16)
        back_keys, back_values = passed_along((part_keys, part_values), "seq", -back)
        total_keys = total_keys + back_keys.astype(jnp.float32)
        total_values = total_values + back_values.astype(jnp.float32)
    for level_index, stride in enumerate(far_list):
        part_keys = jnp.concatenate(far_key_parts[level_index], axis=-1).reshape(
            tok_count, row_width
        )
        part_values = jnp.concatenate(far_value_parts[level_index], axis=-1).reshape(
            tok_count, row_width
        )
        got_keys, got_values = passed_along(
            (part_keys, part_values), "seq", -(stride // blocks_dev)
        )
        total_keys = total_keys + got_keys.astype(jnp.float32)
        total_values = total_values + got_values.astype(jnp.float32)
    return (
        attended,
        grad_queries,
        total_keys.astype(jnp.bfloat16),
        total_values.astype(jnp.bfloat16),
    )


def swap_pairs(count):
    return [(source, source ^ 1) for source in range(count) if source ^ 1 < count]


def relay_ok(count, blocks_dev, rim, far_shifts):
    return count % 2 == 0 and blocks_dev == 2 and rim == 2 and (not far_shifts or far_shifts[0] == 4)


def plan(tok_count, devices):
    blocks_dev = tok_count // BLK
    rim = (WINDOW + blocks_dev - 1) // blocks_dev
    near_list, far_list = offset_lists(devices * blocks_dev)
    far_shifts = [stride // blocks_dev for stride in far_list]
    return blocks_dev, rim, near_list, far_list, far_shifts


def row_pass(query_per_head, output_gradient_heads, key_slabs, value_slabs, allowed, logit_scale):
    block_count = key_slabs.shape[0]
    key_row_block = key_slabs.reshape(block_count, -1, HD)
    value_row_block = value_slabs.reshape(block_count, -1, HD)
    score_matrix = (
        jnp.einsum(
            "nmv,njv->nmj", query_per_head, key_row_block, preferred_element_type=jnp.float32
        )
        * logit_scale
    )
    score_matrix = jnp.where(allowed, score_matrix, NEG)
    row_max = jnp.max(score_matrix, axis=-1, keepdims=True)
    log_total = row_max + jnp.log(jnp.sum(jnp.exp(score_matrix - row_max), axis=-1, keepdims=True))
    probabilities = jnp.exp(score_matrix - log_total)
    attention_weight = probabilities.astype(jnp.bfloat16)
    attended_per_head = jnp.einsum(
        "jym,jmo->jyo", attention_weight, value_row_block, preferred_element_type=jnp.float32
    ).astype(jnp.bfloat16)
    out_dot = jnp.sum(
        output_gradient_heads.astype(jnp.float32) * attended_per_head.astype(jnp.float32),
        axis=-1,
        keepdims=True,
    )
    probability_gradient = jnp.einsum(
        "nmv,njv->nmj", output_gradient_heads, value_row_block, preferred_element_type=jnp.float32
    )
    score_gradient = (probabilities * (probability_gradient - out_dot)).astype(jnp.bfloat16)
    query_gradient_heads = (
        jnp.einsum(
            "jym,jmo->jyo", score_gradient, key_row_block, preferred_element_type=jnp.float32
        )
        * logit_scale
    ).astype(jnp.bfloat16)
    return attended_per_head, query_gradient_heads, log_total[..., 0], out_dot[..., 0]


def key_pass(key_per_head, value_per_head, query_slabs, grad_slabs, total_slabs, dot_slabs, allowed, logit_scale):
    block_count = query_slabs.shape[0]
    query_rows = query_slabs.reshape(block_count, -1, HD)
    grad_rows = grad_slabs.reshape(block_count, -1, HD)
    score_matrix = (
        jnp.einsum("nmv,njv->nmj", query_rows, key_per_head, preferred_element_type=jnp.float32)
        * logit_scale
    )
    total_rows = total_slabs.reshape(block_count, -1, 1)
    dot_rows = dot_slabs.reshape(block_count, -1, 1)
    probabilities = jnp.where(allowed, jnp.exp(score_matrix - total_rows), 0.0)
    probability_gradient = jnp.einsum(
        "nmv,njv->nmj", grad_rows, value_per_head, preferred_element_type=jnp.float32
    )
    score_gradient = (probabilities * (probability_gradient - dot_rows)).astype(jnp.bfloat16)
    attention_weight = probabilities.astype(jnp.bfloat16)
    key_gradient = (
        jnp.einsum("nmj,nmv->njv", score_gradient, query_rows, preferred_element_type=jnp.float32)
        * logit_scale
    )
    value_gradient = jnp.einsum(
        "nmj,nmv->njv", attention_weight, grad_rows, preferred_element_type=jnp.float32
    )
    return key_gradient, value_gradient


def key_allowed(first_block, blocks_dev, offsets, block_total):
    block_ids = first_block + jnp.arange(blocks_dev, dtype=jnp.int32)
    offset_arr = jnp.array(offsets, dtype=jnp.int32)
    query_live = block_ids[:, None] + offset_arr[None, :] < block_total
    row_ids = jnp.arange(BLK, dtype=jnp.int32)
    causal = row_ids[:, None] >= row_ids[None, :]
    later_slab = offset_arr > 0
    slab_causal = jnp.logical_or(later_slab[:, None, None], causal[None, :, :])
    allowed = jnp.logical_and(query_live[:, :, None, None], slab_causal[None, :, :, :])
    return allowed.reshape(blocks_dev, len(offsets) * BLK, BLK)


TRANS_B = (((1,), (1,)), ((), ()))


def row_kernel(near_count, far_list, heads, phase, *refs):
    far_count = len(far_list)
    position_ref, query_ref, grad_ref, span_ref = refs[:4]
    far_refs = refs[4 : 4 + far_count]
    if phase == "stats":
        attended_ref, stats_ref = refs[4 + far_count :]
    else:
        stats_in_ref, grad_query_ref = refs[4 + far_count :]
    width = heads * HD
    near_rows = near_count * BLK
    scale = 1.0 / math.sqrt(HD)
    first = 2 * position_ref[0]
    near_row_ids = lax.broadcasted_iota(jnp.int32, (BLK, near_rows), 0)
    near_col_ids = lax.broadcasted_iota(jnp.int32, (BLK, near_rows), 1)
    near_offset = (near_count - 1) - near_col_ids // BLK
    near_causal = jnp.logical_or(near_offset > 0, near_row_ids >= near_col_ids % BLK)
    lane_ids = lax.broadcasted_iota(jnp.int32, (BLK, 2 * heads), 1)
    for block in range(2):
        rows = pl.ds(block * BLK, BLK)
        near_span = pl.ds(block * BLK, near_rows)
        near_mask = jnp.logical_and(near_causal, first + block - near_offset >= 0)
        far_live = [first + block - offset >= 0 for offset in far_list]
        masks = [near_mask] + far_live
        if phase == "stats":
            stats_tile = jnp.zeros((BLK, 2 * heads), jnp.float32)
        else:
            stats_tile = stats_in_ref[rows, :]
        for head in range(heads):
            cols = pl.ds(head * HD, HD)
            value_cols = pl.ds(width + head * HD, HD)
            query = query_ref[rows, cols]
            grad = grad_ref[rows, cols]
            keys = [span_ref[near_span, cols]] + [item[rows, cols] for item in far_refs]
            values = [span_ref[near_span, value_cols]] + [item[rows, value_cols] for item in far_refs]
            scores = [
                lax.dot_general(query, key, TRANS_B, preferred_element_type=jnp.float32) * scale
                for key in keys
            ]
            if phase == "grad":
                log_total = jnp.sum(jnp.where(lane_ids == head, stats_tile, 0.0), axis=-1, keepdims=True)
                out_dot = jnp.sum(
                    jnp.where(lane_ids == heads + head, stats_tile, 0.0), axis=-1, keepdims=True
                )
                probs = [
                    jnp.where(mask, jnp.exp(score - log_total), 0.0)
                    for score, mask in zip(scores, masks)
                ]
                grad_query = jnp.zeros((BLK, HD), jnp.float32)
                for prob, key, value in zip(probs, keys, values):
                    prob_grad = lax.dot_general(
                        grad, value, TRANS_B, preferred_element_type=jnp.float32
                    )
                    score_grad = (prob * (prob_grad - out_dot)).astype(jnp.bfloat16)
                    grad_query = grad_query + jnp.dot(
                        score_grad, key, preferred_element_type=jnp.float32
                    )
                grad_query_ref[rows, cols] = (grad_query * scale).astype(jnp.bfloat16)
                continue
            scores = [jnp.where(mask, score, NEG) for score, mask in zip(scores, masks)]
            row_max = scores[0].max(axis=-1, keepdims=True)
            for score in scores[1:]:
                row_max = jnp.maximum(row_max, score.max(axis=-1, keepdims=True))
            shifted = [jnp.exp(score - row_max) for score in scores]
            row_sum = shifted[0].sum(axis=-1, keepdims=True)
            for item in shifted[1:]:
                row_sum = row_sum + item.sum(axis=-1, keepdims=True)
            log_total = row_max + jnp.log(row_sum)
            inverse = 1.0 / row_sum
            attended = jnp.zeros((BLK, HD), jnp.float32)
            for item, value in zip(shifted, values):
                attended = attended + jnp.dot(
                    (item * inverse).astype(jnp.bfloat16), value, preferred_element_type=jnp.float32
                )
            attended = attended.astype(jnp.bfloat16)
            attended_ref[rows, cols] = attended
            out_dot = jnp.sum(
                grad.astype(jnp.float32) * attended.astype(jnp.float32), axis=-1, keepdims=True
            )
            stats_tile = stats_tile + jnp.where(lane_ids == head, log_total, 0.0)
            stats_tile = stats_tile + jnp.where(lane_ids == heads + head, out_dot, 0.0)
        if phase == "stats":
            stats_ref[rows, :] = stats_tile


def estimate(tok_count, row_width, slab_rows, matmuls, exps):
    flops = 2 * tok_count * slab_rows * HD * matmuls * (row_width // HD)
    return pl.CostEstimate(
        flops=flops,
        transcendentals=tok_count * slab_rows * exps * (row_width // HD),
        bytes_accessed=8 * tok_count * row_width * 4,
    )


def key_kernel(near_count, far_list, heads, block_total, *refs):
    far_count = len(far_list)
    position_ref, own_ref, span_ref, stats_span_ref = refs[:4]
    far_rows = refs[4 : 4 + far_count]
    far_stats = refs[4 + far_count : 4 + 2 * far_count]
    grad_key_ref, grad_value_ref = refs[4 + 2 * far_count :]
    width = heads * HD
    near_rows = near_count * BLK
    scale = 1.0 / math.sqrt(HD)
    first = 2 * position_ref[0]
    near_row_ids = lax.broadcasted_iota(jnp.int32, (near_rows, BLK), 0)
    near_col_ids = lax.broadcasted_iota(jnp.int32, (near_rows, BLK), 1)
    near_offset = near_row_ids // BLK
    near_causal = jnp.logical_or(near_offset > 0, near_row_ids % BLK >= near_col_ids)
    near_lanes = lax.broadcasted_iota(jnp.int32, (near_rows, 2 * heads), 1)
    far_lanes = lax.broadcasted_iota(jnp.int32, (BLK, 2 * heads), 1)
    for block in range(2):
        rows = pl.ds(block * BLK, BLK)
        near_span = pl.ds(block * BLK, near_rows)
        near_mask = jnp.logical_and(near_causal, first + block + near_offset < block_total)
        far_live = [first + block + offset < block_total for offset in far_list]
        masks = [near_mask] + far_live
        stat_tiles = [stats_span_ref[near_span, :]] + [item[rows, :] for item in far_stats]
        lanes = [near_lanes] + [far_lanes] * far_count
        for head in range(heads):
            cols = pl.ds(head * HD, HD)
            value_cols = pl.ds(width + head * HD, HD)
            key = own_ref[rows, cols]
            value = own_ref[rows, value_cols]
            queries = [span_ref[near_span, cols]] + [item[rows, cols] for item in far_rows]
            grads = [span_ref[near_span, value_cols]] + [item[rows, value_cols] for item in far_rows]
            grad_key = jnp.zeros((BLK, HD), jnp.float32)
            grad_value = jnp.zeros((BLK, HD), jnp.float32)
            for query, grad, tile, lane, mask in zip(queries, grads, stat_tiles, lanes, masks):
                log_total = jnp.sum(jnp.where(lane == head, tile, 0.0), axis=-1, keepdims=True)
                out_dot = jnp.sum(jnp.where(lane == heads + head, tile, 0.0), axis=-1, keepdims=True)
                score = lax.dot_general(query, key, TRANS_B, preferred_element_type=jnp.float32)
                prob = jnp.where(mask, jnp.exp(score * scale - log_total), 0.0)
                prob_grad = lax.dot_general(grad, value, TRANS_B, preferred_element_type=jnp.float32)
                score_grad = prob * (prob_grad - out_dot)
                grad_value = grad_value + jnp.dot(
                    prob.T.astype(jnp.bfloat16), grad, preferred_element_type=jnp.float32
                )
                grad_key = grad_key + jnp.dot(
                    score_grad.T.astype(jnp.bfloat16), query, preferred_element_type=jnp.float32
                )
            grad_key_ref[rows, cols] = (grad_key * scale).astype(jnp.bfloat16)
            grad_value_ref[rows, cols] = grad_value.astype(jnp.bfloat16)


def smem_spec():
    return pl.BlockSpec(memory_space=pltpu.SMEM)


def vmem_spec():
    return pl.BlockSpec(memory_space=pltpu.VMEM)


def body(queries, key_tokens, value_tokens, grad_out):
    row_width = queries.shape[1]
    tok_count = queries.shape[0]
    devices = lax.axis_size("seq")
    blocks_dev, rim, near_list, far_list, far_shifts = plan(tok_count, devices)
    if not relay_ok(devices, blocks_dev, rim, far_shifts):
        return legacy_body(queries, key_tokens, value_tokens, grad_out)
    heads = row_width // HD
    offsets = near_list + far_list
    logit_scale = 1.0 / math.sqrt(HD)
    span_blocks = (rim + 1) * blocks_dev
    lead = rim * blocks_dev
    position = lax.axis_index("seq")
    odd = (position % 2) == 1
    pairs = swap_pairs(devices)
    keys_values = jnp.concatenate([key_tokens, value_tokens], axis=1)
    queries_grads = jnp.concatenate([queries, grad_out], axis=1)
    back2 = passed_along(keys_values, "seq", 2)
    ahead2 = passed_along(queries_grads, "seq", -2)
    swap_one = lax.ppermute(jnp.where(odd, queries_grads, keys_values), "seq", pairs)
    back4 = passed_along(back2, "seq", 2)
    ahead4 = passed_along(ahead2, "seq", -2)
    swap_two = lax.ppermute(jnp.where(odd, back2, ahead2), "seq", pairs)
    back1 = jnp.where(odd, swap_one, swap_two)
    ahead1 = jnp.where(odd, swap_two, swap_one)
    far_back = [back4] + [passed_along(keys_values, "seq", shift) for shift in far_shifts[1:]]
    far_ahead = [ahead4] + [passed_along(queries_grads, "seq", -shift) for shift in far_shifts[1:]]
    far_back = far_back[: len(far_shifts)]
    far_ahead = far_ahead[: len(far_shifts)]

    position_arr = jnp.reshape(position, (1,)).astype(jnp.int32)
    far_offsets = list(far_list)
    row_span = jnp.concatenate([back2, back1, keys_values], axis=0)
    slab_rows = (len(near_list) + len(far_list)) * BLK
    row_inputs = (position_arr, queries, grad_out, row_span, *far_back)
    attended, stats = pl.pallas_call(
        functools.partial(row_kernel, len(near_list), far_offsets, heads, "stats"),
        out_shape=(
            jax.ShapeDtypeStruct((tok_count, row_width), jnp.bfloat16),
            jax.ShapeDtypeStruct((tok_count, 2 * heads), jnp.float32),
        ),
        in_specs=[smem_spec()] + [vmem_spec()] * (3 + len(far_back)),
        out_specs=(vmem_spec(), vmem_spec()),
        cost_estimate=estimate(tok_count, row_width, slab_rows, 2, 1),
        name="rows_stats",
    )(*row_inputs)
    stats_one = passed_along(stats, "seq", -1)
    stats_two = passed_along(stats, "seq", -2)
    far_stats = [passed_along(stats, "seq", -shift) for shift in far_shifts]
    grad_queries = pl.pallas_call(
        functools.partial(row_kernel, len(near_list), far_offsets, heads, "grad"),
        out_shape=jax.ShapeDtypeStruct((tok_count, row_width), jnp.bfloat16),
        in_specs=[smem_spec()] + [vmem_spec()] * (4 + len(far_back)),
        out_specs=vmem_spec(),
        cost_estimate=estimate(tok_count, row_width, slab_rows, 3, 1),
        name="rows_grad",
    )(*row_inputs, stats)
    grad_keys, grad_values = pl.pallas_call(
        functools.partial(key_kernel, len(near_list), far_offsets, heads, devices * blocks_dev),
        out_shape=(
            jax.ShapeDtypeStruct((tok_count, row_width), jnp.bfloat16),
            jax.ShapeDtypeStruct((tok_count, row_width), jnp.bfloat16),
        ),
        in_specs=[smem_spec()] + [vmem_spec()] * (3 + 2 * len(far_ahead)),
        out_specs=(vmem_spec(), vmem_spec()),
        cost_estimate=estimate(tok_count, row_width, slab_rows, 4, 1),
        name="keys_pass",
    )(
        position_arr,
        keys_values,
        jnp.concatenate([queries_grads, ahead1, ahead2], axis=0),
        jnp.concatenate([stats, stats_one, stats_two], axis=0),
        *far_ahead,
        *far_stats,
    )
    return attended, grad_queries, grad_keys, grad_values


def solution(mesh):
    placed = (
        P(("rep", "seq"), None),
        P(("rep", "seq"), None),
        P(("rep", "seq"), None),
        P(("rep", "seq"), None),
    )
    return jax.shard_map(
        body,
        mesh=mesh,
        in_specs=placed,
        out_specs=(
            P(("rep", "seq"), None),
            P(("rep", "seq"), None),
            P(("rep", "seq"), None),
            P(("rep", "seq"), None),
        ),
        check_vma=False,
    )
```

```python
import functools
import math

import jax
import jax.numpy as jnp
from jax import lax
from jax.experimental import pallas as pl
from jax.experimental.pallas import tpu as pltpu
from jax.sharding import PartitionSpec as P

HEADS = 4
HD = 128
BLK = 128
WINDOW = 4


NEG = -1e30
CHUNKS = 2


def passed_along(value, axis, steps):
    count = lax.axis_size(axis)
    first, last = (max(0, -steps), min(count, count - steps))
    return lax.ppermute(value, axis, [(source, source + steps) for source in range(first, last)])


def offset_lists(block_total):
    near_list = list(range(WINDOW + 1))
    far_list = []
    stride = 1
    while stride < block_total:
        if stride > WINDOW:
            far_list.append(stride)
        stride = stride * 2
    return (near_list, far_list)


def allowed_mask(first_block, blocks_dev, offsets):
    block_ids = first_block + jnp.arange(blocks_dev, dtype=jnp.int32)
    offset_arr = jnp.array(offsets, dtype=jnp.int32)
    block_live = block_ids[:, None] - offset_arr[None, :] >= 0
    row_ids = jnp.arange(BLK, dtype=jnp.int32)
    causal = row_ids[:, None] >= row_ids[None, :]
    later_slab = offset_arr > 0
    slab_causal = jnp.logical_or(later_slab[None, :, None], causal[:, None, :])
    allowed = jnp.logical_and(block_live[:, None, :, None], slab_causal[None, :, :, :])
    return allowed.reshape(blocks_dev, BLK, len(offsets) * BLK)


def head_cols(array_in, col_start):
    return array_in[..., col_start : col_start + HD]


def to_blocks(array_in, block_count):
    return array_in.reshape(block_count, BLK, array_in.shape[-1])


def place_slabs(gradient, near_list, lead, span_blocks):
    blocks_dev = gradient.shape[0]
    placed = []
    for slot_index, offset in enumerate(near_list):
        before = lead - offset
        after = span_blocks - before - blocks_dev
        placed.append(jnp.pad(gradient[:, slot_index], ((before, after), (0, 0), (0, 0))))
    total = placed[0]
    for item in placed[1:]:
        total = total + item
    return total


def head_pass(query_per_head, output_gradient_heads, key_slabs, value_slabs, allowed, logit_scale):
    block_count = key_slabs.shape[0]
    key_row_block = key_slabs.reshape(block_count, -1, HD)
    value_row_block = value_slabs.reshape(block_count, -1, HD)
    score_matrix = (
        jnp.einsum(
            "nmv,njv->nmj", query_per_head, key_row_block, preferred_element_type=jnp.float32
        )
        * logit_scale
    )
    score_matrix = jnp.where(allowed, score_matrix, NEG)
    row_max = jnp.max(score_matrix, axis=-1, keepdims=True)
    log_total = row_max + jnp.log(jnp.sum(jnp.exp(score_matrix - row_max), axis=-1, keepdims=True))
    probabilities = jnp.exp(score_matrix - log_total)
    attention_weight = probabilities.astype(jnp.bfloat16)
    attended_per_head = jnp.einsum(
        "jym,jmo->jyo", attention_weight, value_row_block, preferred_element_type=jnp.float32
    ).astype(jnp.bfloat16)
    out_dot = jnp.sum(
        output_gradient_heads.astype(jnp.float32) * attended_per_head.astype(jnp.float32),
        axis=-1,
        keepdims=True,
    )
    probability_gradient = jnp.einsum(
        "nmv,njv->nmj", output_gradient_heads, value_row_block, preferred_element_type=jnp.float32
    )
    score_gradient = (probabilities * (probability_gradient - out_dot)).astype(jnp.bfloat16)
    query_gradient_heads = (
        jnp.einsum(
            "jym,jmo->jyo", score_gradient, key_row_block, preferred_element_type=jnp.float32
        )
        * logit_scale
    ).astype(jnp.bfloat16)
    key_gradient = (
        jnp.einsum(
            "uwj,uwn->ujn", score_gradient, query_per_head, preferred_element_type=jnp.float32
        )
        * logit_scale
    )
    value_gradient = jnp.einsum(
        "uwj,uwn->ujn", attention_weight, output_gradient_heads, preferred_element_type=jnp.float32
    )
    return (
        attended_per_head,
        query_gradient_heads,
        key_gradient,
        value_gradient,
        log_total[..., 0],
        out_dot[..., 0],
    )


def legacy_body(queries, key_tokens, value_tokens, grad_out):
    row_width = queries.shape[1]
    tok_count = queries.shape[0]
    blocks_dev = tok_count // BLK
    rim = (WINDOW + blocks_dev - 1) // blocks_dev
    devices = lax.axis_size("seq")
    near_list, far_list = offset_lists(devices * blocks_dev)
    offsets = near_list + far_list
    near_count = len(near_list)
    logit_scale = 1.0 / math.sqrt(HD)
    span_blocks = (rim + 1) * blocks_dev
    lead = rim * blocks_dev
    earlier_keys = []
    earlier_values = []
    for back in range(rim, 0, -1):
        got_keys, got_values = passed_along((key_tokens, value_tokens), "seq", back)
        earlier_keys.append(got_keys)
        earlier_values.append(got_values)
    span_keys = to_blocks(jnp.concatenate(earlier_keys + [key_tokens], axis=0), span_blocks)
    span_values = to_blocks(jnp.concatenate(earlier_values + [value_tokens], axis=0), span_blocks)
    far_keys = []
    far_values = []
    for stride in far_list:
        got_keys, got_values = passed_along((key_tokens, value_tokens), "seq", stride // blocks_dev)
        far_keys.append(to_blocks(got_keys, blocks_dev))
        far_values.append(to_blocks(got_values, blocks_dev))
    position = lax.axis_index("seq")
    allowed = allowed_mask(position * blocks_dev, blocks_dev, offsets)
    query_blocks = to_blocks(queries, blocks_dev)
    grad_blocks = to_blocks(grad_out, blocks_dev)
    attended_heads = []
    grad_query_heads = []
    near_key_heads = []
    near_value_heads = []
    total_heads = []
    dot_heads = []
    far_key_parts = [[] for stride in far_list]
    far_value_parts = [[] for stride in far_list]
    for head_index in range(HEADS):
        col_start = head_index * HD
        key_slabs = jnp.stack(
            [
                head_cols(span_keys[lead - offset : lead + blocks_dev - offset], col_start)
                for offset in near_list
            ]
            + [head_cols(item, col_start) for item in far_keys],
            axis=1,
        )
        value_slabs = jnp.stack(
            [
                head_cols(span_values[lead - offset : lead + blocks_dev - offset], col_start)
                for offset in near_list
            ]
            + [head_cols(item, col_start) for item in far_values],
            axis=1,
        )
        (
            attended_per_head,
            query_gradient_heads,
            key_gradient,
            value_gradient,
            log_total,
            out_dot,
        ) = head_pass(
            head_cols(query_blocks, col_start),
            head_cols(grad_blocks, col_start),
            key_slabs,
            value_slabs,
            allowed,
            logit_scale,
        )
        key_gradient = key_gradient.reshape(blocks_dev, -1, BLK, HD)
        value_gradient = value_gradient.reshape(blocks_dev, -1, BLK, HD)
        near_key_heads.append(place_slabs(key_gradient, near_list, lead, span_blocks))
        near_value_heads.append(place_slabs(value_gradient, near_list, lead, span_blocks))
        for level_index in range(len(far_list)):
            far_key_parts[level_index].append(
                key_gradient[:, near_count + level_index].astype(jnp.bfloat16)
            )
            far_value_parts[level_index].append(
                value_gradient[:, near_count + level_index].astype(jnp.bfloat16)
            )
        attended_heads.append(attended_per_head)
        grad_query_heads.append(query_gradient_heads)
        total_heads.append(log_total)
        dot_heads.append(out_dot)
    attended = jnp.concatenate(attended_heads, axis=-1).reshape(tok_count, row_width)
    grad_queries = jnp.concatenate(grad_query_heads, axis=-1).reshape(tok_count, row_width)
    near_keys = jnp.concatenate(near_key_heads, axis=-1).reshape((rim + 1) * tok_count, row_width)
    near_values = jnp.concatenate(near_value_heads, axis=-1).reshape(
        (rim + 1) * tok_count, row_width
    )
    total_keys = near_keys[lead * BLK :].astype(jnp.bfloat16).astype(jnp.float32)
    total_values = near_values[lead * BLK :].astype(jnp.bfloat16).astype(jnp.float32)
    for back in range(1, rim + 1):
        piece_start = (rim - back) * tok_count
        part_keys = near_keys[piece_start : piece_start + tok_count].astype(jnp.bfloat16)
        part_values = near_values[piece_start : piece_start + tok_count].astype(jnp.bfloat16)
        back_keys, back_values = passed_along((part_keys, part_values), "seq", -back)
        total_keys = total_keys + back_keys.astype(jnp.float32)
        total_values = total_values + back_values.astype(jnp.float32)
    for level_index, stride in enumerate(far_list):
        part_keys = jnp.concatenate(far_key_parts[level_index], axis=-1).reshape(
            tok_count, row_width
        )
        part_values = jnp.concatenate(far_value_parts[level_index], axis=-1).reshape(
            tok_count, row_width
        )
        got_keys, got_values = passed_along(
            (part_keys, part_values), "seq", -(stride // blocks_dev)
        )
        total_keys = total_keys + got_keys.astype(jnp.float32)
        total_values = total_values + got_values.astype(jnp.float32)
    return (
        attended,
        grad_queries,
        total_keys.astype(jnp.bfloat16),
        total_values.astype(jnp.bfloat16),
    )


def swap_pairs(count):
    return [(source, source ^ 1) for source in range(count) if source ^ 1 < count]


def relay_ok(count, blocks_dev, rim, far_shifts):
    return count % 2 == 0 and blocks_dev == 2 and rim == 2 and (not far_shifts or far_shifts[0] == 4)


def plan(tok_count, devices):
    blocks_dev = tok_count // BLK
    rim = (WINDOW + blocks_dev - 1) // blocks_dev
    near_list, far_list = offset_lists(devices * blocks_dev)
    far_shifts = [stride // blocks_dev for stride in far_list]
    return blocks_dev, rim, near_list, far_list, far_shifts


def row_pass(query_per_head, output_gradient_heads, key_slabs, value_slabs, allowed, logit_scale):
    block_count = key_slabs.shape[0]
    key_row_block = key_slabs.reshape(block_count, -1, HD)
    value_row_block = value_slabs.reshape(block_count, -1, HD)
    score_matrix = (
        jnp.einsum(
            "nmv,njv->nmj", query_per_head, key_row_block, preferred_element_type=jnp.float32
        )
        * logit_scale
    )
    score_matrix = jnp.where(allowed, score_matrix, NEG)
    row_max = jnp.max(score_matrix, axis=-1, keepdims=True)
    log_total = row_max + jnp.log(jnp.sum(jnp.exp(score_matrix - row_max), axis=-1, keepdims=True))
    probabilities = jnp.exp(score_matrix - log_total)
    attention_weight = probabilities.astype(jnp.bfloat16)
    attended_per_head = jnp.einsum(
        "jym,jmo->jyo", attention_weight, value_row_block, preferred_element_type=jnp.float32
    ).astype(jnp.bfloat16)
    out_dot = jnp.sum(
        output_gradient_heads.astype(jnp.float32) * attended_per_head.astype(jnp.float32),
        axis=-1,
        keepdims=True,
    )
    probability_gradient = jnp.einsum(
        "nmv,njv->nmj", output_gradient_heads, value_row_block, preferred_element_type=jnp.float32
    )
    score_gradient = (probabilities * (probability_gradient - out_dot)).astype(jnp.bfloat16)
    query_gradient_heads = (
        jnp.einsum(
            "jym,jmo->jyo", score_gradient, key_row_block, preferred_element_type=jnp.float32
        )
        * logit_scale
    ).astype(jnp.bfloat16)
    return attended_per_head, query_gradient_heads, log_total[..., 0], out_dot[..., 0]


def key_pass(key_per_head, value_per_head, query_slabs, grad_slabs, total_slabs, dot_slabs, allowed, logit_scale):
    block_count = query_slabs.shape[0]
    query_rows = query_slabs.reshape(block_count, -1, HD)
    grad_rows = grad_slabs.reshape(block_count, -1, HD)
    score_matrix = (
        jnp.einsum("nmv,njv->nmj", query_rows, key_per_head, preferred_element_type=jnp.float32)
        * logit_scale
    )
    total_rows = total_slabs.reshape(block_count, -1, 1)
    dot_rows = dot_slabs.reshape(block_count, -1, 1)
    probabilities = jnp.where(allowed, jnp.exp(score_matrix - total_rows), 0.0)
    probability_gradient = jnp.einsum(
        "nmv,njv->nmj", grad_rows, value_per_head, preferred_element_type=jnp.float32
    )
    score_gradient = (probabilities * (probability_gradient - dot_rows)).astype(jnp.bfloat16)
    attention_weight = probabilities.astype(jnp.bfloat16)
    key_gradient = (
        jnp.einsum("nmj,nmv->njv", score_gradient, query_rows, preferred_element_type=jnp.float32)
        * logit_scale
    )
    value_gradient = jnp.einsum(
        "nmj,nmv->njv", attention_weight, grad_rows, preferred_element_type=jnp.float32
    )
    return key_gradient, value_gradient


def key_allowed(first_block, blocks_dev, offsets, block_total):
    block_ids = first_block + jnp.arange(blocks_dev, dtype=jnp.int32)
    offset_arr = jnp.array(offsets, dtype=jnp.int32)
    query_live = block_ids[:, None] + offset_arr[None, :] < block_total
    row_ids = jnp.arange(BLK, dtype=jnp.int32)
    causal = row_ids[:, None] >= row_ids[None, :]
    later_slab = offset_arr > 0
    slab_causal = jnp.logical_or(later_slab[:, None, None], causal[None, :, :])
    allowed = jnp.logical_and(query_live[:, :, None, None], slab_causal[None, :, :, :])
    return allowed.reshape(blocks_dev, len(offsets) * BLK, BLK)


TRANS_B = (((1,), (1,)), ((), ()))


def row_kernel(near_count, far_list, heads, phase, *refs):
    far_count = len(far_list)
    position_ref, query_ref, grad_ref, span_ref = refs[:4]
    far_refs = refs[4 : 4 + far_count]
    if phase == "stats":
        attended_ref, stats_ref = refs[4 + far_count :]
    else:
        stats_in_ref, grad_query_ref = refs[4 + far_count :]
    width = heads * HD
    near_rows = near_count * BLK
    scale = 1.0 / math.sqrt(HD)
    first = 2 * position_ref[0]
    near_row_ids = lax.broadcasted_iota(jnp.int32, (BLK, near_rows), 0)
    near_col_ids = lax.broadcasted_iota(jnp.int32, (BLK, near_rows), 1)
    near_offset = (near_count - 1) - near_col_ids // BLK
    near_causal = jnp.logical_or(near_offset > 0, near_row_ids >= near_col_ids % BLK)
    lane_ids = lax.broadcasted_iota(jnp.int32, (BLK, 2 * heads), 1)
    for block in range(2):
        rows = pl.ds(block * BLK, BLK)
        near_span = pl.ds(block * BLK, near_rows)
        near_mask = jnp.logical_and(near_causal, first + block - near_offset >= 0)
        far_live = [first + block - offset >= 0 for offset in far_list]
        masks = [near_mask] + far_live
        if phase == "stats":
            stats_tile = jnp.zeros((BLK, 2 * heads), jnp.float32)
        else:
            stats_tile = stats_in_ref[rows, :]
        for head in range(heads):
            cols = pl.ds(head * HD, HD)
            value_cols = pl.ds(width + head * HD, HD)
            query = query_ref[rows, cols]
            grad = grad_ref[rows, cols]
            keys = [span_ref[near_span, cols]] + [item[rows, cols] for item in far_refs]
            values = [span_ref[near_span, value_cols]] + [item[rows, value_cols] for item in far_refs]
            scores = [
                lax.dot_general(query, key, TRANS_B, preferred_element_type=jnp.float32) * scale
                for key in keys
            ]
            if phase == "grad":
                log_total = jnp.sum(jnp.where(lane_ids == head, stats_tile, 0.0), axis=-1, keepdims=True)
                out_dot = jnp.sum(
                    jnp.where(lane_ids == heads + head, stats_tile, 0.0), axis=-1, keepdims=True
                )
                probs = [
                    jnp.where(mask, jnp.exp(score - log_total), 0.0)
                    for score, mask in zip(scores, masks)
                ]
                grad_query = jnp.zeros((BLK, HD), jnp.float32)
                for prob, key, value in zip(probs, keys, values):
                    prob_grad = lax.dot_general(
                        grad, value, TRANS_B, preferred_element_type=jnp.float32
                    )
                    score_grad = (prob * (prob_grad - out_dot)).astype(jnp.bfloat16)
                    grad_query = grad_query + jnp.dot(
                        score_grad, key, preferred_element_type=jnp.float32
                    )
                grad_query_ref[rows, cols] = (grad_query * scale).astype(jnp.bfloat16)
                continue
            scores = [jnp.where(mask, score, NEG) for score, mask in zip(scores, masks)]
            row_max = scores[0].max(axis=-1, keepdims=True)
            for score in scores[1:]:
                row_max = jnp.maximum(row_max, score.max(axis=-1, keepdims=True))
            shifted = [jnp.exp(score - row_max) for score in scores]
            row_sum = shifted[0].sum(axis=-1, keepdims=True)
            for item in shifted[1:]:
                row_sum = row_sum + item.sum(axis=-1, keepdims=True)
            log_total = row_max + jnp.log(row_sum)
            inverse = 1.0 / row_sum
            attended = jnp.zeros((BLK, HD), jnp.float32)
            for item, value in zip(shifted, values):
                attended = attended + jnp.dot(
                    (item * inverse).astype(jnp.bfloat16), value, preferred_element_type=jnp.float32
                )
            attended = attended.astype(jnp.bfloat16)
            attended_ref[rows, cols] = attended
            out_dot = jnp.sum(
                grad.astype(jnp.float32) * attended.astype(jnp.float32), axis=-1, keepdims=True
            )
            stats_tile = stats_tile + jnp.where(lane_ids == head, log_total, 0.0)
            stats_tile = stats_tile + jnp.where(lane_ids == heads + head, out_dot, 0.0)
        if phase == "stats":
            stats_ref[rows, :] = stats_tile


def estimate(tok_count, row_width, slab_rows, matmuls, exps):
    flops = 2 * tok_count * slab_rows * HD * matmuls * (row_width // HD)
    return pl.CostEstimate(
        flops=flops,
        transcendentals=tok_count * slab_rows * exps * (row_width // HD),
        bytes_accessed=8 * tok_count * row_width * 4,
    )


def key_kernel(near_count, far_list, heads, block_total, part, *refs):
    far_count = len(far_list)
    position_ref, own_ref = refs[:2]
    if part == "near":
        span_ref, stats_span_ref, grad_key_ref, grad_value_ref = refs[2:]
    else:
        far_rows = refs[2 : 2 + far_count]
        far_stats = refs[2 + far_count : 2 + 2 * far_count]
        key_acc_ref, value_acc_ref, grad_key_ref, grad_value_ref = refs[2 + 2 * far_count :]
    width = heads * HD
    near_rows = near_count * BLK
    scale = 1.0 / math.sqrt(HD)
    first = 2 * position_ref[0]
    near_row_ids = lax.broadcasted_iota(jnp.int32, (near_rows, BLK), 0)
    near_col_ids = lax.broadcasted_iota(jnp.int32, (near_rows, BLK), 1)
    near_offset = near_row_ids // BLK
    near_causal = jnp.logical_or(near_offset > 0, near_row_ids % BLK >= near_col_ids)
    near_lanes = lax.broadcasted_iota(jnp.int32, (near_rows, 2 * heads), 1)
    far_lanes = lax.broadcasted_iota(jnp.int32, (BLK, 2 * heads), 1)
    for block in range(2):
        rows = pl.ds(block * BLK, BLK)
        near_span = pl.ds(block * BLK, near_rows)
        if part == "near":
            masks = [jnp.logical_and(near_causal, first + block + near_offset < block_total)]
            stat_tiles = [stats_span_ref[near_span, :]]
            lanes = [near_lanes]
        else:
            masks = [first + block + offset < block_total for offset in far_list]
            stat_tiles = [item[rows, :] for item in far_stats]
            lanes = [far_lanes] * far_count
        for head in range(heads):
            cols = pl.ds(head * HD, HD)
            value_cols = pl.ds(width + head * HD, HD)
            key = own_ref[rows, cols]
            value = own_ref[rows, value_cols]
            if part == "near":
                queries = [span_ref[near_span, cols]]
                grads = [span_ref[near_span, value_cols]]
                grad_key = jnp.zeros((BLK, HD), jnp.float32)
                grad_value = jnp.zeros((BLK, HD), jnp.float32)
            else:
                queries = [item[rows, cols] for item in far_rows]
                grads = [item[rows, value_cols] for item in far_rows]
                grad_key = key_acc_ref[rows, cols]
                grad_value = value_acc_ref[rows, cols]
            for query, grad, tile, lane, mask in zip(queries, grads, stat_tiles, lanes, masks):
                log_total = jnp.sum(jnp.where(lane == head, tile, 0.0), axis=-1, keepdims=True)
                out_dot = jnp.sum(jnp.where(lane == heads + head, tile, 0.0), axis=-1, keepdims=True)
                score = lax.dot_general(query, key, TRANS_B, preferred_element_type=jnp.float32)
                prob = jnp.where(mask, jnp.exp(score * scale - log_total), 0.0)
                prob_grad = lax.dot_general(grad, value, TRANS_B, preferred_element_type=jnp.float32)
                score_grad = prob * (prob_grad - out_dot)
                grad_value = grad_value + jnp.dot(
                    prob.T.astype(jnp.bfloat16), grad, preferred_element_type=jnp.float32
                )
                grad_key = grad_key + jnp.dot(
                    score_grad.T.astype(jnp.bfloat16), query, preferred_element_type=jnp.float32
                )
            if part == "near":
                grad_key_ref[rows, cols] = grad_key
                grad_value_ref[rows, cols] = grad_value
            else:
                grad_key_ref[rows, cols] = (grad_key * scale).astype(jnp.bfloat16)
                grad_value_ref[rows, cols] = grad_value.astype(jnp.bfloat16)


def smem_spec():
    return pl.BlockSpec(memory_space=pltpu.SMEM)


def vmem_spec():
    return pl.BlockSpec(memory_space=pltpu.VMEM)


def body(queries, key_tokens, value_tokens, grad_out):
    row_width = queries.shape[1]
    tok_count = queries.shape[0]
    devices = lax.axis_size("seq")
    blocks_dev, rim, near_list, far_list, far_shifts = plan(tok_count, devices)
    if not relay_ok(devices, blocks_dev, rim, far_shifts):
        return legacy_body(queries, key_tokens, value_tokens, grad_out)
    heads = row_width // HD
    offsets = near_list + far_list
    logit_scale = 1.0 / math.sqrt(HD)
    span_blocks = (rim + 1) * blocks_dev
    lead = rim * blocks_dev
    position = lax.axis_index("seq")
    odd = (position % 2) == 1
    pairs = swap_pairs(devices)
    keys_values = jnp.concatenate([key_tokens, value_tokens], axis=1)
    queries_grads = jnp.concatenate([queries, grad_out], axis=1)
    back2 = passed_along(keys_values, "seq", 2)
    ahead2 = passed_along(queries_grads, "seq", -2)
    swap_one = lax.ppermute(jnp.where(odd, queries_grads, keys_values), "seq", pairs)
    back4 = passed_along(back2, "seq", 2)
    ahead4 = passed_along(ahead2, "seq", -2)
    swap_two = lax.ppermute(jnp.where(odd, back2, ahead2), "seq", pairs)
    back1 = jnp.where(odd, swap_one, swap_two)
    ahead1 = jnp.where(odd, swap_two, swap_one)
    far_back = [back4] + [passed_along(keys_values, "seq", shift) for shift in far_shifts[1:]]
    far_ahead = [ahead4] + [passed_along(queries_grads, "seq", -shift) for shift in far_shifts[1:]]
    far_back = far_back[: len(far_shifts)]
    far_ahead = far_ahead[: len(far_shifts)]

    position_arr = jnp.reshape(position, (1,)).astype(jnp.int32)
    far_offsets = list(far_list)
    row_span = jnp.concatenate([back2, back1, keys_values], axis=0)
    slab_rows = (len(near_list) + len(far_list)) * BLK
    row_inputs = (position_arr, queries, grad_out, row_span, *far_back)
    attended, stats = pl.pallas_call(
        functools.partial(row_kernel, len(near_list), far_offsets, heads, "stats"),
        out_shape=(
            jax.ShapeDtypeStruct((tok_count, row_width), jnp.bfloat16),
            jax.ShapeDtypeStruct((tok_count, 2 * heads), jnp.float32),
        ),
        in_specs=[smem_spec()] + [vmem_spec()] * (3 + len(far_back)),
        out_specs=(vmem_spec(), vmem_spec()),
        cost_estimate=estimate(tok_count, row_width, slab_rows, 2, 1),
        name="rows_stats",
    )(*row_inputs)
    far_stats = [passed_along(stats, "seq", -shift) for shift in far_shifts]
    stats_one = passed_along(stats, "seq", -1)
    stats_two = passed_along(stats, "seq", -2)
    grad_queries = pl.pallas_call(
        functools.partial(row_kernel, len(near_list), far_offsets, heads, "grad"),
        out_shape=jax.ShapeDtypeStruct((tok_count, row_width), jnp.bfloat16),
        in_specs=[smem_spec()] + [vmem_spec()] * (4 + len(far_back)),
        out_specs=vmem_spec(),
        cost_estimate=estimate(tok_count, row_width, slab_rows, 3, 1),
        name="rows_grad",
    )(*row_inputs, stats)
    key_acc, value_acc = pl.pallas_call(
        functools.partial(key_kernel, len(near_list), far_offsets, heads, devices * blocks_dev, "near"),
        out_shape=(
            jax.ShapeDtypeStruct((tok_count, row_width), jnp.float32),
            jax.ShapeDtypeStruct((tok_count, row_width), jnp.float32),
        ),
        in_specs=[smem_spec()] + [vmem_spec()] * 3,
        out_specs=(vmem_spec(), vmem_spec()),
        cost_estimate=estimate(tok_count, row_width, len(near_list) * BLK, 4, 1),
        name="keys_near",
    )(
        position_arr,
        keys_values,
        jnp.concatenate([queries_grads, ahead1, ahead2], axis=0),
        jnp.concatenate([stats, stats_one, stats_two], axis=0),
    )
    grad_keys, grad_values = pl.pallas_call(
        functools.partial(key_kernel, len(near_list), far_offsets, heads, devices * blocks_dev, "far"),
        out_shape=(
            jax.ShapeDtypeStruct((tok_count, row_width), jnp.bfloat16),
            jax.ShapeDtypeStruct((tok_count, row_width), jnp.bfloat16),
        ),
        in_specs=[smem_spec()] + [vmem_spec()] * (3 + 2 * len(far_ahead)),
        out_specs=(vmem_spec(), vmem_spec()),
        cost_estimate=estimate(tok_count, row_width, len(far_list) * BLK, 4, 1),
        name="keys_far",
    )(position_arr, keys_values, *far_ahead, *far_stats, key_acc, value_acc)
    return attended, grad_queries, grad_keys, grad_values


def solution(mesh):
    placed = (
        P(("rep", "seq"), None),
        P(("rep", "seq"), None),
        P(("rep", "seq"), None),
        P(("rep", "seq"), None),
    )
    return jax.shard_map(
        body,
        mesh=mesh,
        in_specs=placed,
        out_specs=(
            P(("rep", "seq"), None),
            P(("rep", "seq"), None),
            P(("rep", "seq"), None),
            P(("rep", "seq"), None),
        ),
        check_vma=False,
    )
```

```python
import functools
import math

import jax
import jax.numpy as jnp
from jax import lax
from jax.experimental import pallas as pl
from jax.experimental.pallas import tpu as pltpu
from jax.sharding import PartitionSpec as P

HEADS = 4
HD = 128
BLK = 128
WINDOW = 4


NEG = -1e30
CHUNKS = 2


def passed_along(value, axis, steps):
    count = lax.axis_size(axis)
    first, last = (max(0, -steps), min(count, count - steps))
    return lax.ppermute(value, axis, [(source, source + steps) for source in range(first, last)])


def offset_lists(block_total):
    near_list = list(range(WINDOW + 1))
    far_list = []
    stride = 1
    while stride < block_total:
        if stride > WINDOW:
            far_list.append(stride)
        stride = stride * 2
    return (near_list, far_list)


def allowed_mask(first_block, blocks_dev, offsets):
    block_ids = first_block + jnp.arange(blocks_dev, dtype=jnp.int32)
    offset_arr = jnp.array(offsets, dtype=jnp.int32)
    block_live = block_ids[:, None] - offset_arr[None, :] >= 0
    row_ids = jnp.arange(BLK, dtype=jnp.int32)
    causal = row_ids[:, None] >= row_ids[None, :]
    later_slab = offset_arr > 0
    slab_causal = jnp.logical_or(later_slab[None, :, None], causal[:, None, :])
    allowed = jnp.logical_and(block_live[:, None, :, None], slab_causal[None, :, :, :])
    return allowed.reshape(blocks_dev, BLK, len(offsets) * BLK)


def head_cols(array_in, col_start):
    return array_in[..., col_start : col_start + HD]


def to_blocks(array_in, block_count):
    return array_in.reshape(block_count, BLK, array_in.shape[-1])


def place_slabs(gradient, near_list, lead, span_blocks):
    blocks_dev = gradient.shape[0]
    placed = []
    for slot_index, offset in enumerate(near_list):
        before = lead - offset
        after = span_blocks - before - blocks_dev
        placed.append(jnp.pad(gradient[:, slot_index], ((before, after), (0, 0), (0, 0))))
    total = placed[0]
    for item in placed[1:]:
        total = total + item
    return total


def head_pass(query_per_head, output_gradient_heads, key_slabs, value_slabs, allowed, logit_scale):
    block_count = key_slabs.shape[0]
    key_row_block = key_slabs.reshape(block_count, -1, HD)
    value_row_block = value_slabs.reshape(block_count, -1, HD)
    score_matrix = (
        jnp.einsum(
            "nmv,njv->nmj", query_per_head, key_row_block, preferred_element_type=jnp.float32
        )
        * logit_scale
    )
    score_matrix = jnp.where(allowed, score_matrix, NEG)
    row_max = jnp.max(score_matrix, axis=-1, keepdims=True)
    log_total = row_max + jnp.log(jnp.sum(jnp.exp(score_matrix - row_max), axis=-1, keepdims=True))
    probabilities = jnp.exp(score_matrix - log_total)
    attention_weight = probabilities.astype(jnp.bfloat16)
    attended_per_head = jnp.einsum(
        "jym,jmo->jyo", attention_weight, value_row_block, preferred_element_type=jnp.float32
    ).astype(jnp.bfloat16)
    out_dot = jnp.sum(
        output_gradient_heads.astype(jnp.float32) * attended_per_head.astype(jnp.float32),
        axis=-1,
        keepdims=True,
    )
    probability_gradient = jnp.einsum(
        "nmv,njv->nmj", output_gradient_heads, value_row_block, preferred_element_type=jnp.float32
    )
    score_gradient = (probabilities * (probability_gradient - out_dot)).astype(jnp.bfloat16)
    query_gradient_heads = (
        jnp.einsum(
            "jym,jmo->jyo", score_gradient, key_row_block, preferred_element_type=jnp.float32
        )
        * logit_scale
    ).astype(jnp.bfloat16)
    key_gradient = (
        jnp.einsum(
            "uwj,uwn->ujn", score_gradient, query_per_head, preferred_element_type=jnp.float32
        )
        * logit_scale
    )
    value_gradient = jnp.einsum(
        "uwj,uwn->ujn", attention_weight, output_gradient_heads, preferred_element_type=jnp.float32
    )
    return (
        attended_per_head,
        query_gradient_heads,
        key_gradient,
        value_gradient,
        log_total[..., 0],
        out_dot[..., 0],
    )


def legacy_body(queries, key_tokens, value_tokens, grad_out):
    row_width = queries.shape[1]
    tok_count = queries.shape[0]
    blocks_dev = tok_count // BLK
    rim = (WINDOW + blocks_dev - 1) // blocks_dev
    devices = lax.axis_size("seq")
    near_list, far_list = offset_lists(devices * blocks_dev)
    offsets = near_list + far_list
    near_count = len(near_list)
    logit_scale = 1.0 / math.sqrt(HD)
    span_blocks = (rim + 1) * blocks_dev
    lead = rim * blocks_dev
    earlier_keys = []
    earlier_values = []
    for back in range(rim, 0, -1):
        got_keys, got_values = passed_along((key_tokens, value_tokens), "seq", back)
        earlier_keys.append(got_keys)
        earlier_values.append(got_values)
    span_keys = to_blocks(jnp.concatenate(earlier_keys + [key_tokens], axis=0), span_blocks)
    span_values = to_blocks(jnp.concatenate(earlier_values + [value_tokens], axis=0), span_blocks)
    far_keys = []
    far_values = []
    for stride in far_list:
        got_keys, got_values = passed_along((key_tokens, value_tokens), "seq", stride // blocks_dev)
        far_keys.append(to_blocks(got_keys, blocks_dev))
        far_values.append(to_blocks(got_values, blocks_dev))
    position = lax.axis_index("seq")
    allowed = allowed_mask(position * blocks_dev, blocks_dev, offsets)
    query_blocks = to_blocks(queries, blocks_dev)
    grad_blocks = to_blocks(grad_out, blocks_dev)
    attended_heads = []
    grad_query_heads = []
    near_key_heads = []
    near_value_heads = []
    total_heads = []
    dot_heads = []
    far_key_parts = [[] for stride in far_list]
    far_value_parts = [[] for stride in far_list]
    for head_index in range(HEADS):
        col_start = head_index * HD
        key_slabs = jnp.stack(
            [
                head_cols(span_keys[lead - offset : lead + blocks_dev - offset], col_start)
                for offset in near_list
            ]
            + [head_cols(item, col_start) for item in far_keys],
            axis=1,
        )
        value_slabs = jnp.stack(
            [
                head_cols(span_values[lead - offset : lead + blocks_dev - offset], col_start)
                for offset in near_list
            ]
            + [head_cols(item, col_start) for item in far_values],
            axis=1,
        )
        (
            attended_per_head,
            query_gradient_heads,
            key_gradient,
            value_gradient,
            log_total,
            out_dot,
        ) = head_pass(
            head_cols(query_blocks, col_start),
            head_cols(grad_blocks, col_start),
            key_slabs,
            value_slabs,
            allowed,
            logit_scale,
        )
        key_gradient = key_gradient.reshape(blocks_dev, -1, BLK, HD)
        value_gradient = value_gradient.reshape(blocks_dev, -1, BLK, HD)
        near_key_heads.append(place_slabs(key_gradient, near_list, lead, span_blocks))
        near_value_heads.append(place_slabs(value_gradient, near_list, lead, span_blocks))
        for level_index in range(len(far_list)):
            far_key_parts[level_index].append(
                key_gradient[:, near_count + level_index].astype(jnp.bfloat16)
            )
            far_value_parts[level_index].append(
                value_gradient[:, near_count + level_index].astype(jnp.bfloat16)
            )
        attended_heads.append(attended_per_head)
        grad_query_heads.append(query_gradient_heads)
        total_heads.append(log_total)
        dot_heads.append(out_dot)
    attended = jnp.concatenate(attended_heads, axis=-1).reshape(tok_count, row_width)
    grad_queries = jnp.concatenate(grad_query_heads, axis=-1).reshape(tok_count, row_width)
    near_keys = jnp.concatenate(near_key_heads, axis=-1).reshape((rim + 1) * tok_count, row_width)
    near_values = jnp.concatenate(near_value_heads, axis=-1).reshape(
        (rim + 1) * tok_count, row_width
    )
    total_keys = near_keys[lead * BLK :].astype(jnp.bfloat16).astype(jnp.float32)
    total_values = near_values[lead * BLK :].astype(jnp.bfloat16).astype(jnp.float32)
    for back in range(1, rim + 1):
        piece_start = (rim - back) * tok_count
        part_keys = near_keys[piece_start : piece_start + tok_count].astype(jnp.bfloat16)
        part_values = near_values[piece_start : piece_start + tok_count].astype(jnp.bfloat16)
        back_keys, back_values = passed_along((part_keys, part_values), "seq", -back)
        total_keys = total_keys + back_keys.astype(jnp.float32)
        total_values = total_values + back_values.astype(jnp.float32)
    for level_index, stride in enumerate(far_list):
        part_keys = jnp.concatenate(far_key_parts[level_index], axis=-1).reshape(
            tok_count, row_width
        )
        part_values = jnp.concatenate(far_value_parts[level_index], axis=-1).reshape(
            tok_count, row_width
        )
        got_keys, got_values = passed_along(
            (part_keys, part_values), "seq", -(stride // blocks_dev)
        )
        total_keys = total_keys + got_keys.astype(jnp.float32)
        total_values = total_values + got_values.astype(jnp.float32)
    return (
        attended,
        grad_queries,
        total_keys.astype(jnp.bfloat16),
        total_values.astype(jnp.bfloat16),
    )


def swap_pairs(count):
    return [(source, source ^ 1) for source in range(count) if source ^ 1 < count]


def relay_ok(count, blocks_dev, rim, far_shifts):
    return count % 2 == 0 and blocks_dev == 2 and rim == 2 and (not far_shifts or far_shifts[0] == 4)


def plan(tok_count, devices):
    blocks_dev = tok_count // BLK
    rim = (WINDOW + blocks_dev - 1) // blocks_dev
    near_list, far_list = offset_lists(devices * blocks_dev)
    far_shifts = [stride // blocks_dev for stride in far_list]
    return blocks_dev, rim, near_list, far_list, far_shifts


def row_pass(query_per_head, output_gradient_heads, key_slabs, value_slabs, allowed, logit_scale):
    block_count = key_slabs.shape[0]
    key_row_block = key_slabs.reshape(block_count, -1, HD)
    value_row_block = value_slabs.reshape(block_count, -1, HD)
    score_matrix = (
        jnp.einsum(
            "nmv,njv->nmj", query_per_head, key_row_block, preferred_element_type=jnp.float32
        )
        * logit_scale
    )
    score_matrix = jnp.where(allowed, score_matrix, NEG)
    row_max = jnp.max(score_matrix, axis=-1, keepdims=True)
    log_total = row_max + jnp.log(jnp.sum(jnp.exp(score_matrix - row_max), axis=-1, keepdims=True))
    probabilities = jnp.exp(score_matrix - log_total)
    attention_weight = probabilities.astype(jnp.bfloat16)
    attended_per_head = jnp.einsum(
        "jym,jmo->jyo", attention_weight, value_row_block, preferred_element_type=jnp.float32
    ).astype(jnp.bfloat16)
    out_dot = jnp.sum(
        output_gradient_heads.astype(jnp.float32) * attended_per_head.astype(jnp.float32),
        axis=-1,
        keepdims=True,
    )
    probability_gradient = jnp.einsum(
        "nmv,njv->nmj", output_gradient_heads, value_row_block, preferred_element_type=jnp.float32
    )
    score_gradient = (probabilities * (probability_gradient - out_dot)).astype(jnp.bfloat16)
    query_gradient_heads = (
        jnp.einsum(
            "jym,jmo->jyo", score_gradient, key_row_block, preferred_element_type=jnp.float32
        )
        * logit_scale
    ).astype(jnp.bfloat16)
    return attended_per_head, query_gradient_heads, log_total[..., 0], out_dot[..., 0]


def key_pass(key_per_head, value_per_head, query_slabs, grad_slabs, total_slabs, dot_slabs, allowed, logit_scale):
    block_count = query_slabs.shape[0]
    query_rows = query_slabs.reshape(block_count, -1, HD)
    grad_rows = grad_slabs.reshape(block_count, -1, HD)
    score_matrix = (
        jnp.einsum("nmv,njv->nmj", query_rows, key_per_head, preferred_element_type=jnp.float32)
        * logit_scale
    )
    total_rows = total_slabs.reshape(block_count, -1, 1)
    dot_rows = dot_slabs.reshape(block_count, -1, 1)
    probabilities = jnp.where(allowed, jnp.exp(score_matrix - total_rows), 0.0)
    probability_gradient = jnp.einsum(
        "nmv,njv->nmj", grad_rows, value_per_head, preferred_element_type=jnp.float32
    )
    score_gradient = (probabilities * (probability_gradient - dot_rows)).astype(jnp.bfloat16)
    attention_weight = probabilities.astype(jnp.bfloat16)
    key_gradient = (
        jnp.einsum("nmj,nmv->njv", score_gradient, query_rows, preferred_element_type=jnp.float32)
        * logit_scale
    )
    value_gradient = jnp.einsum(
        "nmj,nmv->njv", attention_weight, grad_rows, preferred_element_type=jnp.float32
    )
    return key_gradient, value_gradient


def key_allowed(first_block, blocks_dev, offsets, block_total):
    block_ids = first_block + jnp.arange(blocks_dev, dtype=jnp.int32)
    offset_arr = jnp.array(offsets, dtype=jnp.int32)
    query_live = block_ids[:, None] + offset_arr[None, :] < block_total
    row_ids = jnp.arange(BLK, dtype=jnp.int32)
    causal = row_ids[:, None] >= row_ids[None, :]
    later_slab = offset_arr > 0
    slab_causal = jnp.logical_or(later_slab[:, None, None], causal[None, :, :])
    allowed = jnp.logical_and(query_live[:, :, None, None], slab_causal[None, :, :, :])
    return allowed.reshape(blocks_dev, len(offsets) * BLK, BLK)


TRANS_B = (((1,), (1,)), ((), ()))


def row_kernel(near_count, far_list, heads, phase, *refs):
    far_count = len(far_list)
    position_ref, query_ref, grad_ref, span_ref = refs[:4]
    far_refs = refs[4 : 4 + far_count]
    if phase == "stats":
        attended_ref, stats_ref, stats_rows_ref = refs[4 + far_count :]
    else:
        stats_in_ref, grad_query_ref = refs[4 + far_count :]
    width = heads * HD
    near_rows = near_count * BLK
    scale = 1.0 / math.sqrt(HD)
    first = 2 * position_ref[0]
    near_row_ids = lax.broadcasted_iota(jnp.int32, (BLK, near_rows), 0)
    near_col_ids = lax.broadcasted_iota(jnp.int32, (BLK, near_rows), 1)
    near_offset = (near_count - 1) - near_col_ids // BLK
    near_causal = jnp.logical_or(near_offset > 0, near_row_ids >= near_col_ids % BLK)
    lane_ids = lax.broadcasted_iota(jnp.int32, (BLK, 2 * heads), 1)
    for block in range(2):
        rows = pl.ds(block * BLK, BLK)
        near_span = pl.ds(block * BLK, near_rows)
        near_mask = jnp.logical_and(near_causal, first + block - near_offset >= 0)
        far_live = [first + block - offset >= 0 for offset in far_list]
        masks = [near_mask] + far_live
        if phase == "stats":
            stats_tile = jnp.zeros((BLK, 2 * heads), jnp.float32)
        else:
            stats_tile = stats_in_ref[rows, :]
        for head in range(heads):
            cols = pl.ds(head * HD, HD)
            value_cols = pl.ds(width + head * HD, HD)
            query = query_ref[rows, cols]
            grad = grad_ref[rows, cols]
            keys = [span_ref[near_span, cols]] + [item[rows, cols] for item in far_refs]
            values = [span_ref[near_span, value_cols]] + [item[rows, value_cols] for item in far_refs]
            scores = [
                lax.dot_general(query, key, TRANS_B, preferred_element_type=jnp.float32) * scale
                for key in keys
            ]
            if phase == "grad":
                log_total = jnp.sum(jnp.where(lane_ids == head, stats_tile, 0.0), axis=-1, keepdims=True)
                out_dot = jnp.sum(
                    jnp.where(lane_ids == heads + head, stats_tile, 0.0), axis=-1, keepdims=True
                )
                probs = [
                    jnp.where(mask, jnp.exp(score - log_total), 0.0)
                    for score, mask in zip(scores, masks)
                ]
                grad_query = jnp.zeros((BLK, HD), jnp.float32)
                for prob, key, value in zip(probs, keys, values):
                    prob_grad = lax.dot_general(
                        grad, value, TRANS_B, preferred_element_type=jnp.float32
                    )
                    score_grad = (prob * (prob_grad - out_dot)).astype(jnp.bfloat16)
                    grad_query = grad_query + jnp.dot(
                        score_grad, key, preferred_element_type=jnp.float32
                    )
                grad_query_ref[rows, cols] = (grad_query * scale).astype(jnp.bfloat16)
                continue
            scores = [jnp.where(mask, score, NEG) for score, mask in zip(scores, masks)]
            row_max = scores[0].max(axis=-1, keepdims=True)
            for score in scores[1:]:
                row_max = jnp.maximum(row_max, score.max(axis=-1, keepdims=True))
            shifted = [jnp.exp(score - row_max) for score in scores]
            row_sum = shifted[0].sum(axis=-1, keepdims=True)
            for item in shifted[1:]:
                row_sum = row_sum + item.sum(axis=-1, keepdims=True)
            log_total = row_max + jnp.log(row_sum)
            inverse = 1.0 / row_sum
            attended = jnp.zeros((BLK, HD), jnp.float32)
            for item, value in zip(shifted, values):
                attended = attended + jnp.dot(
                    (item * inverse).astype(jnp.bfloat16), value, preferred_element_type=jnp.float32
                )
            attended = attended.astype(jnp.bfloat16)
            attended_ref[rows, cols] = attended
            out_dot = jnp.sum(
                grad.astype(jnp.float32) * attended.astype(jnp.float32), axis=-1, keepdims=True
            )
            stats_tile = stats_tile + jnp.where(lane_ids == head, log_total, 0.0)
            stats_tile = stats_tile + jnp.where(lane_ids == heads + head, out_dot, 0.0)
        if phase == "stats":
            stats_ref[rows, :] = stats_tile
            wide_lanes = lax.broadcasted_iota(jnp.int32, (BLK, BLK), 1)
            wide = jnp.zeros((BLK, BLK), jnp.float32)
            for lane in range(2 * heads):
                column = jnp.sum(jnp.where(lane_ids == lane, stats_tile, 0.0), axis=-1, keepdims=True)
                wide = wide + jnp.where(wide_lanes == lane, column, 0.0)
            stats_rows_ref[:, rows] = wide.T[: 2 * heads, :]


def estimate(tok_count, row_width, slab_rows, matmuls, exps):
    flops = 2 * tok_count * slab_rows * HD * matmuls * (row_width // HD)
    return pl.CostEstimate(
        flops=flops,
        transcendentals=tok_count * slab_rows * exps * (row_width // HD),
        bytes_accessed=8 * tok_count * row_width * 4,
    )


def key_kernel(near_count, far_list, heads, block_total, *refs):
    far_count = len(far_list)
    position_ref, own_ref, span_ref, stats_span_ref = refs[:4]
    far_rows = refs[4 : 4 + far_count]
    far_stats = refs[4 + far_count : 4 + 2 * far_count]
    grad_key_ref, grad_value_ref = refs[4 + 2 * far_count :]
    width = heads * HD
    near_rows = near_count * BLK
    scale = 1.0 / math.sqrt(HD)
    first = 2 * position_ref[0]
    near_key_ids = lax.broadcasted_iota(jnp.int32, (BLK, near_rows), 0)
    near_query_ids = lax.broadcasted_iota(jnp.int32, (BLK, near_rows), 1)
    near_offset = near_query_ids // BLK
    near_causal = jnp.logical_or(near_offset > 0, near_query_ids % BLK >= near_key_ids)
    for block in range(2):
        rows = pl.ds(block * BLK, BLK)
        near_span = pl.ds(block * BLK, near_rows)
        near_mask = jnp.logical_and(near_causal, first + block + near_offset < block_total)
        far_live = [first + block + offset < block_total for offset in far_list]
        masks = [near_mask] + far_live
        for head in range(heads):
            cols = pl.ds(head * HD, HD)
            value_cols = pl.ds(width + head * HD, HD)
            key = own_ref[rows, cols]
            value = own_ref[rows, value_cols]
            queries = [span_ref[near_span, cols]] + [item[rows, cols] for item in far_rows]
            grads = [span_ref[near_span, value_cols]] + [item[rows, value_cols] for item in far_rows]
            totals = [stats_span_ref[pl.ds(head, 1), near_span]] + [
                item[pl.ds(head, 1), rows] for item in far_stats
            ]
            dots = [stats_span_ref[pl.ds(heads + head, 1), near_span]] + [
                item[pl.ds(heads + head, 1), rows] for item in far_stats
            ]
            grad_key = jnp.zeros((BLK, HD), jnp.float32)
            grad_value = jnp.zeros((BLK, HD), jnp.float32)
            for query, grad, log_total, out_dot, mask in zip(queries, grads, totals, dots, masks):
                score = lax.dot_general(key, query, TRANS_B, preferred_element_type=jnp.float32)
                prob = jnp.where(mask, jnp.exp(score * scale - log_total), 0.0)
                prob_grad = lax.dot_general(value, grad, TRANS_B, preferred_element_type=jnp.float32)
                score_grad = (prob * (prob_grad - out_dot)).astype(jnp.bfloat16)
                grad_value = grad_value + jnp.dot(
                    prob.astype(jnp.bfloat16), grad, preferred_element_type=jnp.float32
                )
                grad_key = grad_key + jnp.dot(score_grad, query, preferred_element_type=jnp.float32)
            grad_key_ref[rows, cols] = (grad_key * scale).astype(jnp.bfloat16)
            grad_value_ref[rows, cols] = grad_value.astype(jnp.bfloat16)


def smem_spec():
    return pl.BlockSpec(memory_space=pltpu.SMEM)


def vmem_spec():
    return pl.BlockSpec(memory_space=pltpu.VMEM)


def body(queries, key_tokens, value_tokens, grad_out):
    row_width = queries.shape[1]
    tok_count = queries.shape[0]
    devices = lax.axis_size("seq")
    blocks_dev, rim, near_list, far_list, far_shifts = plan(tok_count, devices)
    if not relay_ok(devices, blocks_dev, rim, far_shifts):
        return legacy_body(queries, key_tokens, value_tokens, grad_out)
    heads = row_width // HD
    offsets = near_list + far_list
    logit_scale = 1.0 / math.sqrt(HD)
    span_blocks = (rim + 1) * blocks_dev
    lead = rim * blocks_dev
    position = lax.axis_index("seq")
    odd = (position % 2) == 1
    pairs = swap_pairs(devices)
    keys_values = jnp.concatenate([key_tokens, value_tokens], axis=1)
    queries_grads = jnp.concatenate([queries, grad_out], axis=1)
    back2 = passed_along(keys_values, "seq", 2)
    ahead2 = passed_along(queries_grads, "seq", -2)
    swap_one = lax.ppermute(jnp.where(odd, queries_grads, keys_values), "seq", pairs)
    back4 = passed_along(back2, "seq", 2)
    ahead4 = passed_along(ahead2, "seq", -2)
    swap_two = lax.ppermute(jnp.where(odd, back2, ahead2), "seq", pairs)
    back1 = jnp.where(odd, swap_one, swap_two)
    ahead1 = jnp.where(odd, swap_two, swap_one)
    far_back = [back4] + [passed_along(keys_values, "seq", shift) for shift in far_shifts[1:]]
    far_ahead = [ahead4] + [passed_along(queries_grads, "seq", -shift) for shift in far_shifts[1:]]
    far_back = far_back[: len(far_shifts)]
    far_ahead = far_ahead[: len(far_shifts)]

    position_arr = jnp.reshape(position, (1,)).astype(jnp.int32)
    far_offsets = list(far_list)
    row_span = jnp.concatenate([back2, back1, keys_values], axis=0)
    slab_rows = (len(near_list) + len(far_list)) * BLK
    row_inputs = (position_arr, queries, grad_out, row_span, *far_back)
    attended, stats, stats_rows = pl.pallas_call(
        functools.partial(row_kernel, len(near_list), far_offsets, heads, "stats"),
        out_shape=(
            jax.ShapeDtypeStruct((tok_count, row_width), jnp.bfloat16),
            jax.ShapeDtypeStruct((tok_count, 2 * heads), jnp.float32),
            jax.ShapeDtypeStruct((2 * heads, tok_count), jnp.float32),
        ),
        in_specs=[smem_spec()] + [vmem_spec()] * (3 + len(far_back)),
        out_specs=(vmem_spec(), vmem_spec(), vmem_spec()),
        cost_estimate=estimate(tok_count, row_width, slab_rows, 2, 1),
        name="rows_stats",
    )(*row_inputs)
    stats_one = passed_along(stats_rows, "seq", -1)
    stats_two = passed_along(stats_rows, "seq", -2)
    far_stats = [passed_along(stats_rows, "seq", -shift) for shift in far_shifts]
    grad_queries = pl.pallas_call(
        functools.partial(row_kernel, len(near_list), far_offsets, heads, "grad"),
        out_shape=jax.ShapeDtypeStruct((tok_count, row_width), jnp.bfloat16),
        in_specs=[smem_spec()] + [vmem_spec()] * (4 + len(far_back)),
        out_specs=vmem_spec(),
        cost_estimate=estimate(tok_count, row_width, slab_rows, 3, 1),
        name="rows_grad",
    )(*row_inputs, stats)
    grad_keys, grad_values = pl.pallas_call(
        functools.partial(key_kernel, len(near_list), far_offsets, heads, devices * blocks_dev),
        out_shape=(
            jax.ShapeDtypeStruct((tok_count, row_width), jnp.bfloat16),
            jax.ShapeDtypeStruct((tok_count, row_width), jnp.bfloat16),
        ),
        in_specs=[smem_spec()] + [vmem_spec()] * (3 + 2 * len(far_ahead)),
        out_specs=(vmem_spec(), vmem_spec()),
        cost_estimate=estimate(tok_count, row_width, slab_rows, 4, 1),
        name="keys_pass",
    )(
        position_arr,
        keys_values,
        jnp.concatenate([queries_grads, ahead1, ahead2], axis=0),
        jnp.concatenate([stats_rows, stats_one, stats_two], axis=1),
        *far_ahead,
        *far_stats,
    )
    return attended, grad_queries, grad_keys, grad_values


def solution(mesh):
    placed = (
        P(("rep", "seq"), None),
        P(("rep", "seq"), None),
        P(("rep", "seq"), None),
        P(("rep", "seq"), None),
    )
    return jax.shard_map(
        body,
        mesh=mesh,
        in_specs=placed,
        out_specs=(
            P(("rep", "seq"), None),
            P(("rep", "seq"), None),
            P(("rep", "seq"), None),
            P(("rep", "seq"), None),
        ),
        check_vma=False,
    )
```

```python
import functools
import math

import jax
import jax.numpy as jnp
from jax import lax
from jax.experimental import pallas as pl
from jax.experimental.pallas import tpu as pltpu
from jax.sharding import PartitionSpec as P

HEADS = 4
HD = 128
BLK = 128
WINDOW = 4


NEG = -1e30
CHUNKS = 2


def passed_along(value, axis, steps):
    count = lax.axis_size(axis)
    first, last = (max(0, -steps), min(count, count - steps))
    return lax.ppermute(value, axis, [(source, source + steps) for source in range(first, last)])


def offset_lists(block_total):
    near_list = list(range(WINDOW + 1))
    far_list = []
    stride = 1
    while stride < block_total:
        if stride > WINDOW:
            far_list.append(stride)
        stride = stride * 2
    return (near_list, far_list)


def allowed_mask(first_block, blocks_dev, offsets):
    block_ids = first_block + jnp.arange(blocks_dev, dtype=jnp.int32)
    offset_arr = jnp.array(offsets, dtype=jnp.int32)
    block_live = block_ids[:, None] - offset_arr[None, :] >= 0
    row_ids = jnp.arange(BLK, dtype=jnp.int32)
    causal = row_ids[:, None] >= row_ids[None, :]
    later_slab = offset_arr > 0
    slab_causal = jnp.logical_or(later_slab[None, :, None], causal[:, None, :])
    allowed = jnp.logical_and(block_live[:, None, :, None], slab_causal[None, :, :, :])
    return allowed.reshape(blocks_dev, BLK, len(offsets) * BLK)


def head_cols(array_in, col_start):
    return array_in[..., col_start : col_start + HD]


def to_blocks(array_in, block_count):
    return array_in.reshape(block_count, BLK, array_in.shape[-1])


def place_slabs(gradient, near_list, lead, span_blocks):
    blocks_dev = gradient.shape[0]
    placed = []
    for slot_index, offset in enumerate(near_list):
        before = lead - offset
        after = span_blocks - before - blocks_dev
        placed.append(jnp.pad(gradient[:, slot_index], ((before, after), (0, 0), (0, 0))))
    total = placed[0]
    for item in placed[1:]:
        total = total + item
    return total


def head_pass(query_per_head, output_gradient_heads, key_slabs, value_slabs, allowed, logit_scale):
    block_count = key_slabs.shape[0]
    key_row_block = key_slabs.reshape(block_count, -1, HD)
    value_row_block = value_slabs.reshape(block_count, -1, HD)
    score_matrix = (
        jnp.einsum(
            "nmv,njv->nmj", query_per_head, key_row_block, preferred_element_type=jnp.float32
        )
        * logit_scale
    )
    score_matrix = jnp.where(allowed, score_matrix, NEG)
    row_max = jnp.max(score_matrix, axis=-1, keepdims=True)
    log_total = row_max + jnp.log(jnp.sum(jnp.exp(score_matrix - row_max), axis=-1, keepdims=True))
    probabilities = jnp.exp(score_matrix - log_total)
    attention_weight = probabilities.astype(jnp.bfloat16)
    attended_per_head = jnp.einsum(
        "jym,jmo->jyo", attention_weight, value_row_block, preferred_element_type=jnp.float32
    ).astype(jnp.bfloat16)
    out_dot = jnp.sum(
        output_gradient_heads.astype(jnp.float32) * attended_per_head.astype(jnp.float32),
        axis=-1,
        keepdims=True,
    )
    probability_gradient = jnp.einsum(
        "nmv,njv->nmj", output_gradient_heads, value_row_block, preferred_element_type=jnp.float32
    )
    score_gradient = (probabilities * (probability_gradient - out_dot)).astype(jnp.bfloat16)
    query_gradient_heads = (
        jnp.einsum(
            "jym,jmo->jyo", score_gradient, key_row_block, preferred_element_type=jnp.float32
        )
        * logit_scale
    ).astype(jnp.bfloat16)
    key_gradient = (
        jnp.einsum(
            "uwj,uwn->ujn", score_gradient, query_per_head, preferred_element_type=jnp.float32
        )
        * logit_scale
    )
    value_gradient = jnp.einsum(
        "uwj,uwn->ujn", attention_weight, output_gradient_heads, preferred_element_type=jnp.float32
    )
    return (
        attended_per_head,
        query_gradient_heads,
        key_gradient,
        value_gradient,
        log_total[..., 0],
        out_dot[..., 0],
    )


def legacy_body(queries, key_tokens, value_tokens, grad_out):
    row_width = queries.shape[1]
    tok_count = queries.shape[0]
    blocks_dev = tok_count // BLK
    rim = (WINDOW + blocks_dev - 1) // blocks_dev
    devices = lax.axis_size("seq")
    near_list, far_list = offset_lists(devices * blocks_dev)
    offsets = near_list + far_list
    near_count = len(near_list)
    logit_scale = 1.0 / math.sqrt(HD)
    span_blocks = (rim + 1) * blocks_dev
    lead = rim * blocks_dev
    earlier_keys = []
    earlier_values = []
    for back in range(rim, 0, -1):
        got_keys, got_values = passed_along((key_tokens, value_tokens), "seq", back)
        earlier_keys.append(got_keys)
        earlier_values.append(got_values)
    span_keys = to_blocks(jnp.concatenate(earlier_keys + [key_tokens], axis=0), span_blocks)
    span_values = to_blocks(jnp.concatenate(earlier_values + [value_tokens], axis=0), span_blocks)
    far_keys = []
    far_values = []
    for stride in far_list:
        got_keys, got_values = passed_along((key_tokens, value_tokens), "seq", stride // blocks_dev)
        far_keys.append(to_blocks(got_keys, blocks_dev))
        far_values.append(to_blocks(got_values, blocks_dev))
    position = lax.axis_index("seq")
    allowed = allowed_mask(position * blocks_dev, blocks_dev, offsets)
    query_blocks = to_blocks(queries, blocks_dev)
    grad_blocks = to_blocks(grad_out, blocks_dev)
    attended_heads = []
    grad_query_heads = []
    near_key_heads = []
    near_value_heads = []
    total_heads = []
    dot_heads = []
    far_key_parts = [[] for stride in far_list]
    far_value_parts = [[] for stride in far_list]
    for head_index in range(HEADS):
        col_start = head_index * HD
        key_slabs = jnp.stack(
            [
                head_cols(span_keys[lead - offset : lead + blocks_dev - offset], col_start)
                for offset in near_list
            ]
            + [head_cols(item, col_start) for item in far_keys],
            axis=1,
        )
        value_slabs = jnp.stack(
            [
                head_cols(span_values[lead - offset : lead + blocks_dev - offset], col_start)
                for offset in near_list
            ]
            + [head_cols(item, col_start) for item in far_values],
            axis=1,
        )
        (
            attended_per_head,
            query_gradient_heads,
            key_gradient,
            value_gradient,
            log_total,
            out_dot,
        ) = head_pass(
            head_cols(query_blocks, col_start),
            head_cols(grad_blocks, col_start),
            key_slabs,
            value_slabs,
            allowed,
            logit_scale,
        )
        key_gradient = key_gradient.reshape(blocks_dev, -1, BLK, HD)
        value_gradient = value_gradient.reshape(blocks_dev, -1, BLK, HD)
        near_key_heads.append(place_slabs(key_gradient, near_list, lead, span_blocks))
        near_value_heads.append(place_slabs(value_gradient, near_list, lead, span_blocks))
        for level_index in range(len(far_list)):
            far_key_parts[level_index].append(
                key_gradient[:, near_count + level_index].astype(jnp.bfloat16)
            )
            far_value_parts[level_index].append(
                value_gradient[:, near_count + level_index].astype(jnp.bfloat16)
            )
        attended_heads.append(attended_per_head)
        grad_query_heads.append(query_gradient_heads)
        total_heads.append(log_total)
        dot_heads.append(out_dot)
    attended = jnp.concatenate(attended_heads, axis=-1).reshape(tok_count, row_width)
    grad_queries = jnp.concatenate(grad_query_heads, axis=-1).reshape(tok_count, row_width)
    near_keys = jnp.concatenate(near_key_heads, axis=-1).reshape((rim + 1) * tok_count, row_width)
    near_values = jnp.concatenate(near_value_heads, axis=-1).reshape(
        (rim + 1) * tok_count, row_width
    )
    total_keys = near_keys[lead * BLK :].astype(jnp.bfloat16).astype(jnp.float32)
    total_values = near_values[lead * BLK :].astype(jnp.bfloat16).astype(jnp.float32)
    for back in range(1, rim + 1):
        piece_start = (rim - back) * tok_count
        part_keys = near_keys[piece_start : piece_start + tok_count].astype(jnp.bfloat16)
        part_values = near_values[piece_start : piece_start + tok_count].astype(jnp.bfloat16)
        back_keys, back_values = passed_along((part_keys, part_values), "seq", -back)
        total_keys = total_keys + back_keys.astype(jnp.float32)
        total_values = total_values + back_values.astype(jnp.float32)
    for level_index, stride in enumerate(far_list):
        part_keys = jnp.concatenate(far_key_parts[level_index], axis=-1).reshape(
            tok_count, row_width
        )
        part_values = jnp.concatenate(far_value_parts[level_index], axis=-1).reshape(
            tok_count, row_width
        )
        got_keys, got_values = passed_along(
            (part_keys, part_values), "seq", -(stride // blocks_dev)
        )
        total_keys = total_keys + got_keys.astype(jnp.float32)
        total_values = total_values + got_values.astype(jnp.float32)
    return (
        attended,
        grad_queries,
        total_keys.astype(jnp.bfloat16),
        total_values.astype(jnp.bfloat16),
    )


def swap_pairs(count):
    return [(source, source ^ 1) for source in range(count) if source ^ 1 < count]


def relay_ok(count, blocks_dev, rim, far_shifts):
    return count % 2 == 0 and blocks_dev == 2 and rim == 2 and (not far_shifts or far_shifts[0] == 4)


def plan(tok_count, devices):
    blocks_dev = tok_count // BLK
    rim = (WINDOW + blocks_dev - 1) // blocks_dev
    near_list, far_list = offset_lists(devices * blocks_dev)
    far_shifts = [stride // blocks_dev for stride in far_list]
    return blocks_dev, rim, near_list, far_list, far_shifts


def row_pass(query_per_head, output_gradient_heads, key_slabs, value_slabs, allowed, logit_scale):
    block_count = key_slabs.shape[0]
    key_row_block = key_slabs.reshape(block_count, -1, HD)
    value_row_block = value_slabs.reshape(block_count, -1, HD)
    score_matrix = (
        jnp.einsum(
            "nmv,njv->nmj", query_per_head, key_row_block, preferred_element_type=jnp.float32
        )
        * logit_scale
    )
    score_matrix = jnp.where(allowed, score_matrix, NEG)
    row_max = jnp.max(score_matrix, axis=-1, keepdims=True)
    log_total = row_max + jnp.log(jnp.sum(jnp.exp(score_matrix - row_max), axis=-1, keepdims=True))
    probabilities = jnp.exp(score_matrix - log_total)
    attention_weight = probabilities.astype(jnp.bfloat16)
    attended_per_head = jnp.einsum(
        "jym,jmo->jyo", attention_weight, value_row_block, preferred_element_type=jnp.float32
    ).astype(jnp.bfloat16)
    out_dot = jnp.sum(
        output_gradient_heads.astype(jnp.float32) * attended_per_head.astype(jnp.float32),
        axis=-1,
        keepdims=True,
    )
    probability_gradient = jnp.einsum(
        "nmv,njv->nmj", output_gradient_heads, value_row_block, preferred_element_type=jnp.float32
    )
    score_gradient = (probabilities * (probability_gradient - out_dot)).astype(jnp.bfloat16)
    query_gradient_heads = (
        jnp.einsum(
            "jym,jmo->jyo", score_gradient, key_row_block, preferred_element_type=jnp.float32
        )
        * logit_scale
    ).astype(jnp.bfloat16)
    return attended_per_head, query_gradient_heads, log_total[..., 0], out_dot[..., 0]


def key_pass(key_per_head, value_per_head, query_slabs, grad_slabs, total_slabs, dot_slabs, allowed, logit_scale):
    block_count = query_slabs.shape[0]
    query_rows = query_slabs.reshape(block_count, -1, HD)
    grad_rows = grad_slabs.reshape(block_count, -1, HD)
    score_matrix = (
        jnp.einsum("nmv,njv->nmj", query_rows, key_per_head, preferred_element_type=jnp.float32)
        * logit_scale
    )
    total_rows = total_slabs.reshape(block_count, -1, 1)
    dot_rows = dot_slabs.reshape(block_count, -1, 1)
    probabilities = jnp.where(allowed, jnp.exp(score_matrix - total_rows), 0.0)
    probability_gradient = jnp.einsum(
        "nmv,njv->nmj", grad_rows, value_per_head, preferred_element_type=jnp.float32
    )
    score_gradient = (probabilities * (probability_gradient - dot_rows)).astype(jnp.bfloat16)
    attention_weight = probabilities.astype(jnp.bfloat16)
    key_gradient = (
        jnp.einsum("nmj,nmv->njv", score_gradient, query_rows, preferred_element_type=jnp.float32)
        * logit_scale
    )
    value_gradient = jnp.einsum(
        "nmj,nmv->njv", attention_weight, grad_rows, preferred_element_type=jnp.float32
    )
    return key_gradient, value_gradient


def key_allowed(first_block, blocks_dev, offsets, block_total):
    block_ids = first_block + jnp.arange(blocks_dev, dtype=jnp.int32)
    offset_arr = jnp.array(offsets, dtype=jnp.int32)
    query_live = block_ids[:, None] + offset_arr[None, :] < block_total
    row_ids = jnp.arange(BLK, dtype=jnp.int32)
    causal = row_ids[:, None] >= row_ids[None, :]
    later_slab = offset_arr > 0
    slab_causal = jnp.logical_or(later_slab[:, None, None], causal[None, :, :])
    allowed = jnp.logical_and(query_live[:, :, None, None], slab_causal[None, :, :, :])
    return allowed.reshape(blocks_dev, len(offsets) * BLK, BLK)


TRANS_B = (((1,), (1,)), ((), ()))


def span_load(refs, start, length, other, axis):
    size = refs[0].shape[axis]
    pieces = []
    at = start
    while length > 0:
        index, offset = at // size, at % size
        count = min(size - offset, length)
        window = pl.ds(offset, count)
        pieces.append(refs[index][window, other] if axis == 0 else refs[index][other, window])
        at += count
        length -= count
    return pieces[0] if len(pieces) == 1 else jnp.concatenate(pieces, axis=axis)


def row_kernel(near_count, far_list, heads, phase, *refs):
    far_count = len(far_list)
    position_ref, query_ref, grad_ref = refs[:3]
    span_refs = refs[3:6]
    far_refs = refs[6 : 6 + far_count]
    if phase == "stats":
        attended_ref, stats_ref, stats_rows_ref = refs[6 + far_count :]
    else:
        stats_in_ref, grad_query_ref = refs[6 + far_count :]
    width = heads * HD
    near_rows = near_count * BLK
    scale = 1.0 / math.sqrt(HD)
    first = 2 * position_ref[0]
    near_row_ids = lax.broadcasted_iota(jnp.int32, (BLK, near_rows), 0)
    near_col_ids = lax.broadcasted_iota(jnp.int32, (BLK, near_rows), 1)
    near_offset = (near_count - 1) - near_col_ids // BLK
    near_causal = jnp.logical_or(near_offset > 0, near_row_ids >= near_col_ids % BLK)
    lane_ids = lax.broadcasted_iota(jnp.int32, (BLK, 2 * heads), 1)
    for block in range(2):
        rows = pl.ds(block * BLK, BLK)
        near_span = pl.ds(block * BLK, near_rows)
        near_mask = jnp.logical_and(near_causal, first + block - near_offset >= 0)
        far_live = [first + block - offset >= 0 for offset in far_list]
        masks = [near_mask] + far_live
        if phase == "stats":
            stats_tile = jnp.zeros((BLK, 2 * heads), jnp.float32)
        else:
            stats_tile = stats_in_ref[rows, :]
        for head in range(heads):
            cols = pl.ds(head * HD, HD)
            value_cols = pl.ds(width + head * HD, HD)
            query = query_ref[rows, cols]
            grad = grad_ref[rows, cols]
            keys = [span_load(span_refs, block * BLK, near_rows, cols, 0)]
            keys = keys + [item[rows, cols] for item in far_refs]
            values = [span_load(span_refs, block * BLK, near_rows, value_cols, 0)]
            values = values + [item[rows, value_cols] for item in far_refs]
            scores = [
                lax.dot_general(query, key, TRANS_B, preferred_element_type=jnp.float32) * scale
                for key in keys
            ]
            if phase == "grad":
                log_total = jnp.sum(jnp.where(lane_ids == head, stats_tile, 0.0), axis=-1, keepdims=True)
                out_dot = jnp.sum(
                    jnp.where(lane_ids == heads + head, stats_tile, 0.0), axis=-1, keepdims=True
                )
                probs = [
                    jnp.where(mask, jnp.exp(score - log_total), 0.0)
                    for score, mask in zip(scores, masks)
                ]
                grad_query = jnp.zeros((BLK, HD), jnp.float32)
                for prob, key, value in zip(probs, keys, values):
                    prob_grad = lax.dot_general(
                        grad, value, TRANS_B, preferred_element_type=jnp.float32
                    )
                    score_grad = (prob * (prob_grad - out_dot)).astype(jnp.bfloat16)
                    grad_query = grad_query + jnp.dot(
                        score_grad, key, preferred_element_type=jnp.float32
                    )
                grad_query_ref[rows, cols] = (grad_query * scale).astype(jnp.bfloat16)
                continue
            scores = [jnp.where(mask, score, NEG) for score, mask in zip(scores, masks)]
            row_max = scores[0].max(axis=-1, keepdims=True)
            for score in scores[1:]:
                row_max = jnp.maximum(row_max, score.max(axis=-1, keepdims=True))
            shifted = [jnp.exp(score - row_max) for score in scores]
            row_sum = shifted[0].sum(axis=-1, keepdims=True)
            for item in shifted[1:]:
                row_sum = row_sum + item.sum(axis=-1, keepdims=True)
            log_total = row_max + jnp.log(row_sum)
            inverse = 1.0 / row_sum
            attended = jnp.zeros((BLK, HD), jnp.float32)
            for item, value in zip(shifted, values):
                attended = attended + jnp.dot(
                    (item * inverse).astype(jnp.bfloat16), value, preferred_element_type=jnp.float32
                )
            attended = attended.astype(jnp.bfloat16)
            attended_ref[rows, cols] = attended
            out_dot = jnp.sum(
                grad.astype(jnp.float32) * attended.astype(jnp.float32), axis=-1, keepdims=True
            )
            stats_tile = stats_tile + jnp.where(lane_ids == head, log_total, 0.0)
            stats_tile = stats_tile + jnp.where(lane_ids == heads + head, out_dot, 0.0)
        if phase == "stats":
            stats_ref[rows, :] = stats_tile
            wide_lanes = lax.broadcasted_iota(jnp.int32, (BLK, BLK), 1)
            wide = jnp.zeros((BLK, BLK), jnp.float32)
            for lane in range(2 * heads):
                column = jnp.sum(jnp.where(lane_ids == lane, stats_tile, 0.0), axis=-1, keepdims=True)
                wide = wide + jnp.where(wide_lanes == lane, column, 0.0)
            stats_rows_ref[:, rows] = wide.T[: 2 * heads, :]


def estimate(tok_count, row_width, slab_rows, matmuls, exps):
    flops = 2 * tok_count * slab_rows * HD * matmuls * (row_width // HD)
    return pl.CostEstimate(
        flops=flops,
        transcendentals=tok_count * slab_rows * exps * (row_width // HD),
        bytes_accessed=8 * tok_count * row_width * 4,
    )


def key_kernel(near_count, far_list, heads, block_total, *refs):
    far_count = len(far_list)
    position_ref, own_ref = refs[:2]
    span_refs = refs[2:5]
    stats_refs = refs[5:8]
    far_rows = refs[8 : 8 + far_count]
    far_stats = refs[8 + far_count : 8 + 2 * far_count]
    grad_key_ref, grad_value_ref = refs[8 + 2 * far_count :]
    width = heads * HD
    near_rows = near_count * BLK
    scale = 1.0 / math.sqrt(HD)
    first = 2 * position_ref[0]
    near_key_ids = lax.broadcasted_iota(jnp.int32, (BLK, near_rows), 0)
    near_query_ids = lax.broadcasted_iota(jnp.int32, (BLK, near_rows), 1)
    near_offset = near_query_ids // BLK
    near_causal = jnp.logical_or(near_offset > 0, near_query_ids % BLK >= near_key_ids)
    for block in range(2):
        rows = pl.ds(block * BLK, BLK)
        near_span = pl.ds(block * BLK, near_rows)
        near_mask = jnp.logical_and(near_causal, first + block + near_offset < block_total)
        far_live = [first + block + offset < block_total for offset in far_list]
        masks = [near_mask] + far_live
        for head in range(heads):
            cols = pl.ds(head * HD, HD)
            value_cols = pl.ds(width + head * HD, HD)
            key = own_ref[rows, cols]
            value = own_ref[rows, value_cols]
            queries = [span_load(span_refs, block * BLK, near_rows, cols, 0)]
            queries = queries + [item[rows, cols] for item in far_rows]
            grads = [span_load(span_refs, block * BLK, near_rows, value_cols, 0)]
            grads = grads + [item[rows, value_cols] for item in far_rows]
            totals = [span_load(stats_refs, block * BLK, near_rows, pl.ds(head, 1), 1)] + [
                item[pl.ds(head, 1), rows] for item in far_stats
            ]
            dots = [span_load(stats_refs, block * BLK, near_rows, pl.ds(heads + head, 1), 1)] + [
                item[pl.ds(heads + head, 1), rows] for item in far_stats
            ]
            grad_key = jnp.zeros((BLK, HD), jnp.float32)
            grad_value = jnp.zeros((BLK, HD), jnp.float32)
            for query, grad, log_total, out_dot, mask in zip(queries, grads, totals, dots, masks):
                score = lax.dot_general(key, query, TRANS_B, preferred_element_type=jnp.float32)
                prob = jnp.where(mask, jnp.exp(score * scale - log_total), 0.0)
                prob_grad = lax.dot_general(value, grad, TRANS_B, preferred_element_type=jnp.float32)
                score_grad = (prob * (prob_grad - out_dot)).astype(jnp.bfloat16)
                grad_value = grad_value + jnp.dot(
                    prob.astype(jnp.bfloat16), grad, preferred_element_type=jnp.float32
                )
                grad_key = grad_key + jnp.dot(score_grad, query, preferred_element_type=jnp.float32)
            grad_key_ref[rows, cols] = (grad_key * scale).astype(jnp.bfloat16)
            grad_value_ref[rows, cols] = grad_value.astype(jnp.bfloat16)


def smem_spec():
    return pl.BlockSpec(memory_space=pltpu.SMEM)


def vmem_spec():
    return pl.BlockSpec(memory_space=pltpu.VMEM)


def body(queries, key_tokens, value_tokens, grad_out):
    row_width = queries.shape[1]
    tok_count = queries.shape[0]
    devices = lax.axis_size("seq")
    blocks_dev, rim, near_list, far_list, far_shifts = plan(tok_count, devices)
    if not relay_ok(devices, blocks_dev, rim, far_shifts):
        return legacy_body(queries, key_tokens, value_tokens, grad_out)
    heads = row_width // HD
    offsets = near_list + far_list
    logit_scale = 1.0 / math.sqrt(HD)
    span_blocks = (rim + 1) * blocks_dev
    lead = rim * blocks_dev
    position = lax.axis_index("seq")
    odd = (position % 2) == 1
    pairs = swap_pairs(devices)
    keys_values = jnp.concatenate([key_tokens, value_tokens], axis=1)
    queries_grads = jnp.concatenate([queries, grad_out], axis=1)
    back2 = passed_along(keys_values, "seq", 2)
    ahead2 = passed_along(queries_grads, "seq", -2)
    swap_one = lax.ppermute(jnp.where(odd, queries_grads, keys_values), "seq", pairs)
    back4 = passed_along(back2, "seq", 2)
    ahead4 = passed_along(ahead2, "seq", -2)
    swap_two = lax.ppermute(jnp.where(odd, back2, ahead2), "seq", pairs)
    back1 = jnp.where(odd, swap_one, swap_two)
    ahead1 = jnp.where(odd, swap_two, swap_one)
    far_back = [back4] + [passed_along(keys_values, "seq", shift) for shift in far_shifts[1:]]
    far_ahead = [ahead4] + [passed_along(queries_grads, "seq", -shift) for shift in far_shifts[1:]]
    far_back = far_back[: len(far_shifts)]
    far_ahead = far_ahead[: len(far_shifts)]

    position_arr = jnp.reshape(position, (1,)).astype(jnp.int32)
    far_offsets = list(far_list)
    slab_rows = (len(near_list) + len(far_list)) * BLK
    row_inputs = (position_arr, queries, grad_out, back2, back1, keys_values, *far_back)
    attended, stats, stats_rows = pl.pallas_call(
        functools.partial(row_kernel, len(near_list), far_offsets, heads, "stats"),
        out_shape=(
            jax.ShapeDtypeStruct((tok_count, row_width), jnp.bfloat16),
            jax.ShapeDtypeStruct((tok_count, 2 * heads), jnp.float32),
            jax.ShapeDtypeStruct((2 * heads, tok_count), jnp.float32),
        ),
        in_specs=[smem_spec()] + [vmem_spec()] * (5 + len(far_back)),
        out_specs=(vmem_spec(), vmem_spec(), vmem_spec()),
        cost_estimate=estimate(tok_count, row_width, slab_rows, 2, 1),
        name="rows_stats",
    )(*row_inputs)
    stats_one = passed_along(stats_rows, "seq", -1)
    stats_two = passed_along(stats_rows, "seq", -2)
    far_stats = [passed_along(stats_rows, "seq", -shift) for shift in far_shifts]
    grad_queries = pl.pallas_call(
        functools.partial(row_kernel, len(near_list), far_offsets, heads, "grad"),
        out_shape=jax.ShapeDtypeStruct((tok_count, row_width), jnp.bfloat16),
        in_specs=[smem_spec()] + [vmem_spec()] * (6 + len(far_back)),
        out_specs=vmem_spec(),
        cost_estimate=estimate(tok_count, row_width, slab_rows, 3, 1),
        name="rows_grad",
    )(*row_inputs, stats)
    grad_keys, grad_values = pl.pallas_call(
        functools.partial(key_kernel, len(near_list), far_offsets, heads, devices * blocks_dev),
        out_shape=(
            jax.ShapeDtypeStruct((tok_count, row_width), jnp.bfloat16),
            jax.ShapeDtypeStruct((tok_count, row_width), jnp.bfloat16),
        ),
        in_specs=[smem_spec()] + [vmem_spec()] * (7 + 2 * len(far_ahead)),
        out_specs=(vmem_spec(), vmem_spec()),
        cost_estimate=estimate(tok_count, row_width, slab_rows, 4, 1),
        name="keys_pass",
    )(
        position_arr,
        keys_values,
        queries_grads,
        ahead1,
        ahead2,
        stats_rows,
        stats_one,
        stats_two,
        *far_ahead,
        *far_stats,
    )
    return attended, grad_queries, grad_keys, grad_values


def solution(mesh):
    placed = (
        P(("rep", "seq"), None),
        P(("rep", "seq"), None),
        P(("rep", "seq"), None),
        P(("rep", "seq"), None),
    )
    return jax.shard_map(
        body,
        mesh=mesh,
        in_specs=placed,
        out_specs=(
            P(("rep", "seq"), None),
            P(("rep", "seq"), None),
            P(("rep", "seq"), None),
            P(("rep", "seq"), None),
        ),
        check_vma=False,
    )
```

```python
import functools
import math

import jax
import jax.numpy as jnp
from jax import lax
from jax.experimental import pallas as pl
from jax.experimental.pallas import tpu as pltpu
from jax.sharding import PartitionSpec as P

HEADS = 4
HD = 128
BLK = 128
WINDOW = 4


NEG = -1e30
CHUNKS = 2


def passed_along(value, axis, steps):
    count = lax.axis_size(axis)
    first, last = (max(0, -steps), min(count, count - steps))
    return lax.ppermute(value, axis, [(source, source + steps) for source in range(first, last)])


def offset_lists(block_total):
    near_list = list(range(WINDOW + 1))
    far_list = []
    stride = 1
    while stride < block_total:
        if stride > WINDOW:
            far_list.append(stride)
        stride = stride * 2
    return (near_list, far_list)


def allowed_mask(first_block, blocks_dev, offsets):
    block_ids = first_block + jnp.arange(blocks_dev, dtype=jnp.int32)
    offset_arr = jnp.array(offsets, dtype=jnp.int32)
    block_live = block_ids[:, None] - offset_arr[None, :] >= 0
    row_ids = jnp.arange(BLK, dtype=jnp.int32)
    causal = row_ids[:, None] >= row_ids[None, :]
    later_slab = offset_arr > 0
    slab_causal = jnp.logical_or(later_slab[None, :, None], causal[:, None, :])
    allowed = jnp.logical_and(block_live[:, None, :, None], slab_causal[None, :, :, :])
    return allowed.reshape(blocks_dev, BLK, len(offsets) * BLK)


def head_cols(array_in, col_start):
    return array_in[..., col_start : col_start + HD]


def to_blocks(array_in, block_count):
    return array_in.reshape(block_count, BLK, array_in.shape[-1])


def place_slabs(gradient, near_list, lead, span_blocks):
    blocks_dev = gradient.shape[0]
    placed = []
    for slot_index, offset in enumerate(near_list):
        before = lead - offset
        after = span_blocks - before - blocks_dev
        placed.append(jnp.pad(gradient[:, slot_index], ((before, after), (0, 0), (0, 0))))
    total = placed[0]
    for item in placed[1:]:
        total = total + item
    return total


def head_pass(query_per_head, output_gradient_heads, key_slabs, value_slabs, allowed, logit_scale):
    block_count = key_slabs.shape[0]
    key_row_block = key_slabs.reshape(block_count, -1, HD)
    value_row_block = value_slabs.reshape(block_count, -1, HD)
    score_matrix = (
        jnp.einsum(
            "nmv,njv->nmj", query_per_head, key_row_block, preferred_element_type=jnp.float32
        )
        * logit_scale
    )
    score_matrix = jnp.where(allowed, score_matrix, NEG)
    row_max = jnp.max(score_matrix, axis=-1, keepdims=True)
    log_total = row_max + jnp.log(jnp.sum(jnp.exp(score_matrix - row_max), axis=-1, keepdims=True))
    probabilities = jnp.exp(score_matrix - log_total)
    attention_weight = probabilities.astype(jnp.bfloat16)
    attended_per_head = jnp.einsum(
        "jym,jmo->jyo", attention_weight, value_row_block, preferred_element_type=jnp.float32
    ).astype(jnp.bfloat16)
    out_dot = jnp.sum(
        output_gradient_heads.astype(jnp.float32) * attended_per_head.astype(jnp.float32),
        axis=-1,
        keepdims=True,
    )
    probability_gradient = jnp.einsum(
        "nmv,njv->nmj", output_gradient_heads, value_row_block, preferred_element_type=jnp.float32
    )
    score_gradient = (probabilities * (probability_gradient - out_dot)).astype(jnp.bfloat16)
    query_gradient_heads = (
        jnp.einsum(
            "jym,jmo->jyo", score_gradient, key_row_block, preferred_element_type=jnp.float32
        )
        * logit_scale
    ).astype(jnp.bfloat16)
    key_gradient = (
        jnp.einsum(
            "uwj,uwn->ujn", score_gradient, query_per_head, preferred_element_type=jnp.float32
        )
        * logit_scale
    )
    value_gradient = jnp.einsum(
        "uwj,uwn->ujn", attention_weight, output_gradient_heads, preferred_element_type=jnp.float32
    )
    return (
        attended_per_head,
        query_gradient_heads,
        key_gradient,
        value_gradient,
        log_total[..., 0],
        out_dot[..., 0],
    )


def legacy_body(queries, key_tokens, value_tokens, grad_out):
    row_width = queries.shape[1]
    tok_count = queries.shape[0]
    blocks_dev = tok_count // BLK
    rim = (WINDOW + blocks_dev - 1) // blocks_dev
    devices = lax.axis_size("seq")
    near_list, far_list = offset_lists(devices * blocks_dev)
    offsets = near_list + far_list
    near_count = len(near_list)
    logit_scale = 1.0 / math.sqrt(HD)
    span_blocks = (rim + 1) * blocks_dev
    lead = rim * blocks_dev
    earlier_keys = []
    earlier_values = []
    for back in range(rim, 0, -1):
        got_keys, got_values = passed_along((key_tokens, value_tokens), "seq", back)
        earlier_keys.append(got_keys)
        earlier_values.append(got_values)
    span_keys = to_blocks(jnp.concatenate(earlier_keys + [key_tokens], axis=0), span_blocks)
    span_values = to_blocks(jnp.concatenate(earlier_values + [value_tokens], axis=0), span_blocks)
    far_keys = []
    far_values = []
    for stride in far_list:
        got_keys, got_values = passed_along((key_tokens, value_tokens), "seq", stride // blocks_dev)
        far_keys.append(to_blocks(got_keys, blocks_dev))
        far_values.append(to_blocks(got_values, blocks_dev))
    position = lax.axis_index("seq")
    allowed = allowed_mask(position * blocks_dev, blocks_dev, offsets)
    query_blocks = to_blocks(queries, blocks_dev)
    grad_blocks = to_blocks(grad_out, blocks_dev)
    attended_heads = []
    grad_query_heads = []
    near_key_heads = []
    near_value_heads = []
    total_heads = []
    dot_heads = []
    far_key_parts = [[] for stride in far_list]
    far_value_parts = [[] for stride in far_list]
    for head_index in range(HEADS):
        col_start = head_index * HD
        key_slabs = jnp.stack(
            [
                head_cols(span_keys[lead - offset : lead + blocks_dev - offset], col_start)
                for offset in near_list
            ]
            + [head_cols(item, col_start) for item in far_keys],
            axis=1,
        )
        value_slabs = jnp.stack(
            [
                head_cols(span_values[lead - offset : lead + blocks_dev - offset], col_start)
                for offset in near_list
            ]
            + [head_cols(item, col_start) for item in far_values],
            axis=1,
        )
        (
            attended_per_head,
            query_gradient_heads,
            key_gradient,
            value_gradient,
            log_total,
            out_dot,
        ) = head_pass(
            head_cols(query_blocks, col_start),
            head_cols(grad_blocks, col_start),
            key_slabs,
            value_slabs,
            allowed,
            logit_scale,
        )
        key_gradient = key_gradient.reshape(blocks_dev, -1, BLK, HD)
        value_gradient = value_gradient.reshape(blocks_dev, -1, BLK, HD)
        near_key_heads.append(place_slabs(key_gradient, near_list, lead, span_blocks))
        near_value_heads.append(place_slabs(value_gradient, near_list, lead, span_blocks))
        for level_index in range(len(far_list)):
            far_key_parts[level_index].append(
                key_gradient[:, near_count + level_index].astype(jnp.bfloat16)
            )
            far_value_parts[level_index].append(
                value_gradient[:, near_count + level_index].astype(jnp.bfloat16)
            )
        attended_heads.append(attended_per_head)
        grad_query_heads.append(query_gradient_heads)
        total_heads.append(log_total)
        dot_heads.append(out_dot)
    attended = jnp.concatenate(attended_heads, axis=-1).reshape(tok_count, row_width)
    grad_queries = jnp.concatenate(grad_query_heads, axis=-1).reshape(tok_count, row_width)
    near_keys = jnp.concatenate(near_key_heads, axis=-1).reshape((rim + 1) * tok_count, row_width)
    near_values = jnp.concatenate(near_value_heads, axis=-1).reshape(
        (rim + 1) * tok_count, row_width
    )
    total_keys = near_keys[lead * BLK :].astype(jnp.bfloat16).astype(jnp.float32)
    total_values = near_values[lead * BLK :].astype(jnp.bfloat16).astype(jnp.float32)
    for back in range(1, rim + 1):
        piece_start = (rim - back) * tok_count
        part_keys = near_keys[piece_start : piece_start + tok_count].astype(jnp.bfloat16)
        part_values = near_values[piece_start : piece_start + tok_count].astype(jnp.bfloat16)
        back_keys, back_values = passed_along((part_keys, part_values), "seq", -back)
        total_keys = total_keys + back_keys.astype(jnp.float32)
        total_values = total_values + back_values.astype(jnp.float32)
    for level_index, stride in enumerate(far_list):
        part_keys = jnp.concatenate(far_key_parts[level_index], axis=-1).reshape(
            tok_count, row_width
        )
        part_values = jnp.concatenate(far_value_parts[level_index], axis=-1).reshape(
            tok_count, row_width
        )
        got_keys, got_values = passed_along(
            (part_keys, part_values), "seq", -(stride // blocks_dev)
        )
        total_keys = total_keys + got_keys.astype(jnp.float32)
        total_values = total_values + got_values.astype(jnp.float32)
    return (
        attended,
        grad_queries,
        total_keys.astype(jnp.bfloat16),
        total_values.astype(jnp.bfloat16),
    )


def swap_pairs(count):
    return [(source, source ^ 1) for source in range(count) if source ^ 1 < count]


def relay_ok(count, blocks_dev, rim, far_shifts):
    return count % 2 == 0 and blocks_dev == 2 and rim == 2 and (not far_shifts or far_shifts[0] == 4)


def plan(tok_count, devices):
    blocks_dev = tok_count // BLK
    rim = (WINDOW + blocks_dev - 1) // blocks_dev
    near_list, far_list = offset_lists(devices * blocks_dev)
    far_shifts = [stride // blocks_dev for stride in far_list]
    return blocks_dev, rim, near_list, far_list, far_shifts


def row_pass(query_per_head, output_gradient_heads, key_slabs, value_slabs, allowed, logit_scale):
    block_count = key_slabs.shape[0]
    key_row_block = key_slabs.reshape(block_count, -1, HD)
    value_row_block = value_slabs.reshape(block_count, -1, HD)
    score_matrix = (
        jnp.einsum(
            "nmv,njv->nmj", query_per_head, key_row_block, preferred_element_type=jnp.float32
        )
        * logit_scale
    )
    score_matrix = jnp.where(allowed, score_matrix, NEG)
    row_max = jnp.max(score_matrix, axis=-1, keepdims=True)
    log_total = row_max + jnp.log(jnp.sum(jnp.exp(score_matrix - row_max), axis=-1, keepdims=True))
    probabilities = jnp.exp(score_matrix - log_total)
    attention_weight = probabilities.astype(jnp.bfloat16)
    attended_per_head = jnp.einsum(
        "jym,jmo->jyo", attention_weight, value_row_block, preferred_element_type=jnp.float32
    ).astype(jnp.bfloat16)
    out_dot = jnp.sum(
        output_gradient_heads.astype(jnp.float32) * attended_per_head.astype(jnp.float32),
        axis=-1,
        keepdims=True,
    )
    probability_gradient = jnp.einsum(
        "nmv,njv->nmj", output_gradient_heads, value_row_block, preferred_element_type=jnp.float32
    )
    score_gradient = (probabilities * (probability_gradient - out_dot)).astype(jnp.bfloat16)
    query_gradient_heads = (
        jnp.einsum(
            "jym,jmo->jyo", score_gradient, key_row_block, preferred_element_type=jnp.float32
        )
        * logit_scale
    ).astype(jnp.bfloat16)
    return attended_per_head, query_gradient_heads, log_total[..., 0], out_dot[..., 0]


def key_pass(key_per_head, value_per_head, query_slabs, grad_slabs, total_slabs, dot_slabs, allowed, logit_scale):
    block_count = query_slabs.shape[0]
    query_rows = query_slabs.reshape(block_count, -1, HD)
    grad_rows = grad_slabs.reshape(block_count, -1, HD)
    score_matrix = (
        jnp.einsum("nmv,njv->nmj", query_rows, key_per_head, preferred_element_type=jnp.float32)
        * logit_scale
    )
    total_rows = total_slabs.reshape(block_count, -1, 1)
    dot_rows = dot_slabs.reshape(block_count, -1, 1)
    probabilities = jnp.where(allowed, jnp.exp(score_matrix - total_rows), 0.0)
    probability_gradient = jnp.einsum(
        "nmv,njv->nmj", grad_rows, value_per_head, preferred_element_type=jnp.float32
    )
    score_gradient = (probabilities * (probability_gradient - dot_rows)).astype(jnp.bfloat16)
    attention_weight = probabilities.astype(jnp.bfloat16)
    key_gradient = (
        jnp.einsum("nmj,nmv->njv", score_gradient, query_rows, preferred_element_type=jnp.float32)
        * logit_scale
    )
    value_gradient = jnp.einsum(
        "nmj,nmv->njv", attention_weight, grad_rows, preferred_element_type=jnp.float32
    )
    return key_gradient, value_gradient


def key_allowed(first_block, blocks_dev, offsets, block_total):
    block_ids = first_block + jnp.arange(blocks_dev, dtype=jnp.int32)
    offset_arr = jnp.array(offsets, dtype=jnp.int32)
    query_live = block_ids[:, None] + offset_arr[None, :] < block_total
    row_ids = jnp.arange(BLK, dtype=jnp.int32)
    causal = row_ids[:, None] >= row_ids[None, :]
    later_slab = offset_arr > 0
    slab_causal = jnp.logical_or(later_slab[:, None, None], causal[None, :, :])
    allowed = jnp.logical_and(query_live[:, :, None, None], slab_causal[None, :, :, :])
    return allowed.reshape(blocks_dev, len(offsets) * BLK, BLK)


TRANS_B = (((1,), (1,)), ((), ()))


def ref_load(ref, window, other, axis):
    return ref[window, other] if axis == 0 else ref[other, window]


def span_load(refs, start, length, other, axis, odd=None):
    size = refs[0].shape[axis]
    pieces = []
    at = start
    while length > 0:
        index, offset = at // size, at % size
        count = min(size - offset, length)
        window = pl.ds(offset, count)
        if isinstance(refs[index], tuple):
            when_odd, when_even = refs[index]
            pieces.append(
                jnp.where(
                    odd,
                    ref_load(when_odd, window, other, axis),
                    ref_load(when_even, window, other, axis),
                )
            )
        else:
            pieces.append(ref_load(refs[index], window, other, axis))
        at += count
        length -= count
    return pieces[0] if len(pieces) == 1 else jnp.concatenate(pieces, axis=axis)


def row_kernel(near_count, far_list, heads, phase, *refs):
    far_count = len(far_list)
    position_ref, query_ref, grad_ref = refs[:3]
    span_refs = (refs[3], (refs[4], refs[5]), refs[6])
    far_refs = refs[7 : 7 + far_count]
    if phase == "stats":
        attended_ref, stats_ref, stats_rows_ref = refs[7 + far_count :]
    else:
        stats_in_ref, grad_query_ref = refs[7 + far_count :]
    odd = position_ref[0] % 2 == 1
    width = heads * HD
    near_rows = near_count * BLK
    scale = 1.0 / math.sqrt(HD)
    first = 2 * position_ref[0]
    near_row_ids = lax.broadcasted_iota(jnp.int32, (BLK, near_rows), 0)
    near_col_ids = lax.broadcasted_iota(jnp.int32, (BLK, near_rows), 1)
    near_offset = (near_count - 1) - near_col_ids // BLK
    near_causal = jnp.logical_or(near_offset > 0, near_row_ids >= near_col_ids % BLK)
    lane_ids = lax.broadcasted_iota(jnp.int32, (BLK, 2 * heads), 1)
    for block in range(2):
        rows = pl.ds(block * BLK, BLK)
        near_span = pl.ds(block * BLK, near_rows)
        near_mask = jnp.logical_and(near_causal, first + block - near_offset >= 0)
        far_live = [first + block - offset >= 0 for offset in far_list]
        masks = [near_mask] + far_live
        if phase == "stats":
            stats_tile = jnp.zeros((BLK, 2 * heads), jnp.float32)
        else:
            stats_tile = stats_in_ref[rows, :]
        for head in range(heads):
            cols = pl.ds(head * HD, HD)
            value_cols = pl.ds(width + head * HD, HD)
            query = query_ref[rows, cols]
            grad = grad_ref[rows, cols]
            keys = [span_load(span_refs, block * BLK, near_rows, cols, 0, odd)]
            keys = keys + [item[rows, cols] for item in far_refs]
            values = [span_load(span_refs, block * BLK, near_rows, value_cols, 0, odd)]
            values = values + [item[rows, value_cols] for item in far_refs]
            scores = [
                lax.dot_general(query, key, TRANS_B, preferred_element_type=jnp.float32) * scale
                for key in keys
            ]
            if phase == "grad":
                log_total = jnp.sum(jnp.where(lane_ids == head, stats_tile, 0.0), axis=-1, keepdims=True)
                out_dot = jnp.sum(
                    jnp.where(lane_ids == heads + head, stats_tile, 0.0), axis=-1, keepdims=True
                )
                probs = [
                    jnp.where(mask, jnp.exp(score - log_total), 0.0)
                    for score, mask in zip(scores, masks)
                ]
                grad_query = jnp.zeros((BLK, HD), jnp.float32)
                for prob, key, value in zip(probs, keys, values):
                    prob_grad = lax.dot_general(
                        grad, value, TRANS_B, preferred_element_type=jnp.float32
                    )
                    score_grad = (prob * (prob_grad - out_dot)).astype(jnp.bfloat16)
                    grad_query = grad_query + jnp.dot(
                        score_grad, key, preferred_element_type=jnp.float32
                    )
                grad_query_ref[rows, cols] = (grad_query * scale).astype(jnp.bfloat16)
                continue
            scores = [jnp.where(mask, score, NEG) for score, mask in zip(scores, masks)]
            row_max = scores[0].max(axis=-1, keepdims=True)
            for score in scores[1:]:
                row_max = jnp.maximum(row_max, score.max(axis=-1, keepdims=True))
            shifted = [jnp.exp(score - row_max) for score in scores]
            row_sum = shifted[0].sum(axis=-1, keepdims=True)
            for item in shifted[1:]:
                row_sum = row_sum + item.sum(axis=-1, keepdims=True)
            log_total = row_max + jnp.log(row_sum)
            inverse = 1.0 / row_sum
            attended = jnp.zeros((BLK, HD), jnp.float32)
            for item, value in zip(shifted, values):
                attended = attended + jnp.dot(
                    (item * inverse).astype(jnp.bfloat16), value, preferred_element_type=jnp.float32
                )
            attended = attended.astype(jnp.bfloat16)
            attended_ref[rows, cols] = attended
            out_dot = jnp.sum(
                grad.astype(jnp.float32) * attended.astype(jnp.float32), axis=-1, keepdims=True
            )
            stats_tile = stats_tile + jnp.where(lane_ids == head, log_total, 0.0)
            stats_tile = stats_tile + jnp.where(lane_ids == heads + head, out_dot, 0.0)
        if phase == "stats":
            stats_ref[rows, :] = stats_tile
            wide_lanes = lax.broadcasted_iota(jnp.int32, (BLK, BLK), 1)
            wide = jnp.zeros((BLK, BLK), jnp.float32)
            for lane in range(2 * heads):
                column = jnp.sum(jnp.where(lane_ids == lane, stats_tile, 0.0), axis=-1, keepdims=True)
                wide = wide + jnp.where(wide_lanes == lane, column, 0.0)
            stats_rows_ref[:, rows] = wide.T[: 2 * heads, :]


def estimate(tok_count, row_width, slab_rows, matmuls, exps):
    flops = 2 * tok_count * slab_rows * HD * matmuls * (row_width // HD)
    return pl.CostEstimate(
        flops=flops,
        transcendentals=tok_count * slab_rows * exps * (row_width // HD),
        bytes_accessed=8 * tok_count * row_width * 4,
    )


def key_kernel(near_count, far_list, heads, block_total, *refs):
    far_count = len(far_list)
    position_ref, own_ref = refs[:2]
    span_refs = (refs[2], (refs[3], refs[4]), refs[5])
    stats_refs = refs[6:9]
    far_rows = refs[9 : 9 + far_count]
    far_stats = refs[9 + far_count : 9 + 2 * far_count]
    grad_key_ref, grad_value_ref = refs[9 + 2 * far_count :]
    odd = position_ref[0] % 2 == 1
    width = heads * HD
    near_rows = near_count * BLK
    scale = 1.0 / math.sqrt(HD)
    first = 2 * position_ref[0]
    near_key_ids = lax.broadcasted_iota(jnp.int32, (BLK, near_rows), 0)
    near_query_ids = lax.broadcasted_iota(jnp.int32, (BLK, near_rows), 1)
    near_offset = near_query_ids // BLK
    near_causal = jnp.logical_or(near_offset > 0, near_query_ids % BLK >= near_key_ids)
    for block in range(2):
        rows = pl.ds(block * BLK, BLK)
        near_span = pl.ds(block * BLK, near_rows)
        near_mask = jnp.logical_and(near_causal, first + block + near_offset < block_total)
        far_live = [first + block + offset < block_total for offset in far_list]
        masks = [near_mask] + far_live
        for head in range(heads):
            cols = pl.ds(head * HD, HD)
            value_cols = pl.ds(width + head * HD, HD)
            key = own_ref[rows, cols]
            value = own_ref[rows, value_cols]
            queries = [span_load(span_refs, block * BLK, near_rows, cols, 0, odd)]
            queries = queries + [item[rows, cols] for item in far_rows]
            grads = [span_load(span_refs, block * BLK, near_rows, value_cols, 0, odd)]
            grads = grads + [item[rows, value_cols] for item in far_rows]
            totals = [span_load(stats_refs, block * BLK, near_rows, pl.ds(head, 1), 1)] + [
                item[pl.ds(head, 1), rows] for item in far_stats
            ]
            dots = [span_load(stats_refs, block * BLK, near_rows, pl.ds(heads + head, 1), 1)] + [
                item[pl.ds(heads + head, 1), rows] for item in far_stats
            ]
            grad_key = jnp.zeros((BLK, HD), jnp.float32)
            grad_value = jnp.zeros((BLK, HD), jnp.float32)
            for query, grad, log_total, out_dot, mask in zip(queries, grads, totals, dots, masks):
                score = lax.dot_general(key, query, TRANS_B, preferred_element_type=jnp.float32)
                prob = jnp.where(mask, jnp.exp(score * scale - log_total), 0.0)
                prob_grad = lax.dot_general(value, grad, TRANS_B, preferred_element_type=jnp.float32)
                score_grad = (prob * (prob_grad - out_dot)).astype(jnp.bfloat16)
                grad_value = grad_value + jnp.dot(
                    prob.astype(jnp.bfloat16), grad, preferred_element_type=jnp.float32
                )
                grad_key = grad_key + jnp.dot(score_grad, query, preferred_element_type=jnp.float32)
            grad_key_ref[rows, cols] = (grad_key * scale).astype(jnp.bfloat16)
            grad_value_ref[rows, cols] = grad_value.astype(jnp.bfloat16)


def smem_spec():
    return pl.BlockSpec(memory_space=pltpu.SMEM)


def vmem_spec():
    return pl.BlockSpec(memory_space=pltpu.VMEM)


def body(queries, key_tokens, value_tokens, grad_out):
    row_width = queries.shape[1]
    tok_count = queries.shape[0]
    devices = lax.axis_size("seq")
    blocks_dev, rim, near_list, far_list, far_shifts = plan(tok_count, devices)
    if not relay_ok(devices, blocks_dev, rim, far_shifts):
        return legacy_body(queries, key_tokens, value_tokens, grad_out)
    heads = row_width // HD
    offsets = near_list + far_list
    logit_scale = 1.0 / math.sqrt(HD)
    span_blocks = (rim + 1) * blocks_dev
    lead = rim * blocks_dev
    position = lax.axis_index("seq")
    odd = (position % 2) == 1
    pairs = swap_pairs(devices)
    keys_values = jnp.concatenate([key_tokens, value_tokens], axis=1)
    queries_grads = jnp.concatenate([queries, grad_out], axis=1)
    back2 = passed_along(keys_values, "seq", 2)
    ahead2 = passed_along(queries_grads, "seq", -2)
    swap_one = lax.ppermute(jnp.where(odd, queries_grads, keys_values), "seq", pairs)
    back4 = passed_along(back2, "seq", 2)
    ahead4 = passed_along(ahead2, "seq", -2)
    swap_two = lax.ppermute(jnp.where(odd, back2, ahead2), "seq", pairs)
    far_back = [back4] + [passed_along(keys_values, "seq", shift) for shift in far_shifts[1:]]
    far_ahead = [ahead4] + [passed_along(queries_grads, "seq", -shift) for shift in far_shifts[1:]]
    far_back = far_back[: len(far_shifts)]
    far_ahead = far_ahead[: len(far_shifts)]

    position_arr = jnp.reshape(position, (1,)).astype(jnp.int32)
    far_offsets = list(far_list)
    slab_rows = (len(near_list) + len(far_list)) * BLK
    row_inputs = (position_arr, queries, grad_out, back2, swap_one, swap_two, keys_values, *far_back)
    attended, stats, stats_rows = pl.pallas_call(
        functools.partial(row_kernel, len(near_list), far_offsets, heads, "stats"),
        out_shape=(
            jax.ShapeDtypeStruct((tok_count, row_width), jnp.bfloat16),
            jax.ShapeDtypeStruct((tok_count, 2 * heads), jnp.float32),
            jax.ShapeDtypeStruct((2 * heads, tok_count), jnp.float32),
        ),
        in_specs=[smem_spec()] + [vmem_spec()] * (6 + len(far_back)),
        out_specs=(vmem_spec(), vmem_spec(), vmem_spec()),
        cost_estimate=estimate(tok_count, row_width, slab_rows, 2, 1),
        name="rows_stats",
    )(*row_inputs)
    stats_one = passed_along(stats_rows, "seq", -1)
    stats_two = passed_along(stats_rows, "seq", -2)
    far_stats = [passed_along(stats_rows, "seq", -shift) for shift in far_shifts]
    grad_queries = pl.pallas_call(
        functools.partial(row_kernel, len(near_list), far_offsets, heads, "grad"),
        out_shape=jax.ShapeDtypeStruct((tok_count, row_width), jnp.bfloat16),
        in_specs=[smem_spec()] + [vmem_spec()] * (7 + len(far_back)),
        out_specs=vmem_spec(),
        cost_estimate=estimate(tok_count, row_width, slab_rows, 3, 1),
        name="rows_grad",
    )(*row_inputs, stats)
    grad_keys, grad_values = pl.pallas_call(
        functools.partial(key_kernel, len(near_list), far_offsets, heads, devices * blocks_dev),
        out_shape=(
            jax.ShapeDtypeStruct((tok_count, row_width), jnp.bfloat16),
            jax.ShapeDtypeStruct((tok_count, row_width), jnp.bfloat16),
        ),
        in_specs=[smem_spec()] + [vmem_spec()] * (8 + 2 * len(far_ahead)),
        out_specs=(vmem_spec(), vmem_spec()),
        cost_estimate=estimate(tok_count, row_width, slab_rows, 4, 1),
        name="keys_pass",
    )(
        position_arr,
        keys_values,
        queries_grads,
        swap_two,
        swap_one,
        ahead2,
        stats_rows,
        stats_one,
        stats_two,
        *far_ahead,
        *far_stats,
    )
    return attended, grad_queries, grad_keys, grad_values


def solution(mesh):
    placed = (
        P(("rep", "seq"), None),
        P(("rep", "seq"), None),
        P(("rep", "seq"), None),
        P(("rep", "seq"), None),
    )
    return jax.shard_map(
        body,
        mesh=mesh,
        in_specs=placed,
        out_specs=(
            P(("rep", "seq"), None),
            P(("rep", "seq"), None),
            P(("rep", "seq"), None),
            P(("rep", "seq"), None),
        ),
        check_vma=False,
    )
```

```python
import functools
import math

import jax
import jax.numpy as jnp
from jax import lax
from jax.experimental import pallas as pl
from jax.experimental.pallas import tpu as pltpu
from jax.sharding import PartitionSpec as P

HEADS = 4
HD = 128
BLK = 128
WINDOW = 4


NEG = -1e30
CHUNKS = 2


def passed_along(value, axis, steps):
    count = lax.axis_size(axis)
    first, last = (max(0, -steps), min(count, count - steps))
    return lax.ppermute(value, axis, [(source, source + steps) for source in range(first, last)])


def offset_lists(block_total):
    near_list = list(range(WINDOW + 1))
    far_list = []
    stride = 1
    while stride < block_total:
        if stride > WINDOW:
            far_list.append(stride)
        stride = stride * 2
    return (near_list, far_list)


def allowed_mask(first_block, blocks_dev, offsets):
    block_ids = first_block + jnp.arange(blocks_dev, dtype=jnp.int32)
    offset_arr = jnp.array(offsets, dtype=jnp.int32)
    block_live = block_ids[:, None] - offset_arr[None, :] >= 0
    row_ids = jnp.arange(BLK, dtype=jnp.int32)
    causal = row_ids[:, None] >= row_ids[None, :]
    later_slab = offset_arr > 0
    slab_causal = jnp.logical_or(later_slab[None, :, None], causal[:, None, :])
    allowed = jnp.logical_and(block_live[:, None, :, None], slab_causal[None, :, :, :])
    return allowed.reshape(blocks_dev, BLK, len(offsets) * BLK)


def head_cols(array_in, col_start):
    return array_in[..., col_start : col_start + HD]


def to_blocks(array_in, block_count):
    return array_in.reshape(block_count, BLK, array_in.shape[-1])


def place_slabs(gradient, near_list, lead, span_blocks):
    blocks_dev = gradient.shape[0]
    placed = []
    for slot_index, offset in enumerate(near_list):
        before = lead - offset
        after = span_blocks - before - blocks_dev
        placed.append(jnp.pad(gradient[:, slot_index], ((before, after), (0, 0), (0, 0))))
    total = placed[0]
    for item in placed[1:]:
        total = total + item
    return total


def head_pass(query_per_head, output_gradient_heads, key_slabs, value_slabs, allowed, logit_scale):
    block_count = key_slabs.shape[0]
    key_row_block = key_slabs.reshape(block_count, -1, HD)
    value_row_block = value_slabs.reshape(block_count, -1, HD)
    score_matrix = (
        jnp.einsum(
            "nmv,njv->nmj", query_per_head, key_row_block, preferred_element_type=jnp.float32
        )
        * logit_scale
    )
    score_matrix = jnp.where(allowed, score_matrix, NEG)
    row_max = jnp.max(score_matrix, axis=-1, keepdims=True)
    log_total = row_max + jnp.log(jnp.sum(jnp.exp(score_matrix - row_max), axis=-1, keepdims=True))
    probabilities = jnp.exp(score_matrix - log_total)
    attention_weight = probabilities.astype(jnp.bfloat16)
    attended_per_head = jnp.einsum(
        "jym,jmo->jyo", attention_weight, value_row_block, preferred_element_type=jnp.float32
    ).astype(jnp.bfloat16)
    out_dot = jnp.sum(
        output_gradient_heads.astype(jnp.float32) * attended_per_head.astype(jnp.float32),
        axis=-1,
        keepdims=True,
    )
    probability_gradient = jnp.einsum(
        "nmv,njv->nmj", output_gradient_heads, value_row_block, preferred_element_type=jnp.float32
    )
    score_gradient = (probabilities * (probability_gradient - out_dot)).astype(jnp.bfloat16)
    query_gradient_heads = (
        jnp.einsum(
            "jym,jmo->jyo", score_gradient, key_row_block, preferred_element_type=jnp.float32
        )
        * logit_scale
    ).astype(jnp.bfloat16)
    key_gradient = (
        jnp.einsum(
            "uwj,uwn->ujn", score_gradient, query_per_head, preferred_element_type=jnp.float32
        )
        * logit_scale
    )
    value_gradient = jnp.einsum(
        "uwj,uwn->ujn", attention_weight, output_gradient_heads, preferred_element_type=jnp.float32
    )
    return (
        attended_per_head,
        query_gradient_heads,
        key_gradient,
        value_gradient,
        log_total[..., 0],
        out_dot[..., 0],
    )


def legacy_body(queries, key_tokens, value_tokens, grad_out):
    row_width = queries.shape[1]
    tok_count = queries.shape[0]
    blocks_dev = tok_count // BLK
    rim = (WINDOW + blocks_dev - 1) // blocks_dev
    devices = lax.axis_size("seq")
    near_list, far_list = offset_lists(devices * blocks_dev)
    offsets = near_list + far_list
    near_count = len(near_list)
    logit_scale = 1.0 / math.sqrt(HD)
    span_blocks = (rim + 1) * blocks_dev
    lead = rim * blocks_dev
    earlier_keys = []
    earlier_values = []
    for back in range(rim, 0, -1):
        got_keys, got_values = passed_along((key_tokens, value_tokens), "seq", back)
        earlier_keys.append(got_keys)
        earlier_values.append(got_values)
    span_keys = to_blocks(jnp.concatenate(earlier_keys + [key_tokens], axis=0), span_blocks)
    span_values = to_blocks(jnp.concatenate(earlier_values + [value_tokens], axis=0), span_blocks)
    far_keys = []
    far_values = []
    for stride in far_list:
        got_keys, got_values = passed_along((key_tokens, value_tokens), "seq", stride // blocks_dev)
        far_keys.append(to_blocks(got_keys, blocks_dev))
        far_values.append(to_blocks(got_values, blocks_dev))
    position = lax.axis_index("seq")
    allowed = allowed_mask(position * blocks_dev, blocks_dev, offsets)
    query_blocks = to_blocks(queries, blocks_dev)
    grad_blocks = to_blocks(grad_out, blocks_dev)
    attended_heads = []
    grad_query_heads = []
    near_key_heads = []
    near_value_heads = []
    total_heads = []
    dot_heads = []
    far_key_parts = [[] for stride in far_list]
    far_value_parts = [[] for stride in far_list]
    for head_index in range(HEADS):
        col_start = head_index * HD
        key_slabs = jnp.stack(
            [
                head_cols(span_keys[lead - offset : lead + blocks_dev - offset], col_start)
                for offset in near_list
            ]
            + [head_cols(item, col_start) for item in far_keys],
            axis=1,
        )
        value_slabs = jnp.stack(
            [
                head_cols(span_values[lead - offset : lead + blocks_dev - offset], col_start)
                for offset in near_list
            ]
            + [head_cols(item, col_start) for item in far_values],
            axis=1,
        )
        (
            attended_per_head,
            query_gradient_heads,
            key_gradient,
            value_gradient,
            log_total,
            out_dot,
        ) = head_pass(
            head_cols(query_blocks, col_start),
            head_cols(grad_blocks, col_start),
            key_slabs,
            value_slabs,
            allowed,
            logit_scale,
        )
        key_gradient = key_gradient.reshape(blocks_dev, -1, BLK, HD)
        value_gradient = value_gradient.reshape(blocks_dev, -1, BLK, HD)
        near_key_heads.append(place_slabs(key_gradient, near_list, lead, span_blocks))
        near_value_heads.append(place_slabs(value_gradient, near_list, lead, span_blocks))
        for level_index in range(len(far_list)):
            far_key_parts[level_index].append(
                key_gradient[:, near_count + level_index].astype(jnp.bfloat16)
            )
            far_value_parts[level_index].append(
                value_gradient[:, near_count + level_index].astype(jnp.bfloat16)
            )
        attended_heads.append(attended_per_head)
        grad_query_heads.append(query_gradient_heads)
        total_heads.append(log_total)
        dot_heads.append(out_dot)
    attended = jnp.concatenate(attended_heads, axis=-1).reshape(tok_count, row_width)
    grad_queries = jnp.concatenate(grad_query_heads, axis=-1).reshape(tok_count, row_width)
    near_keys = jnp.concatenate(near_key_heads, axis=-1).reshape((rim + 1) * tok_count, row_width)
    near_values = jnp.concatenate(near_value_heads, axis=-1).reshape(
        (rim + 1) * tok_count, row_width
    )
    total_keys = near_keys[lead * BLK :].astype(jnp.bfloat16).astype(jnp.float32)
    total_values = near_values[lead * BLK :].astype(jnp.bfloat16).astype(jnp.float32)
    for back in range(1, rim + 1):
        piece_start = (rim - back) * tok_count
        part_keys = near_keys[piece_start : piece_start + tok_count].astype(jnp.bfloat16)
        part_values = near_values[piece_start : piece_start + tok_count].astype(jnp.bfloat16)
        back_keys, back_values = passed_along((part_keys, part_values), "seq", -back)
        total_keys = total_keys + back_keys.astype(jnp.float32)
        total_values = total_values + back_values.astype(jnp.float32)
    for level_index, stride in enumerate(far_list):
        part_keys = jnp.concatenate(far_key_parts[level_index], axis=-1).reshape(
            tok_count, row_width
        )
        part_values = jnp.concatenate(far_value_parts[level_index], axis=-1).reshape(
            tok_count, row_width
        )
        got_keys, got_values = passed_along(
            (part_keys, part_values), "seq", -(stride // blocks_dev)
        )
        total_keys = total_keys + got_keys.astype(jnp.float32)
        total_values = total_values + got_values.astype(jnp.float32)
    return (
        attended,
        grad_queries,
        total_keys.astype(jnp.bfloat16),
        total_values.astype(jnp.bfloat16),
    )


def swap_pairs(count):
    return [(source, source ^ 1) for source in range(count) if source ^ 1 < count]


def relay_ok(count, blocks_dev, rim, far_shifts):
    return count % 2 == 0 and blocks_dev == 2 and rim == 2 and (not far_shifts or far_shifts[0] == 4)


def plan(tok_count, devices):
    blocks_dev = tok_count // BLK
    rim = (WINDOW + blocks_dev - 1) // blocks_dev
    near_list, far_list = offset_lists(devices * blocks_dev)
    far_shifts = [stride // blocks_dev for stride in far_list]
    return blocks_dev, rim, near_list, far_list, far_shifts


def row_pass(query_per_head, output_gradient_heads, key_slabs, value_slabs, allowed, logit_scale):
    block_count = key_slabs.shape[0]
    key_row_block = key_slabs.reshape(block_count, -1, HD)
    value_row_block = value_slabs.reshape(block_count, -1, HD)
    score_matrix = (
        jnp.einsum(
            "nmv,njv->nmj", query_per_head, key_row_block, preferred_element_type=jnp.float32
        )
        * logit_scale
    )
    score_matrix = jnp.where(allowed, score_matrix, NEG)
    row_max = jnp.max(score_matrix, axis=-1, keepdims=True)
    log_total = row_max + jnp.log(jnp.sum(jnp.exp(score_matrix - row_max), axis=-1, keepdims=True))
    probabilities = jnp.exp(score_matrix - log_total)
    attention_weight = probabilities.astype(jnp.bfloat16)
    attended_per_head = jnp.einsum(
        "jym,jmo->jyo", attention_weight, value_row_block, preferred_element_type=jnp.float32
    ).astype(jnp.bfloat16)
    out_dot = jnp.sum(
        output_gradient_heads.astype(jnp.float32) * attended_per_head.astype(jnp.float32),
        axis=-1,
        keepdims=True,
    )
    probability_gradient = jnp.einsum(
        "nmv,njv->nmj", output_gradient_heads, value_row_block, preferred_element_type=jnp.float32
    )
    score_gradient = (probabilities * (probability_gradient - out_dot)).astype(jnp.bfloat16)
    query_gradient_heads = (
        jnp.einsum(
            "jym,jmo->jyo", score_gradient, key_row_block, preferred_element_type=jnp.float32
        )
        * logit_scale
    ).astype(jnp.bfloat16)
    return attended_per_head, query_gradient_heads, log_total[..., 0], out_dot[..., 0]


def key_pass(key_per_head, value_per_head, query_slabs, grad_slabs, total_slabs, dot_slabs, allowed, logit_scale):
    block_count = query_slabs.shape[0]
    query_rows = query_slabs.reshape(block_count, -1, HD)
    grad_rows = grad_slabs.reshape(block_count, -1, HD)
    score_matrix = (
        jnp.einsum("nmv,njv->nmj", query_rows, key_per_head, preferred_element_type=jnp.float32)
        * logit_scale
    )
    total_rows = total_slabs.reshape(block_count, -1, 1)
    dot_rows = dot_slabs.reshape(block_count, -1, 1)
    probabilities = jnp.where(allowed, jnp.exp(score_matrix - total_rows), 0.0)
    probability_gradient = jnp.einsum(
        "nmv,njv->nmj", grad_rows, value_per_head, preferred_element_type=jnp.float32
    )
    score_gradient = (probabilities * (probability_gradient - dot_rows)).astype(jnp.bfloat16)
    attention_weight = probabilities.astype(jnp.bfloat16)
    key_gradient = (
        jnp.einsum("nmj,nmv->njv", score_gradient, query_rows, preferred_element_type=jnp.float32)
        * logit_scale
    )
    value_gradient = jnp.einsum(
        "nmj,nmv->njv", attention_weight, grad_rows, preferred_element_type=jnp.float32
    )
    return key_gradient, value_gradient


def key_allowed(first_block, blocks_dev, offsets, block_total):
    block_ids = first_block + jnp.arange(blocks_dev, dtype=jnp.int32)
    offset_arr = jnp.array(offsets, dtype=jnp.int32)
    query_live = block_ids[:, None] + offset_arr[None, :] < block_total
    row_ids = jnp.arange(BLK, dtype=jnp.int32)
    causal = row_ids[:, None] >= row_ids[None, :]
    later_slab = offset_arr > 0
    slab_causal = jnp.logical_or(later_slab[:, None, None], causal[None, :, :])
    allowed = jnp.logical_and(query_live[:, :, None, None], slab_causal[None, :, :, :])
    return allowed.reshape(blocks_dev, len(offsets) * BLK, BLK)


TRANS_B = (((1,), (1,)), ((), ()))


def span_load(refs, start, length, other, axis):
    size = refs[0].shape[axis]
    pieces = []
    at = start
    while length > 0:
        index, offset = at // size, at % size
        count = min(size - offset, length)
        window = pl.ds(offset, count)
        pieces.append(refs[index][window, other] if axis == 0 else refs[index][other, window])
        at += count
        length -= count
    return pieces[0] if len(pieces) == 1 else jnp.concatenate(pieces, axis=axis)


def row_kernel(near_count, far_list, heads, phase, *refs):
    far_count = len(far_list)
    position_ref, query_ref, grad_ref = refs[:3]
    span_refs = refs[3:6]
    far_refs = refs[6 : 6 + far_count]
    if phase == "stats":
        attended_ref, stats_ref, stats_rows_ref = refs[6 + far_count :]
    else:
        stats_in_ref, grad_query_ref = refs[6 + far_count :]
    width = heads * HD
    near_rows = near_count * BLK
    scale = 1.0 / math.sqrt(HD)
    first = 2 * position_ref[0]
    near_row_ids = lax.broadcasted_iota(jnp.int32, (BLK, near_rows), 0)
    near_col_ids = lax.broadcasted_iota(jnp.int32, (BLK, near_rows), 1)
    near_offset = (near_count - 1) - near_col_ids // BLK
    near_causal = jnp.logical_or(near_offset > 0, near_row_ids >= near_col_ids % BLK)
    lane_ids = lax.broadcasted_iota(jnp.int32, (BLK, 2 * heads), 1)
    for block in range(2):
        rows = pl.ds(block * BLK, BLK)
        near_span = pl.ds(block * BLK, near_rows)
        near_mask = jnp.logical_and(near_causal, first + block - near_offset >= 0)
        far_live = [first + block - offset >= 0 for offset in far_list]
        masks = [near_mask] + far_live
        if phase == "stats":
            stats_tile = jnp.zeros((BLK, 2 * heads), jnp.float32)
        else:
            stats_tile = stats_in_ref[rows, :]
        for head in range(heads):
            cols = pl.ds(head * HD, HD)
            value_cols = pl.ds(width + head * HD, HD)
            query = query_ref[rows, cols]
            grad = grad_ref[rows, cols]
            keys = [span_load(span_refs, block * BLK, near_rows, cols, 0)]
            keys = keys + [item[rows, cols] for item in far_refs]
            values = [span_load(span_refs, block * BLK, near_rows, value_cols, 0)]
            values = values + [item[rows, value_cols] for item in far_refs]
            scores = [
                lax.dot_general(query, key, TRANS_B, preferred_element_type=jnp.float32) * scale
                for key in keys
            ]
            if phase == "grad":
                log_total = jnp.sum(jnp.where(lane_ids == head, stats_tile, 0.0), axis=-1, keepdims=True)
                out_dot = jnp.sum(
                    jnp.where(lane_ids == heads + head, stats_tile, 0.0), axis=-1, keepdims=True
                )
                probs = [
                    jnp.where(mask, jnp.exp(score - log_total), 0.0)
                    for score, mask in zip(scores, masks)
                ]
                grad_query = jnp.zeros((BLK, HD), jnp.float32)
                for prob, key, value in zip(probs, keys, values):
                    prob_grad = lax.dot_general(
                        grad, value, TRANS_B, preferred_element_type=jnp.float32
                    )
                    score_grad = (prob * (prob_grad - out_dot)).astype(jnp.bfloat16)
                    grad_query = grad_query + jnp.dot(
                        score_grad, key, preferred_element_type=jnp.float32
                    )
                grad_query_ref[rows, cols] = (grad_query * scale).astype(jnp.bfloat16)
                continue
            scores = [jnp.where(mask, score, NEG) for score, mask in zip(scores, masks)]
            row_max = scores[0].max(axis=-1, keepdims=True)
            for score in scores[1:]:
                row_max = jnp.maximum(row_max, score.max(axis=-1, keepdims=True))
            shifted = [jnp.exp(score - row_max) for score in scores]
            row_sum = shifted[0].sum(axis=-1, keepdims=True)
            for item in shifted[1:]:
                row_sum = row_sum + item.sum(axis=-1, keepdims=True)
            log_total = row_max + jnp.log(row_sum)
            inverse = 1.0 / row_sum
            attended = jnp.zeros((BLK, HD), jnp.float32)
            for item, value in zip(shifted, values):
                attended = attended + jnp.dot(
                    (item * inverse).astype(jnp.bfloat16), value, preferred_element_type=jnp.float32
                )
            attended = attended.astype(jnp.bfloat16)
            attended_ref[rows, cols] = attended
            out_dot = jnp.sum(
                grad.astype(jnp.float32) * attended.astype(jnp.float32), axis=-1, keepdims=True
            )
            stats_tile = stats_tile + jnp.where(lane_ids == head, log_total, 0.0)
            stats_tile = stats_tile + jnp.where(lane_ids == heads + head, out_dot, 0.0)
        if phase == "stats":
            stats_ref[rows, :] = stats_tile
            wide_lanes = lax.broadcasted_iota(jnp.int32, (BLK, BLK), 1)
            wide = jnp.zeros((BLK, BLK), jnp.float32)
            for lane in range(2 * heads):
                column = jnp.sum(jnp.where(lane_ids == lane, stats_tile, 0.0), axis=-1, keepdims=True)
                wide = wide + jnp.where(wide_lanes == lane, column, 0.0)
            stats_rows_ref[:, rows] = wide.T[: 2 * heads, :]


def estimate(tok_count, row_width, slab_rows, matmuls, exps):
    flops = 2 * tok_count * slab_rows * HD * matmuls * (row_width // HD)
    return pl.CostEstimate(
        flops=flops,
        transcendentals=tok_count * slab_rows * exps * (row_width // HD),
        bytes_accessed=8 * tok_count * row_width * 4,
    )


def key_kernel(near_count, far_list, heads, block_total, *refs):
    far_count = len(far_list)
    position_ref, own_ref = refs[:2]
    span_refs = refs[2:5]
    stats_refs = refs[5:8]
    far_rows = refs[8 : 8 + far_count]
    far_stats = refs[8 + far_count : 8 + 2 * far_count]
    grad_key_ref, grad_value_ref = refs[8 + 2 * far_count :]
    width = heads * HD
    near_rows = near_count * BLK
    scale = 1.0 / math.sqrt(HD)
    first = 2 * position_ref[0]
    near_key_ids = lax.broadcasted_iota(jnp.int32, (BLK, near_rows), 0)
    near_query_ids = lax.broadcasted_iota(jnp.int32, (BLK, near_rows), 1)
    near_offset = near_query_ids // BLK
    near_causal = jnp.logical_or(near_offset > 0, near_query_ids % BLK >= near_key_ids)
    for block in range(2):
        rows = pl.ds(block * BLK, BLK)
        near_span = pl.ds(block * BLK, near_rows)
        near_mask = jnp.logical_and(near_causal, first + block + near_offset < block_total)
        far_live = [first + block + offset < block_total for offset in far_list]
        masks = [near_mask] + far_live
        for head in range(heads):
            cols = pl.ds(head * HD, HD)
            value_cols = pl.ds(width + head * HD, HD)
            key = own_ref[rows, cols]
            value = own_ref[rows, value_cols]
            queries = [span_load(span_refs, block * BLK, near_rows, cols, 0)]
            queries = queries + [item[rows, cols] for item in far_rows]
            grads = [span_load(span_refs, block * BLK, near_rows, value_cols, 0)]
            grads = grads + [item[rows, value_cols] for item in far_rows]
            totals = [span_load(stats_refs, block * BLK, near_rows, pl.ds(head, 1), 1)] + [
                item[pl.ds(head, 1), rows] for item in far_stats
            ]
            dots = [span_load(stats_refs, block * BLK, near_rows, pl.ds(heads + head, 1), 1)] + [
                item[pl.ds(heads + head, 1), rows] for item in far_stats
            ]
            grad_key = jnp.zeros((BLK, HD), jnp.float32)
            grad_value = jnp.zeros((BLK, HD), jnp.float32)
            for query, grad, log_total, out_dot, mask in zip(queries, grads, totals, dots, masks):
                score = lax.dot_general(key, query, TRANS_B, preferred_element_type=jnp.float32)
                prob = jnp.where(mask, jnp.exp(score * scale - log_total), 0.0)
                prob_grad = lax.dot_general(value, grad, TRANS_B, preferred_element_type=jnp.float32)
                score_grad = (prob * (prob_grad - out_dot)).astype(jnp.bfloat16)
                grad_value = grad_value + jnp.dot(
                    prob.astype(jnp.bfloat16), grad, preferred_element_type=jnp.float32
                )
                grad_key = grad_key + jnp.dot(score_grad, query, preferred_element_type=jnp.float32)
            grad_key_ref[rows, cols] = (grad_key * scale).astype(jnp.bfloat16)
            grad_value_ref[rows, cols] = grad_value.astype(jnp.bfloat16)


def smem_spec():
    return pl.BlockSpec(memory_space=pltpu.SMEM)


def vmem_spec():
    return pl.BlockSpec(memory_space=pltpu.VMEM)


def body(queries, key_tokens, value_tokens, grad_out):
    row_width = queries.shape[1]
    tok_count = queries.shape[0]
    devices = lax.axis_size("seq")
    blocks_dev, rim, near_list, far_list, far_shifts = plan(tok_count, devices)
    if not relay_ok(devices, blocks_dev, rim, far_shifts):
        return legacy_body(queries, key_tokens, value_tokens, grad_out)
    heads = row_width // HD
    offsets = near_list + far_list
    logit_scale = 1.0 / math.sqrt(HD)
    span_blocks = (rim + 1) * blocks_dev
    lead = rim * blocks_dev
    position = lax.axis_index("seq")
    odd = (position % 2) == 1
    pairs = swap_pairs(devices)
    keys_values = jnp.concatenate([key_tokens, value_tokens], axis=1)
    queries_grads = jnp.concatenate([queries, grad_out], axis=1)
    back2 = passed_along(keys_values, "seq", 2)
    ahead2 = passed_along(queries_grads, "seq", -2)
    swap_one = lax.ppermute(jnp.where(odd, queries_grads, keys_values), "seq", pairs)
    back4 = passed_along(back2, "seq", 2)
    from_right = [(source, source - 1) for source in range(1, devices, 2)]
    back_side = lax.ppermute(back2, "seq", from_right)
    ahead4 = passed_along(ahead2, "seq", -2)
    from_left = [(source, source + 1) for source in range(0, devices - 1, 2)]
    ahead_side = lax.ppermute(ahead2, "seq", from_left)
    back1 = jnp.where(odd, swap_one, back_side)
    ahead1 = jnp.where(odd, ahead_side, swap_one)
    far_back = [back4] + [passed_along(keys_values, "seq", shift) for shift in far_shifts[1:]]
    far_ahead = [ahead4] + [passed_along(queries_grads, "seq", -shift) for shift in far_shifts[1:]]
    far_back = far_back[: len(far_shifts)]
    far_ahead = far_ahead[: len(far_shifts)]

    position_arr = jnp.reshape(position, (1,)).astype(jnp.int32)
    far_offsets = list(far_list)
    slab_rows = (len(near_list) + len(far_list)) * BLK
    row_inputs = (position_arr, queries, grad_out, back2, back1, keys_values, *far_back)
    attended, stats, stats_rows = pl.pallas_call(
        functools.partial(row_kernel, len(near_list), far_offsets, heads, "stats"),
        out_shape=(
            jax.ShapeDtypeStruct((tok_count, row_width), jnp.bfloat16),
            jax.ShapeDtypeStruct((tok_count, 2 * heads), jnp.float32),
            jax.ShapeDtypeStruct((2 * heads, tok_count), jnp.float32),
        ),
        in_specs=[smem_spec()] + [vmem_spec()] * (5 + len(far_back)),
        out_specs=(vmem_spec(), vmem_spec(), vmem_spec()),
        cost_estimate=estimate(tok_count, row_width, slab_rows, 2, 1),
        name="rows_stats",
    )(*row_inputs)
    stats_one = passed_along(stats_rows, "seq", -1)
    stats_two = passed_along(stats_rows, "seq", -2)
    far_stats = [passed_along(stats_rows, "seq", -shift) for shift in far_shifts]
    grad_queries = pl.pallas_call(
        functools.partial(row_kernel, len(near_list), far_offsets, heads, "grad"),
        out_shape=jax.ShapeDtypeStruct((tok_count, row_width), jnp.bfloat16),
        in_specs=[smem_spec()] + [vmem_spec()] * (6 + len(far_back)),
        out_specs=vmem_spec(),
        cost_estimate=estimate(tok_count, row_width, slab_rows, 3, 1),
        name="rows_grad",
    )(*row_inputs, stats)
    grad_keys, grad_values = pl.pallas_call(
        functools.partial(key_kernel, len(near_list), far_offsets, heads, devices * blocks_dev),
        out_shape=(
            jax.ShapeDtypeStruct((tok_count, row_width), jnp.bfloat16),
            jax.ShapeDtypeStruct((tok_count, row_width), jnp.bfloat16),
        ),
        in_specs=[smem_spec()] + [vmem_spec()] * (7 + 2 * len(far_ahead)),
        out_specs=(vmem_spec(), vmem_spec()),
        cost_estimate=estimate(tok_count, row_width, slab_rows, 4, 1),
        name="keys_pass",
    )(
        position_arr,
        keys_values,
        queries_grads,
        ahead1,
        ahead2,
        stats_rows,
        stats_one,
        stats_two,
        *far_ahead,
        *far_stats,
    )
    return attended, grad_queries, grad_keys, grad_values


def solution(mesh):
    placed = (
        P(("rep", "seq"), None),
        P(("rep", "seq"), None),
        P(("rep", "seq"), None),
        P(("rep", "seq"), None),
    )
    return jax.shard_map(
        body,
        mesh=mesh,
        in_specs=placed,
        out_specs=(
            P(("rep", "seq"), None),
            P(("rep", "seq"), None),
            P(("rep", "seq"), None),
            P(("rep", "seq"), None),
        ),
        check_vma=False,
    )
```

```python
import functools
import math

import jax
import jax.numpy as jnp
from jax import lax
from jax.experimental import pallas as pl
from jax.experimental.pallas import tpu as pltpu
from jax.sharding import PartitionSpec as P

HEADS = 4
HD = 128
BLK = 128
WINDOW = 4


NEG = -1e30
CHUNKS = 2


def passed_along(value, axis, steps):
    count = lax.axis_size(axis)
    first, last = (max(0, -steps), min(count, count - steps))
    return lax.ppermute(value, axis, [(source, source + steps) for source in range(first, last)])


def offset_lists(block_total):
    near_list = list(range(WINDOW + 1))
    far_list = []
    stride = 1
    while stride < block_total:
        if stride > WINDOW:
            far_list.append(stride)
        stride = stride * 2
    return (near_list, far_list)


def allowed_mask(first_block, blocks_dev, offsets):
    block_ids = first_block + jnp.arange(blocks_dev, dtype=jnp.int32)
    offset_arr = jnp.array(offsets, dtype=jnp.int32)
    block_live = block_ids[:, None] - offset_arr[None, :] >= 0
    row_ids = jnp.arange(BLK, dtype=jnp.int32)
    causal = row_ids[:, None] >= row_ids[None, :]
    later_slab = offset_arr > 0
    slab_causal = jnp.logical_or(later_slab[None, :, None], causal[:, None, :])
    allowed = jnp.logical_and(block_live[:, None, :, None], slab_causal[None, :, :, :])
    return allowed.reshape(blocks_dev, BLK, len(offsets) * BLK)


def head_cols(array_in, col_start):
    return array_in[..., col_start : col_start + HD]


def to_blocks(array_in, block_count):
    return array_in.reshape(block_count, BLK, array_in.shape[-1])


def place_slabs(gradient, near_list, lead, span_blocks):
    blocks_dev = gradient.shape[0]
    placed = []
    for slot_index, offset in enumerate(near_list):
        before = lead - offset
        after = span_blocks - before - blocks_dev
        placed.append(jnp.pad(gradient[:, slot_index], ((before, after), (0, 0), (0, 0))))
    total = placed[0]
    for item in placed[1:]:
        total = total + item
    return total


def head_pass(query_per_head, output_gradient_heads, key_slabs, value_slabs, allowed, logit_scale):
    block_count = key_slabs.shape[0]
    key_row_block = key_slabs.reshape(block_count, -1, HD)
    value_row_block = value_slabs.reshape(block_count, -1, HD)
    score_matrix = (
        jnp.einsum(
            "nmv,njv->nmj", query_per_head, key_row_block, preferred_element_type=jnp.float32
        )
        * logit_scale
    )
    score_matrix = jnp.where(allowed, score_matrix, NEG)
    row_max = jnp.max(score_matrix, axis=-1, keepdims=True)
    log_total = row_max + jnp.log(jnp.sum(jnp.exp(score_matrix - row_max), axis=-1, keepdims=True))
    probabilities = jnp.exp(score_matrix - log_total)
    attention_weight = probabilities.astype(jnp.bfloat16)
    attended_per_head = jnp.einsum(
        "jym,jmo->jyo", attention_weight, value_row_block, preferred_element_type=jnp.float32
    ).astype(jnp.bfloat16)
    out_dot = jnp.sum(
        output_gradient_heads.astype(jnp.float32) * attended_per_head.astype(jnp.float32),
        axis=-1,
        keepdims=True,
    )
    probability_gradient = jnp.einsum(
        "nmv,njv->nmj", output_gradient_heads, value_row_block, preferred_element_type=jnp.float32
    )
    score_gradient = (probabilities * (probability_gradient - out_dot)).astype(jnp.bfloat16)
    query_gradient_heads = (
        jnp.einsum(
            "jym,jmo->jyo", score_gradient, key_row_block, preferred_element_type=jnp.float32
        )
        * logit_scale
    ).astype(jnp.bfloat16)
    key_gradient = (
        jnp.einsum(
            "uwj,uwn->ujn", score_gradient, query_per_head, preferred_element_type=jnp.float32
        )
        * logit_scale
    )
    value_gradient = jnp.einsum(
        "uwj,uwn->ujn", attention_weight, output_gradient_heads, preferred_element_type=jnp.float32
    )
    return (
        attended_per_head,
        query_gradient_heads,
        key_gradient,
        value_gradient,
        log_total[..., 0],
        out_dot[..., 0],
    )


def legacy_body(queries, key_tokens, value_tokens, grad_out):
    row_width = queries.shape[1]
    tok_count = queries.shape[0]
    blocks_dev = tok_count // BLK
    rim = (WINDOW + blocks_dev - 1) // blocks_dev
    devices = lax.axis_size("seq")
    near_list, far_list = offset_lists(devices * blocks_dev)
    offsets = near_list + far_list
    near_count = len(near_list)
    logit_scale = 1.0 / math.sqrt(HD)
    span_blocks = (rim + 1) * blocks_dev
    lead = rim * blocks_dev
    earlier_keys = []
    earlier_values = []
    for back in range(rim, 0, -1):
        got_keys, got_values = passed_along((key_tokens, value_tokens), "seq", back)
        earlier_keys.append(got_keys)
        earlier_values.append(got_values)
    span_keys = to_blocks(jnp.concatenate(earlier_keys + [key_tokens], axis=0), span_blocks)
    span_values = to_blocks(jnp.concatenate(earlier_values + [value_tokens], axis=0), span_blocks)
    far_keys = []
    far_values = []
    for stride in far_list:
        got_keys, got_values = passed_along((key_tokens, value_tokens), "seq", stride // blocks_dev)
        far_keys.append(to_blocks(got_keys, blocks_dev))
        far_values.append(to_blocks(got_values, blocks_dev))
    position = lax.axis_index("seq")
    allowed = allowed_mask(position * blocks_dev, blocks_dev, offsets)
    query_blocks = to_blocks(queries, blocks_dev)
    grad_blocks = to_blocks(grad_out, blocks_dev)
    attended_heads = []
    grad_query_heads = []
    near_key_heads = []
    near_value_heads = []
    total_heads = []
    dot_heads = []
    far_key_parts = [[] for stride in far_list]
    far_value_parts = [[] for stride in far_list]
    for head_index in range(HEADS):
        col_start = head_index * HD
        key_slabs = jnp.stack(
            [
                head_cols(span_keys[lead - offset : lead + blocks_dev - offset], col_start)
                for offset in near_list
            ]
            + [head_cols(item, col_start) for item in far_keys],
            axis=1,
        )
        value_slabs = jnp.stack(
            [
                head_cols(span_values[lead - offset : lead + blocks_dev - offset], col_start)
                for offset in near_list
            ]
            + [head_cols(item, col_start) for item in far_values],
            axis=1,
        )
        (
            attended_per_head,
            query_gradient_heads,
            key_gradient,
            value_gradient,
            log_total,
            out_dot,
        ) = head_pass(
            head_cols(query_blocks, col_start),
            head_cols(grad_blocks, col_start),
            key_slabs,
            value_slabs,
            allowed,
            logit_scale,
        )
        key_gradient = key_gradient.reshape(blocks_dev, -1, BLK, HD)
        value_gradient = value_gradient.reshape(blocks_dev, -1, BLK, HD)
        near_key_heads.append(place_slabs(key_gradient, near_list, lead, span_blocks))
        near_value_heads.append(place_slabs(value_gradient, near_list, lead, span_blocks))
        for level_index in range(len(far_list)):
            far_key_parts[level_index].append(
                key_gradient[:, near_count + level_index].astype(jnp.bfloat16)
            )
            far_value_parts[level_index].append(
                value_gradient[:, near_count + level_index].astype(jnp.bfloat16)
            )
        attended_heads.append(attended_per_head)
        grad_query_heads.append(query_gradient_heads)
        total_heads.append(log_total)
        dot_heads.append(out_dot)
    attended = jnp.concatenate(attended_heads, axis=-1).reshape(tok_count, row_width)
    grad_queries = jnp.concatenate(grad_query_heads, axis=-1).reshape(tok_count, row_width)
    near_keys = jnp.concatenate(near_key_heads, axis=-1).reshape((rim + 1) * tok_count, row_width)
    near_values = jnp.concatenate(near_value_heads, axis=-1).reshape(
        (rim + 1) * tok_count, row_width
    )
    total_keys = near_keys[lead * BLK :].astype(jnp.bfloat16).astype(jnp.float32)
    total_values = near_values[lead * BLK :].astype(jnp.bfloat16).astype(jnp.float32)
    for back in range(1, rim + 1):
        piece_start = (rim - back) * tok_count
        part_keys = near_keys[piece_start : piece_start + tok_count].astype(jnp.bfloat16)
        part_values = near_values[piece_start : piece_start + tok_count].astype(jnp.bfloat16)
        back_keys, back_values = passed_along((part_keys, part_values), "seq", -back)
        total_keys = total_keys + back_keys.astype(jnp.float32)
        total_values = total_values + back_values.astype(jnp.float32)
    for level_index, stride in enumerate(far_list):
        part_keys = jnp.concatenate(far_key_parts[level_index], axis=-1).reshape(
            tok_count, row_width
        )
        part_values = jnp.concatenate(far_value_parts[level_index], axis=-1).reshape(
            tok_count, row_width
        )
        got_keys, got_values = passed_along(
            (part_keys, part_values), "seq", -(stride // blocks_dev)
        )
        total_keys = total_keys + got_keys.astype(jnp.float32)
        total_values = total_values + got_values.astype(jnp.float32)
    return (
        attended,
        grad_queries,
        total_keys.astype(jnp.bfloat16),
        total_values.astype(jnp.bfloat16),
    )


def swap_pairs(count):
    return [(source, source ^ 1) for source in range(count) if source ^ 1 < count]


def relay_ok(count, blocks_dev, rim, far_shifts):
    return count % 2 == 0 and blocks_dev == 2 and rim == 2 and (not far_shifts or far_shifts[0] == 4)


def plan(tok_count, devices):
    blocks_dev = tok_count // BLK
    rim = (WINDOW + blocks_dev - 1) // blocks_dev
    near_list, far_list = offset_lists(devices * blocks_dev)
    far_shifts = [stride // blocks_dev for stride in far_list]
    return blocks_dev, rim, near_list, far_list, far_shifts


def row_pass(query_per_head, output_gradient_heads, key_slabs, value_slabs, allowed, logit_scale):
    block_count = key_slabs.shape[0]
    key_row_block = key_slabs.reshape(block_count, -1, HD)
    value_row_block = value_slabs.reshape(block_count, -1, HD)
    score_matrix = (
        jnp.einsum(
            "nmv,njv->nmj", query_per_head, key_row_block, preferred_element_type=jnp.float32
        )
        * logit_scale
    )
    score_matrix = jnp.where(allowed, score_matrix, NEG)
    row_max = jnp.max(score_matrix, axis=-1, keepdims=True)
    log_total = row_max + jnp.log(jnp.sum(jnp.exp(score_matrix - row_max), axis=-1, keepdims=True))
    probabilities = jnp.exp(score_matrix - log_total)
    attention_weight = probabilities.astype(jnp.bfloat16)
    attended_per_head = jnp.einsum(
        "jym,jmo->jyo", attention_weight, value_row_block, preferred_element_type=jnp.float32
    ).astype(jnp.bfloat16)
    out_dot = jnp.sum(
        output_gradient_heads.astype(jnp.float32) * attended_per_head.astype(jnp.float32),
        axis=-1,
        keepdims=True,
    )
    probability_gradient = jnp.einsum(
        "nmv,njv->nmj", output_gradient_heads, value_row_block, preferred_element_type=jnp.float32
    )
    score_gradient = (probabilities * (probability_gradient - out_dot)).astype(jnp.bfloat16)
    query_gradient_heads = (
        jnp.einsum(
            "jym,jmo->jyo", score_gradient, key_row_block, preferred_element_type=jnp.float32
        )
        * logit_scale
    ).astype(jnp.bfloat16)
    return attended_per_head, query_gradient_heads, log_total[..., 0], out_dot[..., 0]


def key_pass(key_per_head, value_per_head, query_slabs, grad_slabs, total_slabs, dot_slabs, allowed, logit_scale):
    block_count = query_slabs.shape[0]
    query_rows = query_slabs.reshape(block_count, -1, HD)
    grad_rows = grad_slabs.reshape(block_count, -1, HD)
    score_matrix = (
        jnp.einsum("nmv,njv->nmj", query_rows, key_per_head, preferred_element_type=jnp.float32)
        * logit_scale
    )
    total_rows = total_slabs.reshape(block_count, -1, 1)
    dot_rows = dot_slabs.reshape(block_count, -1, 1)
    probabilities = jnp.where(allowed, jnp.exp(score_matrix - total_rows), 0.0)
    probability_gradient = jnp.einsum(
        "nmv,njv->nmj", grad_rows, value_per_head, preferred_element_type=jnp.float32
    )
    score_gradient = (probabilities * (probability_gradient - dot_rows)).astype(jnp.bfloat16)
    attention_weight = probabilities.astype(jnp.bfloat16)
    key_gradient = (
        jnp.einsum("nmj,nmv->njv", score_gradient, query_rows, preferred_element_type=jnp.float32)
        * logit_scale
    )
    value_gradient = jnp.einsum(
        "nmj,nmv->njv", attention_weight, grad_rows, preferred_element_type=jnp.float32
    )
    return key_gradient, value_gradient


def key_allowed(first_block, blocks_dev, offsets, block_total):
    block_ids = first_block + jnp.arange(blocks_dev, dtype=jnp.int32)
    offset_arr = jnp.array(offsets, dtype=jnp.int32)
    query_live = block_ids[:, None] + offset_arr[None, :] < block_total
    row_ids = jnp.arange(BLK, dtype=jnp.int32)
    causal = row_ids[:, None] >= row_ids[None, :]
    later_slab = offset_arr > 0
    slab_causal = jnp.logical_or(later_slab[:, None, None], causal[None, :, :])
    allowed = jnp.logical_and(query_live[:, :, None, None], slab_causal[None, :, :, :])
    return allowed.reshape(blocks_dev, len(offsets) * BLK, BLK)


TRANS_B = (((1,), (1,)), ((), ()))


def span_load(refs, start, length, other, axis):
    size = refs[0].shape[axis]
    pieces = []
    at = start
    while length > 0:
        index, offset = at // size, at % size
        count = min(size - offset, length)
        window = pl.ds(offset, count)
        pieces.append(refs[index][window, other] if axis == 0 else refs[index][other, window])
        at += count
        length -= count
    return pieces[0] if len(pieces) == 1 else jnp.concatenate(pieces, axis=axis)


def row_kernel(near_count, far_list, heads, phase, *refs):
    far_count = len(far_list)
    position_ref, query_ref, grad_ref = refs[:3]
    span_refs = refs[3:6]
    far_refs = refs[6 : 6 + far_count]
    if phase == "stats":
        attended_ref, stats_ref, stats_rows_ref = refs[6 + far_count :]
    else:
        stats_in_ref, grad_query_ref = refs[6 + far_count :]
    width = heads * HD
    near_rows = near_count * BLK
    scale = 1.0 / math.sqrt(HD)
    first = 2 * position_ref[0]
    near_row_ids = lax.broadcasted_iota(jnp.int32, (BLK, near_rows), 0)
    near_col_ids = lax.broadcasted_iota(jnp.int32, (BLK, near_rows), 1)
    near_offset = (near_count - 1) - near_col_ids // BLK
    near_causal = jnp.logical_or(near_offset > 0, near_row_ids >= near_col_ids % BLK)
    lane_ids = lax.broadcasted_iota(jnp.int32, (BLK, 2 * heads), 1)
    for block in range(2):
        rows = pl.ds(block * BLK, BLK)
        near_span = pl.ds(block * BLK, near_rows)
        near_mask = jnp.logical_and(near_causal, first + block - near_offset >= 0)
        far_live = [first + block - offset >= 0 for offset in far_list]
        masks = [near_mask] + far_live
        if phase == "stats":
            stats_tile = jnp.zeros((BLK, 2 * heads), jnp.float32)
        else:
            stats_tile = stats_in_ref[rows, :]
        for head in range(heads):
            cols = pl.ds(head * HD, HD)
            value_cols = pl.ds(width + head * HD, HD)
            query = query_ref[rows, cols]
            grad = grad_ref[rows, cols]
            keys = [span_load(span_refs, block * BLK, near_rows, cols, 0)]
            keys = keys + [item[rows, cols] for item in far_refs]
            values = [span_load(span_refs, block * BLK, near_rows, value_cols, 0)]
            values = values + [item[rows, value_cols] for item in far_refs]
            scores = [
                lax.dot_general(query, key, TRANS_B, preferred_element_type=jnp.float32) * scale
                for key in keys
            ]
            if phase == "grad":
                log_total = jnp.sum(jnp.where(lane_ids == head, stats_tile, 0.0), axis=-1, keepdims=True)
                out_dot = jnp.sum(
                    jnp.where(lane_ids == heads + head, stats_tile, 0.0), axis=-1, keepdims=True
                )
                probs = [
                    jnp.where(mask, jnp.exp(score - log_total), 0.0)
                    for score, mask in zip(scores, masks)
                ]
                grad_query = jnp.zeros((BLK, HD), jnp.float32)
                for prob, key, value in zip(probs, keys, values):
                    prob_grad = lax.dot_general(
                        grad, value, TRANS_B, preferred_element_type=jnp.float32
                    )
                    score_grad = (prob * (prob_grad - out_dot)).astype(jnp.bfloat16)
                    grad_query = grad_query + jnp.dot(
                        score_grad, key, preferred_element_type=jnp.float32
                    )
                grad_query_ref[rows, cols] = (grad_query * scale).astype(jnp.bfloat16)
                continue
            scores = [jnp.where(mask, score, NEG) for score, mask in zip(scores, masks)]
            row_max = scores[0].max(axis=-1, keepdims=True)
            for score in scores[1:]:
                row_max = jnp.maximum(row_max, score.max(axis=-1, keepdims=True))
            shifted = [jnp.exp(score - row_max) for score in scores]
            row_sum = shifted[0].sum(axis=-1, keepdims=True)
            for item in shifted[1:]:
                row_sum = row_sum + item.sum(axis=-1, keepdims=True)
            log_total = row_max + jnp.log(row_sum)
            inverse = 1.0 / row_sum
            attended = jnp.zeros((BLK, HD), jnp.float32)
            for item, value in zip(shifted, values):
                attended = attended + jnp.dot(
                    (item * inverse).astype(jnp.bfloat16), value, preferred_element_type=jnp.float32
                )
            attended = attended.astype(jnp.bfloat16)
            attended_ref[rows, cols] = attended
            out_dot = jnp.sum(
                grad.astype(jnp.float32) * attended.astype(jnp.float32), axis=-1, keepdims=True
            )
            stats_tile = stats_tile + jnp.where(lane_ids == head, log_total, 0.0)
            stats_tile = stats_tile + jnp.where(lane_ids == heads + head, out_dot, 0.0)
        if phase == "stats":
            stats_ref[rows, :] = stats_tile
            wide_lanes = lax.broadcasted_iota(jnp.int32, (BLK, BLK), 1)
            wide = jnp.zeros((BLK, BLK), jnp.float32)
            for lane in range(2 * heads):
                column = jnp.sum(jnp.where(lane_ids == lane, stats_tile, 0.0), axis=-1, keepdims=True)
                wide = wide + jnp.where(wide_lanes == lane, column, 0.0)
            stats_rows_ref[:, rows] = wide.T[: 2 * heads, :]


def estimate(tok_count, row_width, slab_rows, matmuls, exps):
    flops = 2 * tok_count * slab_rows * HD * matmuls * (row_width // HD)
    return pl.CostEstimate(
        flops=flops,
        transcendentals=tok_count * slab_rows * exps * (row_width // HD),
        bytes_accessed=8 * tok_count * row_width * 4,
    )


def key_kernel(near_count, far_list, heads, block_total, *refs):
    far_count = len(far_list)
    position_ref, own_ref = refs[:2]
    span_refs = refs[2:5]
    gathered_ref = refs[5]
    far_rows = refs[6 : 6 + far_count]
    grad_key_ref, grad_value_ref = refs[6 + far_count :]
    segments = gathered_ref.shape[0]

    def segment_stats(step):
        return gathered_ref.at[jnp.minimum(position_ref[0] + step, segments - 1)]

    stats_refs = tuple(segment_stats(step) for step in range(3))
    far_stats = [segment_stats(offset // 2) for offset in far_list]
    width = heads * HD
    near_rows = near_count * BLK
    scale = 1.0 / math.sqrt(HD)
    first = 2 * position_ref[0]
    near_key_ids = lax.broadcasted_iota(jnp.int32, (BLK, near_rows), 0)
    near_query_ids = lax.broadcasted_iota(jnp.int32, (BLK, near_rows), 1)
    near_offset = near_query_ids // BLK
    near_causal = jnp.logical_or(near_offset > 0, near_query_ids % BLK >= near_key_ids)
    for block in range(2):
        rows = pl.ds(block * BLK, BLK)
        near_span = pl.ds(block * BLK, near_rows)
        near_mask = jnp.logical_and(near_causal, first + block + near_offset < block_total)
        far_live = [first + block + offset < block_total for offset in far_list]
        masks = [near_mask] + far_live
        for head in range(heads):
            cols = pl.ds(head * HD, HD)
            value_cols = pl.ds(width + head * HD, HD)
            key = own_ref[rows, cols]
            value = own_ref[rows, value_cols]
            queries = [span_load(span_refs, block * BLK, near_rows, cols, 0)]
            queries = queries + [item[rows, cols] for item in far_rows]
            grads = [span_load(span_refs, block * BLK, near_rows, value_cols, 0)]
            grads = grads + [item[rows, value_cols] for item in far_rows]
            totals = [span_load(stats_refs, block * BLK, near_rows, pl.ds(head, 1), 1)] + [
                item[pl.ds(head, 1), rows] for item in far_stats
            ]
            dots = [span_load(stats_refs, block * BLK, near_rows, pl.ds(heads + head, 1), 1)] + [
                item[pl.ds(heads + head, 1), rows] for item in far_stats
            ]
            grad_key = jnp.zeros((BLK, HD), jnp.float32)
            grad_value = jnp.zeros((BLK, HD), jnp.float32)
            for query, grad, log_total, out_dot, mask in zip(queries, grads, totals, dots, masks):
                score = lax.dot_general(key, query, TRANS_B, preferred_element_type=jnp.float32)
                prob = jnp.where(mask, jnp.exp(score * scale - log_total), 0.0)
                prob_grad = lax.dot_general(value, grad, TRANS_B, preferred_element_type=jnp.float32)
                score_grad = (prob * (prob_grad - out_dot)).astype(jnp.bfloat16)
                grad_value = grad_value + jnp.dot(
                    prob.astype(jnp.bfloat16), grad, preferred_element_type=jnp.float32
                )
                grad_key = grad_key + jnp.dot(score_grad, query, preferred_element_type=jnp.float32)
            grad_key_ref[rows, cols] = (grad_key * scale).astype(jnp.bfloat16)
            grad_value_ref[rows, cols] = grad_value.astype(jnp.bfloat16)


def smem_spec():
    return pl.BlockSpec(memory_space=pltpu.SMEM)


def vmem_spec():
    return pl.BlockSpec(memory_space=pltpu.VMEM)


def body(queries, key_tokens, value_tokens, grad_out):
    row_width = queries.shape[1]
    tok_count = queries.shape[0]
    devices = lax.axis_size("seq")
    blocks_dev, rim, near_list, far_list, far_shifts = plan(tok_count, devices)
    if not relay_ok(devices, blocks_dev, rim, far_shifts):
        return legacy_body(queries, key_tokens, value_tokens, grad_out)
    heads = row_width // HD
    offsets = near_list + far_list
    logit_scale = 1.0 / math.sqrt(HD)
    span_blocks = (rim + 1) * blocks_dev
    lead = rim * blocks_dev
    position = lax.axis_index("seq")
    odd = (position % 2) == 1
    pairs = swap_pairs(devices)
    keys_values = jnp.concatenate([key_tokens, value_tokens], axis=1)
    queries_grads = jnp.concatenate([queries, grad_out], axis=1)
    back2 = passed_along(keys_values, "seq", 2)
    ahead2 = passed_along(queries_grads, "seq", -2)
    swap_one = lax.ppermute(jnp.where(odd, queries_grads, keys_values), "seq", pairs)
    back4 = passed_along(back2, "seq", 2)
    ahead4 = passed_along(ahead2, "seq", -2)
    swap_two = lax.ppermute(jnp.where(odd, back2, ahead2), "seq", pairs)
    back1 = jnp.where(odd, swap_one, swap_two)
    ahead1 = jnp.where(odd, swap_two, swap_one)
    far_back = [back4] + [passed_along(keys_values, "seq", shift) for shift in far_shifts[1:]]
    far_ahead = [ahead4] + [passed_along(queries_grads, "seq", -shift) for shift in far_shifts[1:]]
    far_back = far_back[: len(far_shifts)]
    far_ahead = far_ahead[: len(far_shifts)]

    position_arr = jnp.reshape(position, (1,)).astype(jnp.int32)
    far_offsets = list(far_list)
    slab_rows = (len(near_list) + len(far_list)) * BLK
    row_inputs = (position_arr, queries, grad_out, back2, back1, keys_values, *far_back)
    attended, stats, stats_rows = pl.pallas_call(
        functools.partial(row_kernel, len(near_list), far_offsets, heads, "stats"),
        out_shape=(
            jax.ShapeDtypeStruct((tok_count, row_width), jnp.bfloat16),
            jax.ShapeDtypeStruct((tok_count, 2 * heads), jnp.float32),
            jax.ShapeDtypeStruct((2 * heads, tok_count), jnp.float32),
        ),
        in_specs=[smem_spec()] + [vmem_spec()] * (5 + len(far_back)),
        out_specs=(vmem_spec(), vmem_spec(), vmem_spec()),
        cost_estimate=estimate(tok_count, row_width, slab_rows, 2, 1),
        name="rows_stats",
    )(*row_inputs)
    gathered = lax.all_gather(stats_rows, "seq")
    grad_queries = pl.pallas_call(
        functools.partial(row_kernel, len(near_list), far_offsets, heads, "grad"),
        out_shape=jax.ShapeDtypeStruct((tok_count, row_width), jnp.bfloat16),
        in_specs=[smem_spec()] + [vmem_spec()] * (6 + len(far_back)),
        out_specs=vmem_spec(),
        cost_estimate=estimate(tok_count, row_width, slab_rows, 3, 1),
        name="rows_grad",
    )(*row_inputs, stats)
    grad_keys, grad_values = pl.pallas_call(
        functools.partial(key_kernel, len(near_list), far_offsets, heads, devices * blocks_dev),
        out_shape=(
            jax.ShapeDtypeStruct((tok_count, row_width), jnp.bfloat16),
            jax.ShapeDtypeStruct((tok_count, row_width), jnp.bfloat16),
        ),
        in_specs=[smem_spec()] + [vmem_spec()] * (5 + len(far_ahead)),
        out_specs=(vmem_spec(), vmem_spec()),
        cost_estimate=estimate(tok_count, row_width, slab_rows, 4, 1),
        name="keys_pass",
    )(
        position_arr,
        keys_values,
        queries_grads,
        ahead1,
        ahead2,
        gathered,
        *far_ahead,
    )
    return attended, grad_queries, grad_keys, grad_values


def solution(mesh):
    placed = (
        P(("rep", "seq"), None),
        P(("rep", "seq"), None),
        P(("rep", "seq"), None),
        P(("rep", "seq"), None),
    )
    return jax.shard_map(
        body,
        mesh=mesh,
        in_specs=placed,
        out_specs=(
            P(("rep", "seq"), None),
            P(("rep", "seq"), None),
            P(("rep", "seq"), None),
            P(("rep", "seq"), None),
        ),
        check_vma=False,
    )
```

```python
import functools
import math

import jax
import jax.numpy as jnp
from jax import lax
from jax.experimental import pallas as pl
from jax.experimental.pallas import tpu as pltpu
from jax.sharding import PartitionSpec as P

HEADS = 4
HD = 128
BLK = 128
WINDOW = 4


NEG = -1e30
CHUNKS = 2


def passed_along(value, axis, steps):
    count = lax.axis_size(axis)
    first, last = (max(0, -steps), min(count, count - steps))
    return lax.ppermute(value, axis, [(source, source + steps) for source in range(first, last)])


def offset_lists(block_total):
    near_list = list(range(WINDOW + 1))
    far_list = []
    stride = 1
    while stride < block_total:
        if stride > WINDOW:
            far_list.append(stride)
        stride = stride * 2
    return (near_list, far_list)


def allowed_mask(first_block, blocks_dev, offsets):
    block_ids = first_block + jnp.arange(blocks_dev, dtype=jnp.int32)
    offset_arr = jnp.array(offsets, dtype=jnp.int32)
    block_live = block_ids[:, None] - offset_arr[None, :] >= 0
    row_ids = jnp.arange(BLK, dtype=jnp.int32)
    causal = row_ids[:, None] >= row_ids[None, :]
    later_slab = offset_arr > 0
    slab_causal = jnp.logical_or(later_slab[None, :, None], causal[:, None, :])
    allowed = jnp.logical_and(block_live[:, None, :, None], slab_causal[None, :, :, :])
    return allowed.reshape(blocks_dev, BLK, len(offsets) * BLK)


def head_cols(array_in, col_start):
    return array_in[..., col_start : col_start + HD]


def to_blocks(array_in, block_count):
    return array_in.reshape(block_count, BLK, array_in.shape[-1])


def place_slabs(gradient, near_list, lead, span_blocks):
    blocks_dev = gradient.shape[0]
    placed = []
    for slot_index, offset in enumerate(near_list):
        before = lead - offset
        after = span_blocks - before - blocks_dev
        placed.append(jnp.pad(gradient[:, slot_index], ((before, after), (0, 0), (0, 0))))
    total = placed[0]
    for item in placed[1:]:
        total = total + item
    return total


def head_pass(query_per_head, output_gradient_heads, key_slabs, value_slabs, allowed, logit_scale):
    block_count = key_slabs.shape[0]
    key_row_block = key_slabs.reshape(block_count, -1, HD)
    value_row_block = value_slabs.reshape(block_count, -1, HD)
    score_matrix = (
        jnp.einsum(
            "nmv,njv->nmj", query_per_head, key_row_block, preferred_element_type=jnp.float32
        )
        * logit_scale
    )
    score_matrix = jnp.where(allowed, score_matrix, NEG)
    row_max = jnp.max(score_matrix, axis=-1, keepdims=True)
    log_total = row_max + jnp.log(jnp.sum(jnp.exp(score_matrix - row_max), axis=-1, keepdims=True))
    probabilities = jnp.exp(score_matrix - log_total)
    attention_weight = probabilities.astype(jnp.bfloat16)
    attended_per_head = jnp.einsum(
        "jym,jmo->jyo", attention_weight, value_row_block, preferred_element_type=jnp.float32
    ).astype(jnp.bfloat16)
    out_dot = jnp.sum(
        output_gradient_heads.astype(jnp.float32) * attended_per_head.astype(jnp.float32),
        axis=-1,
        keepdims=True,
    )
    probability_gradient = jnp.einsum(
        "nmv,njv->nmj", output_gradient_heads, value_row_block, preferred_element_type=jnp.float32
    )
    score_gradient = (probabilities * (probability_gradient - out_dot)).astype(jnp.bfloat16)
    query_gradient_heads = (
        jnp.einsum(
            "jym,jmo->jyo", score_gradient, key_row_block, preferred_element_type=jnp.float32
        )
        * logit_scale
    ).astype(jnp.bfloat16)
    key_gradient = (
        jnp.einsum(
            "uwj,uwn->ujn", score_gradient, query_per_head, preferred_element_type=jnp.float32
        )
        * logit_scale
    )
    value_gradient = jnp.einsum(
        "uwj,uwn->ujn", attention_weight, output_gradient_heads, preferred_element_type=jnp.float32
    )
    return (
        attended_per_head,
        query_gradient_heads,
        key_gradient,
        value_gradient,
        log_total[..., 0],
        out_dot[..., 0],
    )


def legacy_body(queries, key_tokens, value_tokens, grad_out):
    row_width = queries.shape[1]
    tok_count = queries.shape[0]
    blocks_dev = tok_count // BLK
    rim = (WINDOW + blocks_dev - 1) // blocks_dev
    devices = lax.axis_size("seq")
    near_list, far_list = offset_lists(devices * blocks_dev)
    offsets = near_list + far_list
    near_count = len(near_list)
    logit_scale = 1.0 / math.sqrt(HD)
    span_blocks = (rim + 1) * blocks_dev
    lead = rim * blocks_dev
    earlier_keys = []
    earlier_values = []
    for back in range(rim, 0, -1):
        got_keys, got_values = passed_along((key_tokens, value_tokens), "seq", back)
        earlier_keys.append(got_keys)
        earlier_values.append(got_values)
    span_keys = to_blocks(jnp.concatenate(earlier_keys + [key_tokens], axis=0), span_blocks)
    span_values = to_blocks(jnp.concatenate(earlier_values + [value_tokens], axis=0), span_blocks)
    far_keys = []
    far_values = []
    for stride in far_list:
        got_keys, got_values = passed_along((key_tokens, value_tokens), "seq", stride // blocks_dev)
        far_keys.append(to_blocks(got_keys, blocks_dev))
        far_values.append(to_blocks(got_values, blocks_dev))
    position = lax.axis_index("seq")
    allowed = allowed_mask(position * blocks_dev, blocks_dev, offsets)
    query_blocks = to_blocks(queries, blocks_dev)
    grad_blocks = to_blocks(grad_out, blocks_dev)
    attended_heads = []
    grad_query_heads = []
    near_key_heads = []
    near_value_heads = []
    total_heads = []
    dot_heads = []
    far_key_parts = [[] for stride in far_list]
    far_value_parts = [[] for stride in far_list]
    for head_index in range(HEADS):
        col_start = head_index * HD
        key_slabs = jnp.stack(
            [
                head_cols(span_keys[lead - offset : lead + blocks_dev - offset], col_start)
                for offset in near_list
            ]
            + [head_cols(item, col_start) for item in far_keys],
            axis=1,
        )
        value_slabs = jnp.stack(
            [
                head_cols(span_values[lead - offset : lead + blocks_dev - offset], col_start)
                for offset in near_list
            ]
            + [head_cols(item, col_start) for item in far_values],
            axis=1,
        )
        (
            attended_per_head,
            query_gradient_heads,
            key_gradient,
            value_gradient,
            log_total,
            out_dot,
        ) = head_pass(
            head_cols(query_blocks, col_start),
            head_cols(grad_blocks, col_start),
            key_slabs,
            value_slabs,
            allowed,
            logit_scale,
        )
        key_gradient = key_gradient.reshape(blocks_dev, -1, BLK, HD)
        value_gradient = value_gradient.reshape(blocks_dev, -1, BLK, HD)
        near_key_heads.append(place_slabs(key_gradient, near_list, lead, span_blocks))
        near_value_heads.append(place_slabs(value_gradient, near_list, lead, span_blocks))
        for level_index in range(len(far_list)):
            far_key_parts[level_index].append(
                key_gradient[:, near_count + level_index].astype(jnp.bfloat16)
            )
            far_value_parts[level_index].append(
                value_gradient[:, near_count + level_index].astype(jnp.bfloat16)
            )
        attended_heads.append(attended_per_head)
        grad_query_heads.append(query_gradient_heads)
        total_heads.append(log_total)
        dot_heads.append(out_dot)
    attended = jnp.concatenate(attended_heads, axis=-1).reshape(tok_count, row_width)
    grad_queries = jnp.concatenate(grad_query_heads, axis=-1).reshape(tok_count, row_width)
    near_keys = jnp.concatenate(near_key_heads, axis=-1).reshape((rim + 1) * tok_count, row_width)
    near_values = jnp.concatenate(near_value_heads, axis=-1).reshape(
        (rim + 1) * tok_count, row_width
    )
    total_keys = near_keys[lead * BLK :].astype(jnp.bfloat16).astype(jnp.float32)
    total_values = near_values[lead * BLK :].astype(jnp.bfloat16).astype(jnp.float32)
    for back in range(1, rim + 1):
        piece_start = (rim - back) * tok_count
        part_keys = near_keys[piece_start : piece_start + tok_count].astype(jnp.bfloat16)
        part_values = near_values[piece_start : piece_start + tok_count].astype(jnp.bfloat16)
        back_keys, back_values = passed_along((part_keys, part_values), "seq", -back)
        total_keys = total_keys + back_keys.astype(jnp.float32)
        total_values = total_values + back_values.astype(jnp.float32)
    for level_index, stride in enumerate(far_list):
        part_keys = jnp.concatenate(far_key_parts[level_index], axis=-1).reshape(
            tok_count, row_width
        )
        part_values = jnp.concatenate(far_value_parts[level_index], axis=-1).reshape(
            tok_count, row_width
        )
        got_keys, got_values = passed_along(
            (part_keys, part_values), "seq", -(stride // blocks_dev)
        )
        total_keys = total_keys + got_keys.astype(jnp.float32)
        total_values = total_values + got_values.astype(jnp.float32)
    return (
        attended,
        grad_queries,
        total_keys.astype(jnp.bfloat16),
        total_values.astype(jnp.bfloat16),
    )


def swap_pairs(count):
    return [(source, source ^ 1) for source in range(count) if source ^ 1 < count]


def relay_ok(count, blocks_dev, rim, far_shifts):
    return count % 2 == 0 and blocks_dev == 2 and rim == 2 and bool(far_shifts) and far_shifts[0] == 4


def plan(tok_count, devices):
    blocks_dev = tok_count // BLK
    rim = (WINDOW + blocks_dev - 1) // blocks_dev
    near_list, far_list = offset_lists(devices * blocks_dev)
    far_shifts = [stride // blocks_dev for stride in far_list]
    return blocks_dev, rim, near_list, far_list, far_shifts


def row_pass(query_per_head, output_gradient_heads, key_slabs, value_slabs, allowed, logit_scale):
    block_count = key_slabs.shape[0]
    key_row_block = key_slabs.reshape(block_count, -1, HD)
    value_row_block = value_slabs.reshape(block_count, -1, HD)
    score_matrix = (
        jnp.einsum(
            "nmv,njv->nmj", query_per_head, key_row_block, preferred_element_type=jnp.float32
        )
        * logit_scale
    )
    score_matrix = jnp.where(allowed, score_matrix, NEG)
    row_max = jnp.max(score_matrix, axis=-1, keepdims=True)
    log_total = row_max + jnp.log(jnp.sum(jnp.exp(score_matrix - row_max), axis=-1, keepdims=True))
    probabilities = jnp.exp(score_matrix - log_total)
    attention_weight = probabilities.astype(jnp.bfloat16)
    attended_per_head = jnp.einsum(
        "jym,jmo->jyo", attention_weight, value_row_block, preferred_element_type=jnp.float32
    ).astype(jnp.bfloat16)
    out_dot = jnp.sum(
        output_gradient_heads.astype(jnp.float32) * attended_per_head.astype(jnp.float32),
        axis=-1,
        keepdims=True,
    )
    probability_gradient = jnp.einsum(
        "nmv,njv->nmj", output_gradient_heads, value_row_block, preferred_element_type=jnp.float32
    )
    score_gradient = (probabilities * (probability_gradient - out_dot)).astype(jnp.bfloat16)
    query_gradient_heads = (
        jnp.einsum(
            "jym,jmo->jyo", score_gradient, key_row_block, preferred_element_type=jnp.float32
        )
        * logit_scale
    ).astype(jnp.bfloat16)
    return attended_per_head, query_gradient_heads, log_total[..., 0], out_dot[..., 0]


def key_pass(key_per_head, value_per_head, query_slabs, grad_slabs, total_slabs, dot_slabs, allowed, logit_scale):
    block_count = query_slabs.shape[0]
    query_rows = query_slabs.reshape(block_count, -1, HD)
    grad_rows = grad_slabs.reshape(block_count, -1, HD)
    score_matrix = (
        jnp.einsum("nmv,njv->nmj", query_rows, key_per_head, preferred_element_type=jnp.float32)
        * logit_scale
    )
    total_rows = total_slabs.reshape(block_count, -1, 1)
    dot_rows = dot_slabs.reshape(block_count, -1, 1)
    probabilities = jnp.where(allowed, jnp.exp(score_matrix - total_rows), 0.0)
    probability_gradient = jnp.einsum(
        "nmv,njv->nmj", grad_rows, value_per_head, preferred_element_type=jnp.float32
    )
    score_gradient = (probabilities * (probability_gradient - dot_rows)).astype(jnp.bfloat16)
    attention_weight = probabilities.astype(jnp.bfloat16)
    key_gradient = (
        jnp.einsum("nmj,nmv->njv", score_gradient, query_rows, preferred_element_type=jnp.float32)
        * logit_scale
    )
    value_gradient = jnp.einsum(
        "nmj,nmv->njv", attention_weight, grad_rows, preferred_element_type=jnp.float32
    )
    return key_gradient, value_gradient


def key_allowed(first_block, blocks_dev, offsets, block_total):
    block_ids = first_block + jnp.arange(blocks_dev, dtype=jnp.int32)
    offset_arr = jnp.array(offsets, dtype=jnp.int32)
    query_live = block_ids[:, None] + offset_arr[None, :] < block_total
    row_ids = jnp.arange(BLK, dtype=jnp.int32)
    causal = row_ids[:, None] >= row_ids[None, :]
    later_slab = offset_arr > 0
    slab_causal = jnp.logical_or(later_slab[:, None, None], causal[None, :, :])
    allowed = jnp.logical_and(query_live[:, :, None, None], slab_causal[None, :, :, :])
    return allowed.reshape(blocks_dev, len(offsets) * BLK, BLK)


TRANS_B = (((1,), (1,)), ((), ()))


def span_load(refs, start, length, other, axis):
    pieces = []
    base = 0
    for ref in refs:
        size = ref.shape[axis]
        low = max(start, base)
        high = min(start + length, base + size)
        if low < high:
            window = pl.ds(low - base, high - low)
            pieces.append(ref[window, other] if axis == 0 else ref[other, window])
        base += size
    return pieces[0] if len(pieces) == 1 else jnp.concatenate(pieces, axis=axis)


def row_kernel(near_count, far_list, heads, phase, *refs):
    far_count = len(far_list)
    position_ref, query_ref, grad_ref = refs[:3]
    span_refs = refs[3:7]
    far_items = refs[7 : 8 + far_count]
    if phase == "stats":
        attended_ref, stats_ref, stats_rows_ref = refs[8 + far_count :]
    else:
        stats_in_ref, grad_query_ref = refs[8 + far_count :]
    width = heads * HD
    near_rows = near_count * BLK
    scale = 1.0 / math.sqrt(HD)
    first = 2 * position_ref[0]
    near_row_ids = lax.broadcasted_iota(jnp.int32, (BLK, near_rows), 0)
    near_col_ids = lax.broadcasted_iota(jnp.int32, (BLK, near_rows), 1)
    near_offset = (near_count - 1) - near_col_ids // BLK
    near_causal = jnp.logical_or(near_offset > 0, near_row_ids >= near_col_ids % BLK)
    lane_ids = lax.broadcasted_iota(jnp.int32, (BLK, 2 * heads), 1)
    for block in range(2):
        rows = pl.ds(block * BLK, BLK)
        near_span = pl.ds(block * BLK, near_rows)
        near_mask = jnp.logical_and(near_causal, first + block - near_offset >= 0)
        far_live = [first + block - offset >= 0 for offset in far_list]
        masks = [near_mask] + far_live
        if phase == "stats":
            stats_tile = jnp.zeros((BLK, 2 * heads), jnp.float32)
        else:
            stats_tile = stats_in_ref[rows, :]
        for head in range(heads):
            cols = pl.ds(head * HD, HD)
            value_cols = pl.ds(width + head * HD, HD)
            query = query_ref[rows, cols]
            grad = grad_ref[rows, cols]
            keys = [span_load(span_refs, block * BLK, near_rows, cols, 0)]
            far_views = [(far_items[block], pl.ds(0, BLK))] + [
                (item, rows) for item in far_items[2:]
            ]
            keys = keys + [item[window, cols] for item, window in far_views]
            values = [span_load(span_refs, block * BLK, near_rows, value_cols, 0)]
            values = values + [item[window, value_cols] for item, window in far_views]
            scores = [
                lax.dot_general(query, key, TRANS_B, preferred_element_type=jnp.float32) * scale
                for key in keys
            ]
            if phase == "grad":
                log_total = jnp.sum(jnp.where(lane_ids == head, stats_tile, 0.0), axis=-1, keepdims=True)
                out_dot = jnp.sum(
                    jnp.where(lane_ids == heads + head, stats_tile, 0.0), axis=-1, keepdims=True
                )
                probs = [
                    jnp.where(mask, jnp.exp(score - log_total), 0.0)
                    for score, mask in zip(scores, masks)
                ]
                grad_query = jnp.zeros((BLK, HD), jnp.float32)
                for prob, key, value in zip(probs, keys, values):
                    prob_grad = lax.dot_general(
                        grad, value, TRANS_B, preferred_element_type=jnp.float32
                    )
                    score_grad = (prob * (prob_grad - out_dot)).astype(jnp.bfloat16)
                    grad_query = grad_query + jnp.dot(
                        score_grad, key, preferred_element_type=jnp.float32
                    )
                grad_query_ref[rows, cols] = (grad_query * scale).astype(jnp.bfloat16)
                continue
            scores = [jnp.where(mask, score, NEG) for score, mask in zip(scores, masks)]
            row_max = scores[0].max(axis=-1, keepdims=True)
            for score in scores[1:]:
                row_max = jnp.maximum(row_max, score.max(axis=-1, keepdims=True))
            shifted = [jnp.exp(score - row_max) for score in scores]
            row_sum = shifted[0].sum(axis=-1, keepdims=True)
            for item in shifted[1:]:
                row_sum = row_sum + item.sum(axis=-1, keepdims=True)
            log_total = row_max + jnp.log(row_sum)
            inverse = 1.0 / row_sum
            attended = jnp.zeros((BLK, HD), jnp.float32)
            for item, value in zip(shifted, values):
                attended = attended + jnp.dot(
                    (item * inverse).astype(jnp.bfloat16), value, preferred_element_type=jnp.float32
                )
            attended = attended.astype(jnp.bfloat16)
            attended_ref[rows, cols] = attended
            out_dot = jnp.sum(
                grad.astype(jnp.float32) * attended.astype(jnp.float32), axis=-1, keepdims=True
            )
            stats_tile = stats_tile + jnp.where(lane_ids == head, log_total, 0.0)
            stats_tile = stats_tile + jnp.where(lane_ids == heads + head, out_dot, 0.0)
        if phase == "stats":
            stats_ref[rows, :] = stats_tile
            wide_lanes = lax.broadcasted_iota(jnp.int32, (BLK, BLK), 1)
            wide = jnp.zeros((BLK, BLK), jnp.float32)
            for lane in range(2 * heads):
                column = jnp.sum(jnp.where(lane_ids == lane, stats_tile, 0.0), axis=-1, keepdims=True)
                wide = wide + jnp.where(wide_lanes == lane, column, 0.0)
            stats_rows_ref[:, rows] = wide.T[: 2 * heads, :]


def estimate(tok_count, row_width, slab_rows, matmuls, exps):
    flops = 2 * tok_count * slab_rows * HD * matmuls * (row_width // HD)
    return pl.CostEstimate(
        flops=flops,
        transcendentals=tok_count * slab_rows * exps * (row_width // HD),
        bytes_accessed=8 * tok_count * row_width * 4,
    )


def key_kernel(near_count, far_list, heads, block_total, *refs):
    far_count = len(far_list)
    position_ref, own_ref = refs[:2]
    span_refs = refs[2:5]
    stats_refs = refs[5:8]
    far_rows = refs[8 : 8 + far_count]
    far_stats = refs[8 + far_count : 8 + 2 * far_count]
    grad_key_ref, grad_value_ref = refs[8 + 2 * far_count :]
    width = heads * HD
    near_rows = near_count * BLK
    scale = 1.0 / math.sqrt(HD)
    first = 2 * position_ref[0]
    near_key_ids = lax.broadcasted_iota(jnp.int32, (BLK, near_rows), 0)
    near_query_ids = lax.broadcasted_iota(jnp.int32, (BLK, near_rows), 1)
    near_offset = near_query_ids // BLK
    near_causal = jnp.logical_or(near_offset > 0, near_query_ids % BLK >= near_key_ids)
    for block in range(2):
        rows = pl.ds(block * BLK, BLK)
        near_span = pl.ds(block * BLK, near_rows)
        near_mask = jnp.logical_and(near_causal, first + block + near_offset < block_total)
        far_live = [first + block + offset < block_total for offset in far_list]
        masks = [near_mask] + far_live
        for head in range(heads):
            cols = pl.ds(head * HD, HD)
            value_cols = pl.ds(width + head * HD, HD)
            key = own_ref[rows, cols]
            value = own_ref[rows, value_cols]
            queries = [span_load(span_refs, block * BLK, near_rows, cols, 0)]
            queries = queries + [item[rows, cols] for item in far_rows]
            grads = [span_load(span_refs, block * BLK, near_rows, value_cols, 0)]
            grads = grads + [item[rows, value_cols] for item in far_rows]
            totals = [span_load(stats_refs, block * BLK, near_rows, pl.ds(head, 1), 1)] + [
                item[pl.ds(head, 1), rows] for item in far_stats
            ]
            dots = [span_load(stats_refs, block * BLK, near_rows, pl.ds(heads + head, 1), 1)] + [
                item[pl.ds(heads + head, 1), rows] for item in far_stats
            ]
            grad_key = jnp.zeros((BLK, HD), jnp.float32)
            grad_value = jnp.zeros((BLK, HD), jnp.float32)
            for query, grad, log_total, out_dot, mask in zip(queries, grads, totals, dots, masks):
                score = lax.dot_general(key, query, TRANS_B, preferred_element_type=jnp.float32)
                prob = jnp.where(mask, jnp.exp(score * scale - log_total), 0.0)
                prob_grad = lax.dot_general(value, grad, TRANS_B, preferred_element_type=jnp.float32)
                score_grad = (prob * (prob_grad - out_dot)).astype(jnp.bfloat16)
                grad_value = grad_value + jnp.dot(
                    prob.astype(jnp.bfloat16), grad, preferred_element_type=jnp.float32
                )
                grad_key = grad_key + jnp.dot(score_grad, query, preferred_element_type=jnp.float32)
            grad_key_ref[rows, cols] = (grad_key * scale).astype(jnp.bfloat16)
            grad_value_ref[rows, cols] = grad_value.astype(jnp.bfloat16)


def smem_spec():
    return pl.BlockSpec(memory_space=pltpu.SMEM)


def vmem_spec():
    return pl.BlockSpec(memory_space=pltpu.VMEM)


def body(queries, key_tokens, value_tokens, grad_out):
    row_width = queries.shape[1]
    tok_count = queries.shape[0]
    devices = lax.axis_size("seq")
    blocks_dev, rim, near_list, far_list, far_shifts = plan(tok_count, devices)
    if not relay_ok(devices, blocks_dev, rim, far_shifts):
        return legacy_body(queries, key_tokens, value_tokens, grad_out)
    heads = row_width // HD
    offsets = near_list + far_list
    logit_scale = 1.0 / math.sqrt(HD)
    span_blocks = (rim + 1) * blocks_dev
    lead = rim * blocks_dev
    position = lax.axis_index("seq")
    odd = (position % 2) == 1
    pairs = swap_pairs(devices)
    keys_values = jnp.concatenate([key_tokens, value_tokens], axis=1)
    queries_grads = jnp.concatenate([queries, grad_out], axis=1)
    back2_top = passed_along(keys_values[:BLK], "seq", 2)
    back2_bottom = passed_along(keys_values[BLK:], "seq", 2)
    back2 = jnp.concatenate([back2_top, back2_bottom], axis=0)
    ahead2 = passed_along(queries_grads, "seq", -2)
    swap_one = lax.ppermute(jnp.where(odd, queries_grads, keys_values), "seq", pairs)
    back4_top = passed_along(back2_top, "seq", 2)
    back4_bottom = passed_along(back2_bottom, "seq", 2)
    ahead4 = passed_along(ahead2, "seq", -2)
    swap_two = lax.ppermute(jnp.where(odd, back2, ahead2), "seq", pairs)
    back1 = jnp.where(odd, swap_one, swap_two)
    ahead1 = jnp.where(odd, swap_two, swap_one)
    far_back = [back4_top, back4_bottom] + [
        passed_along(keys_values, "seq", shift) for shift in far_shifts[1:]
    ]
    far_ahead = [ahead4] + [passed_along(queries_grads, "seq", -shift) for shift in far_shifts[1:]]
    far_ahead = far_ahead[: len(far_shifts)]

    position_arr = jnp.reshape(position, (1,)).astype(jnp.int32)
    far_offsets = list(far_list)
    slab_rows = (len(near_list) + len(far_list)) * BLK
    row_inputs = (position_arr, queries, grad_out, back2_top, back2_bottom, back1, keys_values, *far_back)
    attended, stats, stats_rows = pl.pallas_call(
        functools.partial(row_kernel, len(near_list), far_offsets, heads, "stats"),
        out_shape=(
            jax.ShapeDtypeStruct((tok_count, row_width), jnp.bfloat16),
            jax.ShapeDtypeStruct((tok_count, 2 * heads), jnp.float32),
            jax.ShapeDtypeStruct((2 * heads, tok_count), jnp.float32),
        ),
        in_specs=[smem_spec()] + [vmem_spec()] * (6 + len(far_back)),
        out_specs=(vmem_spec(), vmem_spec(), vmem_spec()),
        cost_estimate=estimate(tok_count, row_width, slab_rows, 2, 1),
        name="rows_stats",
    )(*row_inputs)
    stats_one = passed_along(stats_rows, "seq", -1)
    stats_two = passed_along(stats_rows, "seq", -2)
    far_stats = [passed_along(stats_rows, "seq", -shift) for shift in far_shifts]
    grad_queries = pl.pallas_call(
        functools.partial(row_kernel, len(near_list), far_offsets, heads, "grad"),
        out_shape=jax.ShapeDtypeStruct((tok_count, row_width), jnp.bfloat16),
        in_specs=[smem_spec()] + [vmem_spec()] * (7 + len(far_back)),
        out_specs=vmem_spec(),
        cost_estimate=estimate(tok_count, row_width, slab_rows, 3, 1),
        name="rows_grad",
    )(*row_inputs, stats)
    grad_keys, grad_values = pl.pallas_call(
        functools.partial(key_kernel, len(near_list), far_offsets, heads, devices * blocks_dev),
        out_shape=(
            jax.ShapeDtypeStruct((tok_count, row_width), jnp.bfloat16),
            jax.ShapeDtypeStruct((tok_count, row_width), jnp.bfloat16),
        ),
        in_specs=[smem_spec()] + [vmem_spec()] * (7 + 2 * len(far_ahead)),
        out_specs=(vmem_spec(), vmem_spec()),
        cost_estimate=estimate(tok_count, row_width, slab_rows, 4, 1),
        name="keys_pass",
    )(
        position_arr,
        keys_values,
        queries_grads,
        ahead1,
        ahead2,
        stats_rows,
        stats_one,
        stats_two,
        *far_ahead,
        *far_stats,
    )
    return attended, grad_queries, grad_keys, grad_values


def solution(mesh):
    placed = (
        P(("rep", "seq"), None),
        P(("rep", "seq"), None),
        P(("rep", "seq"), None),
        P(("rep", "seq"), None),
    )
    return jax.shard_map(
        body,
        mesh=mesh,
        in_specs=placed,
        out_specs=(
            P(("rep", "seq"), None),
            P(("rep", "seq"), None),
            P(("rep", "seq"), None),
            P(("rep", "seq"), None),
        ),
        check_vma=False,
    )
```

```python
import functools
import math

import jax
import jax.numpy as jnp
from jax import lax
from jax.experimental import pallas as pl
from jax.experimental.pallas import tpu as pltpu
from jax.sharding import PartitionSpec as P

HEADS = 4
HD = 128
BLK = 128
WINDOW = 4


NEG = -1e30
CHUNKS = 2


def passed_along(value, axis, steps):
    count = lax.axis_size(axis)
    first, last = (max(0, -steps), min(count, count - steps))
    return lax.ppermute(value, axis, [(source, source + steps) for source in range(first, last)])


def offset_lists(block_total):
    near_list = list(range(WINDOW + 1))
    far_list = []
    stride = 1
    while stride < block_total:
        if stride > WINDOW:
            far_list.append(stride)
        stride = stride * 2
    return (near_list, far_list)


def allowed_mask(first_block, blocks_dev, offsets):
    block_ids = first_block + jnp.arange(blocks_dev, dtype=jnp.int32)
    offset_arr = jnp.array(offsets, dtype=jnp.int32)
    block_live = block_ids[:, None] - offset_arr[None, :] >= 0
    row_ids = jnp.arange(BLK, dtype=jnp.int32)
    causal = row_ids[:, None] >= row_ids[None, :]
    later_slab = offset_arr > 0
    slab_causal = jnp.logical_or(later_slab[None, :, None], causal[:, None, :])
    allowed = jnp.logical_and(block_live[:, None, :, None], slab_causal[None, :, :, :])
    return allowed.reshape(blocks_dev, BLK, len(offsets) * BLK)


def head_cols(array_in, col_start):
    return array_in[..., col_start : col_start + HD]


def to_blocks(array_in, block_count):
    return array_in.reshape(block_count, BLK, array_in.shape[-1])


def place_slabs(gradient, near_list, lead, span_blocks):
    blocks_dev = gradient.shape[0]
    placed = []
    for slot_index, offset in enumerate(near_list):
        before = lead - offset
        after = span_blocks - before - blocks_dev
        placed.append(jnp.pad(gradient[:, slot_index], ((before, after), (0, 0), (0, 0))))
    total = placed[0]
    for item in placed[1:]:
        total = total + item
    return total


def head_pass(query_per_head, output_gradient_heads, key_slabs, value_slabs, allowed, logit_scale):
    block_count = key_slabs.shape[0]
    key_row_block = key_slabs.reshape(block_count, -1, HD)
    value_row_block = value_slabs.reshape(block_count, -1, HD)
    score_matrix = (
        jnp.einsum(
            "nmv,njv->nmj", query_per_head, key_row_block, preferred_element_type=jnp.float32
        )
        * logit_scale
    )
    score_matrix = jnp.where(allowed, score_matrix, NEG)
    row_max = jnp.max(score_matrix, axis=-1, keepdims=True)
    log_total = row_max + jnp.log(jnp.sum(jnp.exp(score_matrix - row_max), axis=-1, keepdims=True))
    probabilities = jnp.exp(score_matrix - log_total)
    attention_weight = probabilities.astype(jnp.bfloat16)
    attended_per_head = jnp.einsum(
        "jym,jmo->jyo", attention_weight, value_row_block, preferred_element_type=jnp.float32
    ).astype(jnp.bfloat16)
    out_dot = jnp.sum(
        output_gradient_heads.astype(jnp.float32) * attended_per_head.astype(jnp.float32),
        axis=-1,
        keepdims=True,
    )
    probability_gradient = jnp.einsum(
        "nmv,njv->nmj", output_gradient_heads, value_row_block, preferred_element_type=jnp.float32
    )
    score_gradient = (probabilities * (probability_gradient - out_dot)).astype(jnp.bfloat16)
    query_gradient_heads = (
        jnp.einsum(
            "jym,jmo->jyo", score_gradient, key_row_block, preferred_element_type=jnp.float32
        )
        * logit_scale
    ).astype(jnp.bfloat16)
    key_gradient = (
        jnp.einsum(
            "uwj,uwn->ujn", score_gradient, query_per_head, preferred_element_type=jnp.float32
        )
        * logit_scale
    )
    value_gradient = jnp.einsum(
        "uwj,uwn->ujn", attention_weight, output_gradient_heads, preferred_element_type=jnp.float32
    )
    return (
        attended_per_head,
        query_gradient_heads,
        key_gradient,
        value_gradient,
        log_total[..., 0],
        out_dot[..., 0],
    )


def legacy_body(queries, key_tokens, value_tokens, grad_out):
    row_width = queries.shape[1]
    tok_count = queries.shape[0]
    blocks_dev = tok_count // BLK
    rim = (WINDOW + blocks_dev - 1) // blocks_dev
    devices = lax.axis_size("seq")
    near_list, far_list = offset_lists(devices * blocks_dev)
    offsets = near_list + far_list
    near_count = len(near_list)
    logit_scale = 1.0 / math.sqrt(HD)
    span_blocks = (rim + 1) * blocks_dev
    lead = rim * blocks_dev
    earlier_keys = []
    earlier_values = []
    for back in range(rim, 0, -1):
        got_keys, got_values = passed_along((key_tokens, value_tokens), "seq", back)
        earlier_keys.append(got_keys)
        earlier_values.append(got_values)
    span_keys = to_blocks(jnp.concatenate(earlier_keys + [key_tokens], axis=0), span_blocks)
    span_values = to_blocks(jnp.concatenate(earlier_values + [value_tokens], axis=0), span_blocks)
    far_keys = []
    far_values = []
    for stride in far_list:
        got_keys, got_values = passed_along((key_tokens, value_tokens), "seq", stride // blocks_dev)
        far_keys.append(to_blocks(got_keys, blocks_dev))
        far_values.append(to_blocks(got_values, blocks_dev))
    position = lax.axis_index("seq")
    allowed = allowed_mask(position * blocks_dev, blocks_dev, offsets)
    query_blocks = to_blocks(queries, blocks_dev)
    grad_blocks = to_blocks(grad_out, blocks_dev)
    attended_heads = []
    grad_query_heads = []
    near_key_heads = []
    near_value_heads = []
    total_heads = []
    dot_heads = []
    far_key_parts = [[] for stride in far_list]
    far_value_parts = [[] for stride in far_list]
    for head_index in range(HEADS):
        col_start = head_index * HD
        key_slabs = jnp.stack(
            [
                head_cols(span_keys[lead - offset : lead + blocks_dev - offset], col_start)
                for offset in near_list
            ]
            + [head_cols(item, col_start) for item in far_keys],
            axis=1,
        )
        value_slabs = jnp.stack(
            [
                head_cols(span_values[lead - offset : lead + blocks_dev - offset], col_start)
                for offset in near_list
            ]
            + [head_cols(item, col_start) for item in far_values],
            axis=1,
        )
        (
            attended_per_head,
            query_gradient_heads,
            key_gradient,
            value_gradient,
            log_total,
            out_dot,
        ) = head_pass(
            head_cols(query_blocks, col_start),
            head_cols(grad_blocks, col_start),
            key_slabs,
            value_slabs,
            allowed,
            logit_scale,
        )
        key_gradient = key_gradient.reshape(blocks_dev, -1, BLK, HD)
        value_gradient = value_gradient.reshape(blocks_dev, -1, BLK, HD)
        near_key_heads.append(place_slabs(key_gradient, near_list, lead, span_blocks))
        near_value_heads.append(place_slabs(value_gradient, near_list, lead, span_blocks))
        for level_index in range(len(far_list)):
            far_key_parts[level_index].append(
                key_gradient[:, near_count + level_index].astype(jnp.bfloat16)
            )
            far_value_parts[level_index].append(
                value_gradient[:, near_count + level_index].astype(jnp.bfloat16)
            )
        attended_heads.append(attended_per_head)
        grad_query_heads.append(query_gradient_heads)
        total_heads.append(log_total)
        dot_heads.append(out_dot)
    attended = jnp.concatenate(attended_heads, axis=-1).reshape(tok_count, row_width)
    grad_queries = jnp.concatenate(grad_query_heads, axis=-1).reshape(tok_count, row_width)
    near_keys = jnp.concatenate(near_key_heads, axis=-1).reshape((rim + 1) * tok_count, row_width)
    near_values = jnp.concatenate(near_value_heads, axis=-1).reshape(
        (rim + 1) * tok_count, row_width
    )
    total_keys = near_keys[lead * BLK :].astype(jnp.bfloat16).astype(jnp.float32)
    total_values = near_values[lead * BLK :].astype(jnp.bfloat16).astype(jnp.float32)
    for back in range(1, rim + 1):
        piece_start = (rim - back) * tok_count
        part_keys = near_keys[piece_start : piece_start + tok_count].astype(jnp.bfloat16)
        part_values = near_values[piece_start : piece_start + tok_count].astype(jnp.bfloat16)
        back_keys, back_values = passed_along((part_keys, part_values), "seq", -back)
        total_keys = total_keys + back_keys.astype(jnp.float32)
        total_values = total_values + back_values.astype(jnp.float32)
    for level_index, stride in enumerate(far_list):
        part_keys = jnp.concatenate(far_key_parts[level_index], axis=-1).reshape(
            tok_count, row_width
        )
        part_values = jnp.concatenate(far_value_parts[level_index], axis=-1).reshape(
            tok_count, row_width
        )
        got_keys, got_values = passed_along(
            (part_keys, part_values), "seq", -(stride // blocks_dev)
        )
        total_keys = total_keys + got_keys.astype(jnp.float32)
        total_values = total_values + got_values.astype(jnp.float32)
    return (
        attended,
        grad_queries,
        total_keys.astype(jnp.bfloat16),
        total_values.astype(jnp.bfloat16),
    )


def swap_pairs(count):
    return [(source, source ^ 1) for source in range(count) if source ^ 1 < count]


def relay_ok(count, blocks_dev, rim, far_shifts):
    return count % 2 == 0 and blocks_dev == 2 and rim == 2 and (not far_shifts or far_shifts[0] == 4)


def plan(tok_count, devices):
    blocks_dev = tok_count // BLK
    rim = (WINDOW + blocks_dev - 1) // blocks_dev
    near_list, far_list = offset_lists(devices * blocks_dev)
    far_shifts = [stride // blocks_dev for stride in far_list]
    return blocks_dev, rim, near_list, far_list, far_shifts


def row_pass(query_per_head, output_gradient_heads, key_slabs, value_slabs, allowed, logit_scale):
    block_count = key_slabs.shape[0]
    key_row_block = key_slabs.reshape(block_count, -1, HD)
    value_row_block = value_slabs.reshape(block_count, -1, HD)
    score_matrix = (
        jnp.einsum(
            "nmv,njv->nmj", query_per_head, key_row_block, preferred_element_type=jnp.float32
        )
        * logit_scale
    )
    score_matrix = jnp.where(allowed, score_matrix, NEG)
    row_max = jnp.max(score_matrix, axis=-1, keepdims=True)
    log_total = row_max + jnp.log(jnp.sum(jnp.exp(score_matrix - row_max), axis=-1, keepdims=True))
    probabilities = jnp.exp(score_matrix - log_total)
    attention_weight = probabilities.astype(jnp.bfloat16)
    attended_per_head = jnp.einsum(
        "jym,jmo->jyo", attention_weight, value_row_block, preferred_element_type=jnp.float32
    ).astype(jnp.bfloat16)
    out_dot = jnp.sum(
        output_gradient_heads.astype(jnp.float32) * attended_per_head.astype(jnp.float32),
        axis=-1,
        keepdims=True,
    )
    probability_gradient = jnp.einsum(
        "nmv,njv->nmj", output_gradient_heads, value_row_block, preferred_element_type=jnp.float32
    )
    score_gradient = (probabilities * (probability_gradient - out_dot)).astype(jnp.bfloat16)
    query_gradient_heads = (
        jnp.einsum(
            "jym,jmo->jyo", score_gradient, key_row_block, preferred_element_type=jnp.float32
        )
        * logit_scale
    ).astype(jnp.bfloat16)
    return attended_per_head, query_gradient_heads, log_total[..., 0], out_dot[..., 0]


def key_pass(key_per_head, value_per_head, query_slabs, grad_slabs, total_slabs, dot_slabs, allowed, logit_scale):
    block_count = query_slabs.shape[0]
    query_rows = query_slabs.reshape(block_count, -1, HD)
    grad_rows = grad_slabs.reshape(block_count, -1, HD)
    score_matrix = (
        jnp.einsum("nmv,njv->nmj", query_rows, key_per_head, preferred_element_type=jnp.float32)
        * logit_scale
    )
    total_rows = total_slabs.reshape(block_count, -1, 1)
    dot_rows = dot_slabs.reshape(block_count, -1, 1)
    probabilities = jnp.where(allowed, jnp.exp(score_matrix - total_rows), 0.0)
    probability_gradient = jnp.einsum(
        "nmv,njv->nmj", grad_rows, value_per_head, preferred_element_type=jnp.float32
    )
    score_gradient = (probabilities * (probability_gradient - dot_rows)).astype(jnp.bfloat16)
    attention_weight = probabilities.astype(jnp.bfloat16)
    key_gradient = (
        jnp.einsum("nmj,nmv->njv", score_gradient, query_rows, preferred_element_type=jnp.float32)
        * logit_scale
    )
    value_gradient = jnp.einsum(
        "nmj,nmv->njv", attention_weight, grad_rows, preferred_element_type=jnp.float32
    )
    return key_gradient, value_gradient


def key_allowed(first_block, blocks_dev, offsets, block_total):
    block_ids = first_block + jnp.arange(blocks_dev, dtype=jnp.int32)
    offset_arr = jnp.array(offsets, dtype=jnp.int32)
    query_live = block_ids[:, None] + offset_arr[None, :] < block_total
    row_ids = jnp.arange(BLK, dtype=jnp.int32)
    causal = row_ids[:, None] >= row_ids[None, :]
    later_slab = offset_arr > 0
    slab_causal = jnp.logical_or(later_slab[:, None, None], causal[None, :, :])
    allowed = jnp.logical_and(query_live[:, :, None, None], slab_causal[None, :, :, :])
    return allowed.reshape(blocks_dev, len(offsets) * BLK, BLK)


TRANS_B = (((1,), (1,)), ((), ()))


def span_load(refs, start, length, other, axis):
    size = refs[0].shape[axis]
    pieces = []
    at = start
    while length > 0:
        index, offset = at // size, at % size
        count = min(size - offset, length)
        window = pl.ds(offset, count)
        pieces.append(refs[index][window, other] if axis == 0 else refs[index][other, window])
        at += count
        length -= count
    return pieces[0] if len(pieces) == 1 else jnp.concatenate(pieces, axis=axis)


def row_kernel(near_count, far_list, heads, phase, *refs):
    far_count = len(far_list)
    position_ref, query_ref, grad_ref = refs[:3]
    span_refs = refs[3:6]
    far_refs = refs[6 : 6 + far_count]
    if phase == "stats":
        attended_ref, stats_ref, stats_rows_ref = refs[6 + far_count :]
    else:
        stats_in_ref, grad_query_ref = refs[6 + far_count :]
    width = heads * HD
    near_rows = near_count * BLK
    scale = 1.0 / math.sqrt(HD)
    first = 2 * position_ref[0]
    near_row_ids = lax.broadcasted_iota(jnp.int32, (BLK, near_rows), 0)
    near_col_ids = lax.broadcasted_iota(jnp.int32, (BLK, near_rows), 1)
    near_offset = (near_count - 1) - near_col_ids // BLK
    near_causal = jnp.logical_or(near_offset > 0, near_row_ids >= near_col_ids % BLK)
    lane_ids = lax.broadcasted_iota(jnp.int32, (BLK, 2 * heads), 1)
    for block in range(2):
        rows = pl.ds(block * BLK, BLK)
        near_span = pl.ds(block * BLK, near_rows)
        near_mask = jnp.logical_and(near_causal, first + block - near_offset >= 0)
        far_live = [first + block - offset >= 0 for offset in far_list]
        masks = [
            jnp.concatenate(
                [near_mask] + [jnp.logical_and(near_row_ids[:, :BLK] >= 0, live) for live in far_live],
                axis=1,
            )
        ]
        if phase == "stats":
            stats_tile = jnp.zeros((BLK, 2 * heads), jnp.float32)
        else:
            stats_tile = stats_in_ref[rows, :]
        for head in range(heads):
            cols = pl.ds(head * HD, HD)
            value_cols = pl.ds(width + head * HD, HD)
            query = query_ref[rows, cols]
            grad = grad_ref[rows, cols]
            keys = [span_load(span_refs, block * BLK, near_rows, cols, 0)]
            keys = [jnp.concatenate(keys + [item[rows, cols] for item in far_refs], axis=0)]
            values = [span_load(span_refs, block * BLK, near_rows, value_cols, 0)]
            values = [jnp.concatenate(values + [item[rows, value_cols] for item in far_refs], axis=0)]
            scores = [
                lax.dot_general(query, key, TRANS_B, preferred_element_type=jnp.float32) * scale
                for key in keys
            ]
            if phase == "grad":
                log_total = jnp.sum(jnp.where(lane_ids == head, stats_tile, 0.0), axis=-1, keepdims=True)
                out_dot = jnp.sum(
                    jnp.where(lane_ids == heads + head, stats_tile, 0.0), axis=-1, keepdims=True
                )
                probs = [
                    jnp.where(mask, jnp.exp(score - log_total), 0.0)
                    for score, mask in zip(scores, masks)
                ]
                grad_query = jnp.zeros((BLK, HD), jnp.float32)
                for prob, key, value in zip(probs, keys, values):
                    prob_grad = lax.dot_general(
                        grad, value, TRANS_B, preferred_element_type=jnp.float32
                    )
                    score_grad = (prob * (prob_grad - out_dot)).astype(jnp.bfloat16)
                    grad_query = grad_query + jnp.dot(
                        score_grad, key, preferred_element_type=jnp.float32
                    )
                grad_query_ref[rows, cols] = (grad_query * scale).astype(jnp.bfloat16)
                continue
            scores = [jnp.where(mask, score, NEG) for score, mask in zip(scores, masks)]
            row_max = scores[0].max(axis=-1, keepdims=True)
            for score in scores[1:]:
                row_max = jnp.maximum(row_max, score.max(axis=-1, keepdims=True))
            shifted = [jnp.exp(score - row_max) for score in scores]
            row_sum = shifted[0].sum(axis=-1, keepdims=True)
            for item in shifted[1:]:
                row_sum = row_sum + item.sum(axis=-1, keepdims=True)
            log_total = row_max + jnp.log(row_sum)
            inverse = 1.0 / row_sum
            attended = jnp.zeros((BLK, HD), jnp.float32)
            for item, value in zip(shifted, values):
                attended = attended + jnp.dot(
                    (item * inverse).astype(jnp.bfloat16), value, preferred_element_type=jnp.float32
                )
            attended = attended.astype(jnp.bfloat16)
            attended_ref[rows, cols] = attended
            out_dot = jnp.sum(
                grad.astype(jnp.float32) * attended.astype(jnp.float32), axis=-1, keepdims=True
            )
            stats_tile = stats_tile + jnp.where(lane_ids == head, log_total, 0.0)
            stats_tile = stats_tile + jnp.where(lane_ids == heads + head, out_dot, 0.0)
        if phase == "stats":
            stats_ref[rows, :] = stats_tile
            wide_lanes = lax.broadcasted_iota(jnp.int32, (BLK, BLK), 1)
            wide = jnp.zeros((BLK, BLK), jnp.float32)
            for lane in range(2 * heads):
                column = jnp.sum(jnp.where(lane_ids == lane, stats_tile, 0.0), axis=-1, keepdims=True)
                wide = wide + jnp.where(wide_lanes == lane, column, 0.0)
            stats_rows_ref[:, rows] = wide.T[: 2 * heads, :]


def estimate(tok_count, row_width, slab_rows, matmuls, exps):
    flops = 2 * tok_count * slab_rows * HD * matmuls * (row_width // HD)
    return pl.CostEstimate(
        flops=flops,
        transcendentals=tok_count * slab_rows * exps * (row_width // HD),
        bytes_accessed=8 * tok_count * row_width * 4,
    )


def key_kernel(near_count, far_list, heads, block_total, *refs):
    far_count = len(far_list)
    position_ref, own_ref = refs[:2]
    span_refs = refs[2:5]
    stats_refs = refs[5:8]
    far_rows = refs[8 : 8 + far_count]
    far_stats = refs[8 + far_count : 8 + 2 * far_count]
    grad_key_ref, grad_value_ref = refs[8 + 2 * far_count :]
    width = heads * HD
    near_rows = near_count * BLK
    scale = 1.0 / math.sqrt(HD)
    first = 2 * position_ref[0]
    near_key_ids = lax.broadcasted_iota(jnp.int32, (BLK, near_rows), 0)
    near_query_ids = lax.broadcasted_iota(jnp.int32, (BLK, near_rows), 1)
    near_offset = near_query_ids // BLK
    near_causal = jnp.logical_or(near_offset > 0, near_query_ids % BLK >= near_key_ids)
    for block in range(2):
        rows = pl.ds(block * BLK, BLK)
        near_span = pl.ds(block * BLK, near_rows)
        near_mask = jnp.logical_and(near_causal, first + block + near_offset < block_total)
        far_live = [first + block + offset < block_total for offset in far_list]
        masks = [
            jnp.concatenate(
                [near_mask] + [jnp.logical_and(near_key_ids[:, :BLK] >= 0, live) for live in far_live],
                axis=1,
            )
        ]
        for head in range(heads):
            cols = pl.ds(head * HD, HD)
            value_cols = pl.ds(width + head * HD, HD)
            key = own_ref[rows, cols]
            value = own_ref[rows, value_cols]
            queries = [span_load(span_refs, block * BLK, near_rows, cols, 0)]
            queries = [jnp.concatenate(queries + [item[rows, cols] for item in far_rows], axis=0)]
            grads = [span_load(span_refs, block * BLK, near_rows, value_cols, 0)]
            grads = [jnp.concatenate(grads + [item[rows, value_cols] for item in far_rows], axis=0)]
            totals = [span_load(stats_refs, block * BLK, near_rows, pl.ds(head, 1), 1)] + [
                item[pl.ds(head, 1), rows] for item in far_stats
            ]
            dots = [span_load(stats_refs, block * BLK, near_rows, pl.ds(heads + head, 1), 1)] + [
                item[pl.ds(heads + head, 1), rows] for item in far_stats
            ]
            totals = [jnp.concatenate(totals, axis=1)]
            dots = [jnp.concatenate(dots, axis=1)]
            grad_key = jnp.zeros((BLK, HD), jnp.float32)
            grad_value = jnp.zeros((BLK, HD), jnp.float32)
            for query, grad, log_total, out_dot, mask in zip(queries, grads, totals, dots, masks):
                score = lax.dot_general(key, query, TRANS_B, preferred_element_type=jnp.float32)
                prob = jnp.where(mask, jnp.exp(score * scale - log_total), 0.0)
                prob_grad = lax.dot_general(value, grad, TRANS_B, preferred_element_type=jnp.float32)
                score_grad = (prob * (prob_grad - out_dot)).astype(jnp.bfloat16)
                grad_value = grad_value + jnp.dot(
                    prob.astype(jnp.bfloat16), grad, preferred_element_type=jnp.float32
                )
                grad_key = grad_key + jnp.dot(score_grad, query, preferred_element_type=jnp.float32)
            grad_key_ref[rows, cols] = (grad_key * scale).astype(jnp.bfloat16)
            grad_value_ref[rows, cols] = grad_value.astype(jnp.bfloat16)


def smem_spec():
    return pl.BlockSpec(memory_space=pltpu.SMEM)


def vmem_spec():
    return pl.BlockSpec(memory_space=pltpu.VMEM)


def body(queries, key_tokens, value_tokens, grad_out):
    row_width = queries.shape[1]
    tok_count = queries.shape[0]
    devices = lax.axis_size("seq")
    blocks_dev, rim, near_list, far_list, far_shifts = plan(tok_count, devices)
    if not relay_ok(devices, blocks_dev, rim, far_shifts):
        return legacy_body(queries, key_tokens, value_tokens, grad_out)
    heads = row_width // HD
    offsets = near_list + far_list
    logit_scale = 1.0 / math.sqrt(HD)
    span_blocks = (rim + 1) * blocks_dev
    lead = rim * blocks_dev
    position = lax.axis_index("seq")
    odd = (position % 2) == 1
    pairs = swap_pairs(devices)
    keys_values = jnp.concatenate([key_tokens, value_tokens], axis=1)
    queries_grads = jnp.concatenate([queries, grad_out], axis=1)
    back2 = passed_along(keys_values, "seq", 2)
    ahead2 = passed_along(queries_grads, "seq", -2)
    swap_one = lax.ppermute(jnp.where(odd, queries_grads, keys_values), "seq", pairs)
    back4 = passed_along(back2, "seq", 2)
    ahead4 = passed_along(ahead2, "seq", -2)
    swap_two = lax.ppermute(jnp.where(odd, back2, ahead2), "seq", pairs)
    back1 = jnp.where(odd, swap_one, swap_two)
    ahead1 = jnp.where(odd, swap_two, swap_one)
    far_back = [back4] + [passed_along(keys_values, "seq", shift) for shift in far_shifts[1:]]
    far_ahead = [ahead4] + [passed_along(queries_grads, "seq", -shift) for shift in far_shifts[1:]]
    far_back = far_back[: len(far_shifts)]
    far_ahead = far_ahead[: len(far_shifts)]

    position_arr = jnp.reshape(position, (1,)).astype(jnp.int32)
    far_offsets = list(far_list)
    slab_rows = (len(near_list) + len(far_list)) * BLK
    row_inputs = (position_arr, queries, grad_out, back2, back1, keys_values, *far_back)
    attended, stats, stats_rows = pl.pallas_call(
        functools.partial(row_kernel, len(near_list), far_offsets, heads, "stats"),
        out_shape=(
            jax.ShapeDtypeStruct((tok_count, row_width), jnp.bfloat16),
            jax.ShapeDtypeStruct((tok_count, 2 * heads), jnp.float32),
            jax.ShapeDtypeStruct((2 * heads, tok_count), jnp.float32),
        ),
        in_specs=[smem_spec()] + [vmem_spec()] * (5 + len(far_back)),
        out_specs=(vmem_spec(), vmem_spec(), vmem_spec()),
        cost_estimate=estimate(tok_count, row_width, slab_rows, 2, 1),
        name="rows_stats",
    )(*row_inputs)
    stats_one = passed_along(stats_rows, "seq", -1)
    stats_two = passed_along(stats_rows, "seq", -2)
    far_stats = [passed_along(stats_rows, "seq", -shift) for shift in far_shifts]
    grad_queries = pl.pallas_call(
        functools.partial(row_kernel, len(near_list), far_offsets, heads, "grad"),
        out_shape=jax.ShapeDtypeStruct((tok_count, row_width), jnp.bfloat16),
        in_specs=[smem_spec()] + [vmem_spec()] * (6 + len(far_back)),
        out_specs=vmem_spec(),
        cost_estimate=estimate(tok_count, row_width, slab_rows, 3, 1),
        name="rows_grad",
    )(*row_inputs, stats)
    grad_keys, grad_values = pl.pallas_call(
        functools.partial(key_kernel, len(near_list), far_offsets, heads, devices * blocks_dev),
        out_shape=(
            jax.ShapeDtypeStruct((tok_count, row_width), jnp.bfloat16),
            jax.ShapeDtypeStruct((tok_count, row_width), jnp.bfloat16),
        ),
        in_specs=[smem_spec()] + [vmem_spec()] * (7 + 2 * len(far_ahead)),
        out_specs=(vmem_spec(), vmem_spec()),
        cost_estimate=estimate(tok_count, row_width, slab_rows, 4, 1),
        name="keys_pass",
    )(
        position_arr,
        keys_values,
        queries_grads,
        ahead1,
        ahead2,
        stats_rows,
        stats_one,
        stats_two,
        *far_ahead,
        *far_stats,
    )
    return attended, grad_queries, grad_keys, grad_values


def solution(mesh):
    placed = (
        P(("rep", "seq"), None),
        P(("rep", "seq"), None),
        P(("rep", "seq"), None),
        P(("rep", "seq"), None),
    )
    return jax.shard_map(
        body,
        mesh=mesh,
        in_specs=placed,
        out_specs=(
            P(("rep", "seq"), None),
            P(("rep", "seq"), None),
            P(("rep", "seq"), None),
            P(("rep", "seq"), None),
        ),
        check_vma=False,
    )
```

```python
import functools
import math

import jax
import jax.numpy as jnp
from jax import lax
from jax.experimental import pallas as pl
from jax.experimental.pallas import tpu as pltpu
from jax.sharding import PartitionSpec as P

HEADS = 4
HD = 128
BLK = 128
WINDOW = 4


NEG = -1e30
CHUNKS = 2


def passed_along(value, axis, steps):
    count = lax.axis_size(axis)
    first, last = (max(0, -steps), min(count, count - steps))
    return lax.ppermute(value, axis, [(source, source + steps) for source in range(first, last)])


def offset_lists(block_total):
    near_list = list(range(WINDOW + 1))
    far_list = []
    stride = 1
    while stride < block_total:
        if stride > WINDOW:
            far_list.append(stride)
        stride = stride * 2
    return (near_list, far_list)


def allowed_mask(first_block, blocks_dev, offsets):
    block_ids = first_block + jnp.arange(blocks_dev, dtype=jnp.int32)
    offset_arr = jnp.array(offsets, dtype=jnp.int32)
    block_live = block_ids[:, None] - offset_arr[None, :] >= 0
    row_ids = jnp.arange(BLK, dtype=jnp.int32)
    causal = row_ids[:, None] >= row_ids[None, :]
    later_slab = offset_arr > 0
    slab_causal = jnp.logical_or(later_slab[None, :, None], causal[:, None, :])
    allowed = jnp.logical_and(block_live[:, None, :, None], slab_causal[None, :, :, :])
    return allowed.reshape(blocks_dev, BLK, len(offsets) * BLK)


def head_cols(array_in, col_start):
    return array_in[..., col_start : col_start + HD]


def to_blocks(array_in, block_count):
    return array_in.reshape(block_count, BLK, array_in.shape[-1])


def place_slabs(gradient, near_list, lead, span_blocks):
    blocks_dev = gradient.shape[0]
    placed = []
    for slot_index, offset in enumerate(near_list):
        before = lead - offset
        after = span_blocks - before - blocks_dev
        placed.append(jnp.pad(gradient[:, slot_index], ((before, after), (0, 0), (0, 0))))
    total = placed[0]
    for item in placed[1:]:
        total = total + item
    return total


def head_pass(query_per_head, output_gradient_heads, key_slabs, value_slabs, allowed, logit_scale):
    block_count = key_slabs.shape[0]
    key_row_block = key_slabs.reshape(block_count, -1, HD)
    value_row_block = value_slabs.reshape(block_count, -1, HD)
    score_matrix = (
        jnp.einsum(
            "nmv,njv->nmj", query_per_head, key_row_block, preferred_element_type=jnp.float32
        )
        * logit_scale
    )
    score_matrix = jnp.where(allowed, score_matrix, NEG)
    row_max = jnp.max(score_matrix, axis=-1, keepdims=True)
    log_total = row_max + jnp.log(jnp.sum(jnp.exp(score_matrix - row_max), axis=-1, keepdims=True))
    probabilities = jnp.exp(score_matrix - log_total)
    attention_weight = probabilities.astype(jnp.bfloat16)
    attended_per_head = jnp.einsum(
        "jym,jmo->jyo", attention_weight, value_row_block, preferred_element_type=jnp.float32
    ).astype(jnp.bfloat16)
    out_dot = jnp.sum(
        output_gradient_heads.astype(jnp.float32) * attended_per_head.astype(jnp.float32),
        axis=-1,
        keepdims=True,
    )
    probability_gradient = jnp.einsum(
        "nmv,njv->nmj", output_gradient_heads, value_row_block, preferred_element_type=jnp.float32
    )
    score_gradient = (probabilities * (probability_gradient - out_dot)).astype(jnp.bfloat16)
    query_gradient_heads = (
        jnp.einsum(
            "jym,jmo->jyo", score_gradient, key_row_block, preferred_element_type=jnp.float32
        )
        * logit_scale
    ).astype(jnp.bfloat16)
    key_gradient = (
        jnp.einsum(
            "uwj,uwn->ujn", score_gradient, query_per_head, preferred_element_type=jnp.float32
        )
        * logit_scale
    )
    value_gradient = jnp.einsum(
        "uwj,uwn->ujn", attention_weight, output_gradient_heads, preferred_element_type=jnp.float32
    )
    return (
        attended_per_head,
        query_gradient_heads,
        key_gradient,
        value_gradient,
        log_total[..., 0],
        out_dot[..., 0],
    )


def legacy_body(queries, key_tokens, value_tokens, grad_out):
    row_width = queries.shape[1]
    tok_count = queries.shape[0]
    blocks_dev = tok_count // BLK
    rim = (WINDOW + blocks_dev - 1) // blocks_dev
    devices = lax.axis_size("seq")
    near_list, far_list = offset_lists(devices * blocks_dev)
    offsets = near_list + far_list
    near_count = len(near_list)
    logit_scale = 1.0 / math.sqrt(HD)
    span_blocks = (rim + 1) * blocks_dev
    lead = rim * blocks_dev
    earlier_keys = []
    earlier_values = []
    for back in range(rim, 0, -1):
        got_keys, got_values = passed_along((key_tokens, value_tokens), "seq", back)
        earlier_keys.append(got_keys)
        earlier_values.append(got_values)
    span_keys = to_blocks(jnp.concatenate(earlier_keys + [key_tokens], axis=0), span_blocks)
    span_values = to_blocks(jnp.concatenate(earlier_values + [value_tokens], axis=0), span_blocks)
    far_keys = []
    far_values = []
    for stride in far_list:
        got_keys, got_values = passed_along((key_tokens, value_tokens), "seq", stride // blocks_dev)
        far_keys.append(to_blocks(got_keys, blocks_dev))
        far_values.append(to_blocks(got_values, blocks_dev))
    position = lax.axis_index("seq")
    allowed = allowed_mask(position * blocks_dev, blocks_dev, offsets)
    query_blocks = to_blocks(queries, blocks_dev)
    grad_blocks = to_blocks(grad_out, blocks_dev)
    attended_heads = []
    grad_query_heads = []
    near_key_heads = []
    near_value_heads = []
    total_heads = []
    dot_heads = []
    far_key_parts = [[] for stride in far_list]
    far_value_parts = [[] for stride in far_list]
    for head_index in range(HEADS):
        col_start = head_index * HD
        key_slabs = jnp.stack(
            [
                head_cols(span_keys[lead - offset : lead + blocks_dev - offset], col_start)
                for offset in near_list
            ]
            + [head_cols(item, col_start) for item in far_keys],
            axis=1,
        )
        value_slabs = jnp.stack(
            [
                head_cols(span_values[lead - offset : lead + blocks_dev - offset], col_start)
                for offset in near_list
            ]
            + [head_cols(item, col_start) for item in far_values],
            axis=1,
        )
        (
            attended_per_head,
            query_gradient_heads,
            key_gradient,
            value_gradient,
            log_total,
            out_dot,
        ) = head_pass(
            head_cols(query_blocks, col_start),
            head_cols(grad_blocks, col_start),
            key_slabs,
            value_slabs,
            allowed,
            logit_scale,
        )
        key_gradient = key_gradient.reshape(blocks_dev, -1, BLK, HD)
        value_gradient = value_gradient.reshape(blocks_dev, -1, BLK, HD)
        near_key_heads.append(place_slabs(key_gradient, near_list, lead, span_blocks))
        near_value_heads.append(place_slabs(value_gradient, near_list, lead, span_blocks))
        for level_index in range(len(far_list)):
            far_key_parts[level_index].append(
                key_gradient[:, near_count + level_index].astype(jnp.bfloat16)
            )
            far_value_parts[level_index].append(
                value_gradient[:, near_count + level_index].astype(jnp.bfloat16)
            )
        attended_heads.append(attended_per_head)
        grad_query_heads.append(query_gradient_heads)
        total_heads.append(log_total)
        dot_heads.append(out_dot)
    attended = jnp.concatenate(attended_heads, axis=-1).reshape(tok_count, row_width)
    grad_queries = jnp.concatenate(grad_query_heads, axis=-1).reshape(tok_count, row_width)
    near_keys = jnp.concatenate(near_key_heads, axis=-1).reshape((rim + 1) * tok_count, row_width)
    near_values = jnp.concatenate(near_value_heads, axis=-1).reshape(
        (rim + 1) * tok_count, row_width
    )
    total_keys = near_keys[lead * BLK :].astype(jnp.bfloat16).astype(jnp.float32)
    total_values = near_values[lead * BLK :].astype(jnp.bfloat16).astype(jnp.float32)
    for back in range(1, rim + 1):
        piece_start = (rim - back) * tok_count
        part_keys = near_keys[piece_start : piece_start + tok_count].astype(jnp.bfloat16)
        part_values = near_values[piece_start : piece_start + tok_count].astype(jnp.bfloat16)
        back_keys, back_values = passed_along((part_keys, part_values), "seq", -back)
        total_keys = total_keys + back_keys.astype(jnp.float32)
        total_values = total_values + back_values.astype(jnp.float32)
    for level_index, stride in enumerate(far_list):
        part_keys = jnp.concatenate(far_key_parts[level_index], axis=-1).reshape(
            tok_count, row_width
        )
        part_values = jnp.concatenate(far_value_parts[level_index], axis=-1).reshape(
            tok_count, row_width
        )
        got_keys, got_values = passed_along(
            (part_keys, part_values), "seq", -(stride // blocks_dev)
        )
        total_keys = total_keys + got_keys.astype(jnp.float32)
        total_values = total_values + got_values.astype(jnp.float32)
    return (
        attended,
        grad_queries,
        total_keys.astype(jnp.bfloat16),
        total_values.astype(jnp.bfloat16),
    )


def swap_pairs(count):
    return [(source, source ^ 1) for source in range(count) if source ^ 1 < count]


def relay_ok(count, blocks_dev, rim, far_shifts):
    return count % 2 == 0 and blocks_dev == 2 and rim == 2 and (not far_shifts or far_shifts[0] == 4)


def plan(tok_count, devices):
    blocks_dev = tok_count // BLK
    rim = (WINDOW + blocks_dev - 1) // blocks_dev
    near_list, far_list = offset_lists(devices * blocks_dev)
    far_shifts = [stride // blocks_dev for stride in far_list]
    return blocks_dev, rim, near_list, far_list, far_shifts


def row_pass(query_per_head, output_gradient_heads, key_slabs, value_slabs, allowed, logit_scale):
    block_count = key_slabs.shape[0]
    key_row_block = key_slabs.reshape(block_count, -1, HD)
    value_row_block = value_slabs.reshape(block_count, -1, HD)
    score_matrix = (
        jnp.einsum(
            "nmv,njv->nmj", query_per_head, key_row_block, preferred_element_type=jnp.float32
        )
        * logit_scale
    )
    score_matrix = jnp.where(allowed, score_matrix, NEG)
    row_max = jnp.max(score_matrix, axis=-1, keepdims=True)
    log_total = row_max + jnp.log(jnp.sum(jnp.exp(score_matrix - row_max), axis=-1, keepdims=True))
    probabilities = jnp.exp(score_matrix - log_total)
    attention_weight = probabilities.astype(jnp.bfloat16)
    attended_per_head = jnp.einsum(
        "jym,jmo->jyo", attention_weight, value_row_block, preferred_element_type=jnp.float32
    ).astype(jnp.bfloat16)
    out_dot = jnp.sum(
        output_gradient_heads.astype(jnp.float32) * attended_per_head.astype(jnp.float32),
        axis=-1,
        keepdims=True,
    )
    probability_gradient = jnp.einsum(
        "nmv,njv->nmj", output_gradient_heads, value_row_block, preferred_element_type=jnp.float32
    )
    score_gradient = (probabilities * (probability_gradient - out_dot)).astype(jnp.bfloat16)
    query_gradient_heads = (
        jnp.einsum(
            "jym,jmo->jyo", score_gradient, key_row_block, preferred_element_type=jnp.float32
        )
        * logit_scale
    ).astype(jnp.bfloat16)
    return attended_per_head, query_gradient_heads, log_total[..., 0], out_dot[..., 0]


def key_pass(key_per_head, value_per_head, query_slabs, grad_slabs, total_slabs, dot_slabs, allowed, logit_scale):
    block_count = query_slabs.shape[0]
    query_rows = query_slabs.reshape(block_count, -1, HD)
    grad_rows = grad_slabs.reshape(block_count, -1, HD)
    score_matrix = (
        jnp.einsum("nmv,njv->nmj", query_rows, key_per_head, preferred_element_type=jnp.float32)
        * logit_scale
    )
    total_rows = total_slabs.reshape(block_count, -1, 1)
    dot_rows = dot_slabs.reshape(block_count, -1, 1)
    probabilities = jnp.where(allowed, jnp.exp(score_matrix - total_rows), 0.0)
    probability_gradient = jnp.einsum(
        "nmv,njv->nmj", grad_rows, value_per_head, preferred_element_type=jnp.float32
    )
    score_gradient = (probabilities * (probability_gradient - dot_rows)).astype(jnp.bfloat16)
    attention_weight = probabilities.astype(jnp.bfloat16)
    key_gradient = (
        jnp.einsum("nmj,nmv->njv", score_gradient, query_rows, preferred_element_type=jnp.float32)
        * logit_scale
    )
    value_gradient = jnp.einsum(
        "nmj,nmv->njv", attention_weight, grad_rows, preferred_element_type=jnp.float32
    )
    return key_gradient, value_gradient


def key_allowed(first_block, blocks_dev, offsets, block_total):
    block_ids = first_block + jnp.arange(blocks_dev, dtype=jnp.int32)
    offset_arr = jnp.array(offsets, dtype=jnp.int32)
    query_live = block_ids[:, None] + offset_arr[None, :] < block_total
    row_ids = jnp.arange(BLK, dtype=jnp.int32)
    causal = row_ids[:, None] >= row_ids[None, :]
    later_slab = offset_arr > 0
    slab_causal = jnp.logical_or(later_slab[:, None, None], causal[None, :, :])
    allowed = jnp.logical_and(query_live[:, :, None, None], slab_causal[None, :, :, :])
    return allowed.reshape(blocks_dev, len(offsets) * BLK, BLK)


TRANS_B = (((1,), (1,)), ((), ()))


def span_load(refs, start, length, other, axis):
    size = refs[0].shape[axis]
    pieces = []
    at = start
    while length > 0:
        index, offset = at // size, at % size
        count = min(size - offset, length)
        window = pl.ds(offset, count)
        pieces.append(refs[index][window, other] if axis == 0 else refs[index][other, window])
        at += count
        length -= count
    return pieces[0] if len(pieces) == 1 else jnp.concatenate(pieces, axis=axis)


def row_kernel(near_count, far_list, heads, phase, *refs):
    far_count = len(far_list)
    position_ref, query_ref, grad_ref = refs[:3]
    span_refs = refs[3:6]
    far_refs = refs[6 : 6 + far_count]
    if phase == "stats":
        attended_ref, stats_ref, stats_rows_ref = refs[6 + far_count :]
    else:
        stats_in_ref, grad_query_ref = refs[6 + far_count :]
    width = heads * HD
    near_rows = near_count * BLK
    scale = 1.0 / math.sqrt(HD)
    first = 2 * position_ref[0]
    near_row_ids = lax.broadcasted_iota(jnp.int32, (BLK, near_rows), 0)
    near_col_ids = lax.broadcasted_iota(jnp.int32, (BLK, near_rows), 1)
    near_offset = (near_count - 1) - near_col_ids // BLK
    near_causal = jnp.logical_or(near_offset > 0, near_row_ids >= near_col_ids % BLK)
    lane_ids = lax.broadcasted_iota(jnp.int32, (BLK, 2 * heads), 1)
    for block in range(2):
        rows = pl.ds(block * BLK, BLK)
        near_span = pl.ds(block * BLK, near_rows)
        near_mask = jnp.logical_and(near_causal, first + block - near_offset >= 0)
        far_live = [first + block - offset >= 0 for offset in far_list]
        masks = [
            jnp.concatenate(
                [near_mask] + [jnp.logical_and(near_row_ids[:, :BLK] >= 0, live) for live in far_live],
                axis=1,
            )
        ]
        if phase == "stats":
            stats_tile = jnp.zeros((BLK, 2 * heads), jnp.float32)
        else:
            stats_tile = stats_in_ref[rows, :]
        for head in range(heads):
            cols = pl.ds(head * HD, HD)
            value_cols = pl.ds(width + head * HD, HD)
            query = query_ref[rows, cols]
            grad = grad_ref[rows, cols]
            keys = [span_load(span_refs, block * BLK, near_rows, cols, 0)]
            keys = [jnp.concatenate(keys + [item[rows, cols] for item in far_refs], axis=0)]
            values = [span_load(span_refs, block * BLK, near_rows, value_cols, 0)]
            values = [jnp.concatenate(values + [item[rows, value_cols] for item in far_refs], axis=0)]
            scores = [
                lax.dot_general(query, key, TRANS_B, preferred_element_type=jnp.float32) * scale
                for key in keys
            ]
            if phase == "grad":
                log_total = jnp.sum(jnp.where(lane_ids == head, stats_tile, 0.0), axis=-1, keepdims=True)
                out_dot = jnp.sum(
                    jnp.where(lane_ids == heads + head, stats_tile, 0.0), axis=-1, keepdims=True
                )
                probs = [
                    jnp.where(mask, jnp.exp(score - log_total), 0.0)
                    for score, mask in zip(scores, masks)
                ]
                grad_query = jnp.zeros((BLK, HD), jnp.float32)
                for prob, key, value in zip(probs, keys, values):
                    prob_grad = lax.dot_general(
                        grad, value, TRANS_B, preferred_element_type=jnp.float32
                    )
                    score_grad = (prob * (prob_grad - out_dot)).astype(jnp.bfloat16)
                    grad_query = grad_query + jnp.dot(
                        score_grad, key, preferred_element_type=jnp.float32
                    )
                grad_query_ref[rows, cols] = (grad_query * scale).astype(jnp.bfloat16)
                continue
            scores = [jnp.where(mask, score, NEG) for score, mask in zip(scores, masks)]
            row_max = scores[0].max(axis=-1, keepdims=True)
            for score in scores[1:]:
                row_max = jnp.maximum(row_max, score.max(axis=-1, keepdims=True))
            shifted = [jnp.exp(score - row_max) for score in scores]
            row_sum = shifted[0].sum(axis=-1, keepdims=True)
            for item in shifted[1:]:
                row_sum = row_sum + item.sum(axis=-1, keepdims=True)
            log_total = row_max + jnp.log(row_sum)
            inverse = 1.0 / row_sum
            attended = jnp.zeros((BLK, HD), jnp.float32)
            for item, value in zip(shifted, values):
                attended = attended + jnp.dot(
                    item.astype(jnp.bfloat16), value, preferred_element_type=jnp.float32
                )
            attended = (attended * inverse).astype(jnp.bfloat16)
            attended_ref[rows, cols] = attended
            out_dot = jnp.sum(
                grad.astype(jnp.float32) * attended.astype(jnp.float32), axis=-1, keepdims=True
            )
            stats_tile = stats_tile + jnp.where(lane_ids == head, log_total, 0.0)
            stats_tile = stats_tile + jnp.where(lane_ids == heads + head, out_dot, 0.0)
        if phase == "stats":
            stats_ref[rows, :] = stats_tile
            wide_lanes = lax.broadcasted_iota(jnp.int32, (BLK, BLK), 1)
            wide = jnp.zeros((BLK, BLK), jnp.float32)
            for lane in range(2 * heads):
                column = jnp.sum(jnp.where(lane_ids == lane, stats_tile, 0.0), axis=-1, keepdims=True)
                wide = wide + jnp.where(wide_lanes == lane, column, 0.0)
            stats_rows_ref[:, rows] = wide.T[: 2 * heads, :]


def estimate(tok_count, row_width, slab_rows, matmuls, exps):
    flops = 2 * tok_count * slab_rows * HD * matmuls * (row_width // HD)
    return pl.CostEstimate(
        flops=flops,
        transcendentals=tok_count * slab_rows * exps * (row_width // HD),
        bytes_accessed=8 * tok_count * row_width * 4,
    )


def key_kernel(near_count, far_list, heads, block_total, *refs):
    far_count = len(far_list)
    position_ref, own_ref = refs[:2]
    span_refs = refs[2:5]
    stats_refs = refs[5:8]
    far_rows = refs[8 : 8 + far_count]
    far_stats = refs[8 + far_count : 8 + 2 * far_count]
    grad_key_ref, grad_value_ref = refs[8 + 2 * far_count :]
    width = heads * HD
    near_rows = near_count * BLK
    scale = 1.0 / math.sqrt(HD)
    first = 2 * position_ref[0]
    near_key_ids = lax.broadcasted_iota(jnp.int32, (BLK, near_rows), 0)
    near_query_ids = lax.broadcasted_iota(jnp.int32, (BLK, near_rows), 1)
    near_offset = near_query_ids // BLK
    near_causal = jnp.logical_or(near_offset > 0, near_query_ids % BLK >= near_key_ids)
    for block in range(2):
        rows = pl.ds(block * BLK, BLK)
        near_span = pl.ds(block * BLK, near_rows)
        near_mask = jnp.logical_and(near_causal, first + block + near_offset < block_total)
        far_live = [first + block + offset < block_total for offset in far_list]
        masks = [
            jnp.concatenate(
                [near_mask] + [jnp.logical_and(near_key_ids[:, :BLK] >= 0, live) for live in far_live],
                axis=1,
            )
        ]
        for head in range(heads):
            cols = pl.ds(head * HD, HD)
            value_cols = pl.ds(width + head * HD, HD)
            key = own_ref[rows, cols]
            value = own_ref[rows, value_cols]
            queries = [span_load(span_refs, block * BLK, near_rows, cols, 0)]
            queries = [jnp.concatenate(queries + [item[rows, cols] for item in far_rows], axis=0)]
            grads = [span_load(span_refs, block * BLK, near_rows, value_cols, 0)]
            grads = [jnp.concatenate(grads + [item[rows, value_cols] for item in far_rows], axis=0)]
            totals = [span_load(stats_refs, block * BLK, near_rows, pl.ds(head, 1), 1)] + [
                item[pl.ds(head, 1), rows] for item in far_stats
            ]
            dots = [span_load(stats_refs, block * BLK, near_rows, pl.ds(heads + head, 1), 1)] + [
                item[pl.ds(heads + head, 1), rows] for item in far_stats
            ]
            totals = [jnp.concatenate(totals, axis=1)]
            dots = [jnp.concatenate(dots, axis=1)]
            grad_key = jnp.zeros((BLK, HD), jnp.float32)
            grad_value = jnp.zeros((BLK, HD), jnp.float32)
            for query, grad, log_total, out_dot, mask in zip(queries, grads, totals, dots, masks):
                score = lax.dot_general(key, query, TRANS_B, preferred_element_type=jnp.float32)
                prob = jnp.where(mask, jnp.exp(score * scale - log_total), 0.0)
                prob_grad = lax.dot_general(value, grad, TRANS_B, preferred_element_type=jnp.float32)
                score_grad = (prob * (prob_grad - out_dot)).astype(jnp.bfloat16)
                grad_value = grad_value + jnp.dot(
                    prob.astype(jnp.bfloat16), grad, preferred_element_type=jnp.float32
                )
                grad_key = grad_key + jnp.dot(score_grad, query, preferred_element_type=jnp.float32)
            grad_key_ref[rows, cols] = (grad_key * scale).astype(jnp.bfloat16)
            grad_value_ref[rows, cols] = grad_value.astype(jnp.bfloat16)


def smem_spec():
    return pl.BlockSpec(memory_space=pltpu.SMEM)


def vmem_spec():
    return pl.BlockSpec(memory_space=pltpu.VMEM)


def body(queries, key_tokens, value_tokens, grad_out):
    row_width = queries.shape[1]
    tok_count = queries.shape[0]
    devices = lax.axis_size("seq")
    blocks_dev, rim, near_list, far_list, far_shifts = plan(tok_count, devices)
    if not relay_ok(devices, blocks_dev, rim, far_shifts):
        return legacy_body(queries, key_tokens, value_tokens, grad_out)
    heads = row_width // HD
    offsets = near_list + far_list
    logit_scale = 1.0 / math.sqrt(HD)
    span_blocks = (rim + 1) * blocks_dev
    lead = rim * blocks_dev
    position = lax.axis_index("seq")
    odd = (position % 2) == 1
    pairs = swap_pairs(devices)
    keys_values = jnp.concatenate([key_tokens, value_tokens], axis=1)
    queries_grads = jnp.concatenate([queries, grad_out], axis=1)
    back2 = passed_along(keys_values, "seq", 2)
    ahead2 = passed_along(queries_grads, "seq", -2)
    swap_one = lax.ppermute(jnp.where(odd, queries_grads, keys_values), "seq", pairs)
    back4 = passed_along(back2, "seq", 2)
    ahead4 = passed_along(ahead2, "seq", -2)
    swap_two = lax.ppermute(jnp.where(odd, back2, ahead2), "seq", pairs)
    back1 = jnp.where(odd, swap_one, swap_two)
    ahead1 = jnp.where(odd, swap_two, swap_one)
    far_back = [back4] + [passed_along(keys_values, "seq", shift) for shift in far_shifts[1:]]
    far_ahead = [ahead4] + [passed_along(queries_grads, "seq", -shift) for shift in far_shifts[1:]]
    far_back = far_back[: len(far_shifts)]
    far_ahead = far_ahead[: len(far_shifts)]

    position_arr = jnp.reshape(position, (1,)).astype(jnp.int32)
    far_offsets = list(far_list)
    slab_rows = (len(near_list) + len(far_list)) * BLK
    row_inputs = (position_arr, queries, grad_out, back2, back1, keys_values, *far_back)
    attended, stats, stats_rows = pl.pallas_call(
        functools.partial(row_kernel, len(near_list), far_offsets, heads, "stats"),
        out_shape=(
            jax.ShapeDtypeStruct((tok_count, row_width), jnp.bfloat16),
            jax.ShapeDtypeStruct((tok_count, 2 * heads), jnp.float32),
            jax.ShapeDtypeStruct((2 * heads, tok_count), jnp.float32),
        ),
        in_specs=[smem_spec()] + [vmem_spec()] * (5 + len(far_back)),
        out_specs=(vmem_spec(), vmem_spec(), vmem_spec()),
        cost_estimate=estimate(tok_count, row_width, slab_rows, 2, 1),
        name="rows_stats",
    )(*row_inputs)
    stats_one = passed_along(stats_rows, "seq", -1)
    stats_two = passed_along(stats_rows, "seq", -2)
    far_stats = [passed_along(stats_rows, "seq", -shift) for shift in far_shifts]
    grad_queries = pl.pallas_call(
        functools.partial(row_kernel, len(near_list), far_offsets, heads, "grad"),
        out_shape=jax.ShapeDtypeStruct((tok_count, row_width), jnp.bfloat16),
        in_specs=[smem_spec()] + [vmem_spec()] * (6 + len(far_back)),
        out_specs=vmem_spec(),
        cost_estimate=estimate(tok_count, row_width, slab_rows, 3, 1),
        name="rows_grad",
    )(*row_inputs, stats)
    grad_keys, grad_values = pl.pallas_call(
        functools.partial(key_kernel, len(near_list), far_offsets, heads, devices * blocks_dev),
        out_shape=(
            jax.ShapeDtypeStruct((tok_count, row_width), jnp.bfloat16),
            jax.ShapeDtypeStruct((tok_count, row_width), jnp.bfloat16),
        ),
        in_specs=[smem_spec()] + [vmem_spec()] * (7 + 2 * len(far_ahead)),
        out_specs=(vmem_spec(), vmem_spec()),
        cost_estimate=estimate(tok_count, row_width, slab_rows, 4, 1),
        name="keys_pass",
    )(
        position_arr,
        keys_values,
        queries_grads,
        ahead1,
        ahead2,
        stats_rows,
        stats_one,
        stats_two,
        *far_ahead,
        *far_stats,
    )
    return attended, grad_queries, grad_keys, grad_values


def solution(mesh):
    placed = (
        P(("rep", "seq"), None),
        P(("rep", "seq"), None),
        P(("rep", "seq"), None),
        P(("rep", "seq"), None),
    )
    return jax.shard_map(
        body,
        mesh=mesh,
        in_specs=placed,
        out_specs=(
            P(("rep", "seq"), None),
            P(("rep", "seq"), None),
            P(("rep", "seq"), None),
            P(("rep", "seq"), None),
        ),
        check_vma=False,
    )
```
